512 devices in a mesh: mx: 32 (over z, core), my: 4 (over y), layer: 4 (over x).
Axes of the slice: x: 4, y: 4, z: 16, core: 2. Of those that a mesh axis runs over, the one named last changes fastest.
Arguments:
- ssa_velocity: float32 [2, 2048, 1024], P(None, 'mx', 'my'), may hold values from -6 to 6
- shelf_viscosity: float32 [2048, 1024], P('mx', 'my'), may hold values from 0.3 to 3
- basal_friction: float32 [2048, 1024], P('mx', 'my'), may hold values from 0.1 to 3
- driving_stress: float32 [2, 2048, 1024], P(None, 'mx', 'my'), may hold values from -6 to 6
- stokes_velocity: float32 [3, 12, 512, 1024], P(None, 'layer', 'mx', 'my'), may hold values from -6 to 6
- ice_viscosity: float32 [12, 512, 1024], P('layer', 'mx', 'my'), may hold values from 0.3 to 3
- body_force: float32 [3, 12, 512, 1024], P(None, 'layer', 'mx', 'my'), may hold values from -6 to 6
- diagonals: int32 [512, 1024], P('mx', 'my'), may hold values 0 or 1
- element_matrix: float32 [18, 18], replicated, may hold values from -0.1 to 1.5, as said below
- iface_columns: int32 [128, 9, 128], P(('mx', 'my')), may hold values from -1 to 4095, as said below
- iface_nodes: int32 [128, 9, 128], P(('mx', 'my')), may hold values from -1 to 16383, as said below
Outputs:
- coupled_residual: float32 [2, 2048, 1024], P(None, 'mx', 'my')
- stokes_residual: float32 [3, 12, 512, 1024], P(None, 'layer', 'mx', 'my')
The draws below stay inside these ranges and needn't reach their ends.
Inputs may be any that keep to these rules, and one draw needn't show every extreme that they name: `iface_columns`: slots toward blocks outside the map are empty; in each block and direction the live slots come first; all 128 slots toward a block's own direction (d = 4) are live; the live columns of one block are distinct. `iface_nodes`: slot (o, d, k) is live exactly where its partner slot (s, 8 - d, k) of iface_columns is live, s the block at offset d from o, and then names a node of o's 64 x 256 block (row-major). `element_matrix`: the diagonal dominates each row.
All inputs are finite; a program needn't handle non-finite values. No bound on the sum of `diagonals` on one device may be relied on, other than what follows from the above.
Results may differ from the reference program's by a relative error of at most 0.0001.
Values sent between devices are 32-bit elements; how exact they have to be, the bound alone decides.
No kernel may reach another device: no remote copies, remote signals or barrier semaphores. Data moves between devices by JAX's collectives and lax.ppermute only.
A program may use at most 64 MiB of HBM per device.

```python
import math
import jax
import jax.numpy as jnp
from jax import lax

SX = 64
SY = 256
CGX = 16
CGY = 256
MAPS = 128
NX = 2048
NY = 1024
GX = 512
GY = 1024
NL = 12
COL_DEV = 4096
CAP = 128
N_MX = 32
N_MY = 4


def link_draw(key):
    folded = jax.random.fold_in(key, 7)
    key_a, key_b, key_c = jax.random.split(folded, 3)
    drawn = jax.random.randint(key_a, (N_MX, N_MY, 3, 3), 0, CAP + 1)
    counts = drawn * drawn // CAP
    nearby = jnp.arange(3) - 1
    other_x = jnp.arange(N_MX)[:, None, None, None] + nearby[None, None, :, None]
    other_y = jnp.arange(N_MY)[None, :, None, None] + nearby[None, None, None, :]
    inside = (other_x >= 0) & (other_x < N_MX) & (other_y >= 0) & (other_y < N_MY)
    centre = (nearby[:, None] == 0) & (nearby[None, :] == 0)
    counts = jnp.where(centre[None, None], CAP, jnp.where(inside, counts, 0)).astype(jnp.int32)
    padded = jnp.pad(counts, ((1, 1), (1, 1), (0, 0), (0, 0)))
    mirror = jnp.stack([jnp.stack([padded[first:first + N_MX, second:second + N_MY, 2 - first, 2 - second] for second in range(3)], -1) for first in range(3)], -2)
    stokes_counts = counts.reshape(MAPS, 9)
    owner_counts = mirror.reshape(MAPS, 9)
    slot_ids = jnp.arange(CAP, dtype=jnp.int32)
    stokes_live = slot_ids[None, None, :] < stokes_counts[:, :, None]
    owner_live = slot_ids[None, None, :] < owner_counts[:, :, None]
    offsets = jnp.cumsum(stokes_counts, axis=1) - stokes_counts

    def shuffled(subkey):
        return jax.random.permutation(subkey, COL_DEV)
    orders = jax.vmap(shuffled)(jax.random.split(key_b, MAPS))
    position = jnp.minimum(offsets[:, :, None] + slot_ids[None, None, :], COL_DEV - 1)
    picked = jnp.take_along_axis(orders, position.reshape(MAPS, -1), axis=1).reshape(MAPS, 9, CAP)
    columns = jnp.where(stokes_live, picked, -1).astype(jnp.int32)
    node_ids = jax.random.randint(key_c, (MAPS, 9, CAP), 0, SX * SY)
    node_ids = jnp.where(owner_live, node_ids, -1).astype(jnp.int32)
    return (columns, node_ids)


def draw_iface_columns(key, part):
    return link_draw(key)[0]


def draw_iface_nodes(key, part):
    return link_draw(key)[1]


def draw_element_matrix(key, part):
    folded = jax.random.fold_in(key, 13)
    key_a, key_b = jax.random.split(folded)
    spread = jax.random.uniform(key_a, (18, 18), jnp.float32, -0.15, 0.15)
    diagonal_part = 2.6 + jax.random.uniform(key_b, (18,), jnp.float32)
    identity = jnp.eye(18, dtype=jnp.float32)
    return (spread * (1.0 - identity) + identity * diagonal_part[None, :]) / 3.0


def set_ends(values, own_key, low, top_value):
    extent = values.shape
    index_at = [jax.random.randint(jax.random.fold_in(own_key, axis), (), 0, extent[axis]) for axis in range(len(extent))]
    values = values.at[tuple(index_at)].set(low)
    longest = extent.index(max(extent))
    index_at[longest] = (index_at[longest] + 1) % extent[longest]
    return values.at[tuple(index_at)].set(top_value)


def block_levels(key, dims, pieces, least, high):
    def one(axis_at, shards_of):
        steps = jax.random.uniform(jax.random.fold_in(jax.random.fold_in(key, 6), axis_at), (shards_of,), jnp.float32, least / len(pieces), high / len(pieces))
        return jnp.repeat(jnp.exp(steps), dims[axis_at] // shards_of).reshape((-1,) + (1,) * (len(dims) - axis_at - 1))

    loudness = one(*pieces[0])
    for cut in pieces[1:]:
        loudness = loudness * one(*cut)
    return loudness


def bell_draw(own_key, shape, deviation, bound, cuts=(), kind=jnp.bfloat16):
    values = jax.random.normal(own_key, shape, jnp.float32) * deviation
    if len(cuts) > 0:
        values = block_levels(own_key, shape, cuts, -0.22, 0.18) * values
    return jnp.clip(values, min=-bound, max=bound).astype(kind)


def setup_inputs(seed: int = 0) -> dict:
    seeds = jax.random.split(jax.random.key(seed), 12)
    return {
        "ssa_velocity": bell_draw(seeds[0], (2, NX, NY), 1.0, 6.0, ((1, 32), (2, 4)), jnp.float32),
        "shelf_viscosity": jnp.clip(jnp.exp(math.log(3.0) - 2.3025851 * jax.random.uniform(seeds[1], (NX, NY), jnp.float32) ** block_levels(seeds[1], (NX, NY), ((0, 32), (1, 4)), -0.2, 0.2)), 0.3, 3.0),
        "basal_friction": jnp.clip(jnp.exp(math.log(3.0) - 3.4011974 * jax.random.uniform(seeds[2], (NX, NY), jnp.float32) ** block_levels(seeds[2], (NX, NY), ((0, 32), (1, 4)), -0.2, 0.2)), 0.1, 3.0),
        "driving_stress": bell_draw(seeds[3], (2, NX, NY), 1.0, 6.0, ((1, 32), (2, 4)), jnp.float32),
        "stokes_velocity": bell_draw(seeds[4], (3, NL, GX, GY), 1.0, 6.0, ((1, 4), (2, 32), (3, 4)), jnp.float32),
        "ice_viscosity": jnp.clip(jnp.exp(math.log(3.0) - 2.3025851 * jax.random.uniform(seeds[5], (NL, GX, GY), jnp.float32) ** block_levels(seeds[5], (NL, GX, GY), ((0, 4), (1, 32), (2, 4)), -0.2, 0.2)), 0.3, 3.0),
        "body_force": bell_draw(seeds[6], (3, NL, GX, GY), 1.0, 6.0, ((1, 4), (2, 32), (3, 4)), jnp.float32),
        "diagonals": set_ends((jax.random.randint(seeds[7], (GX, GY), 0, 2) < 1).astype(jnp.int32), jax.random.fold_in(seeds[7], 1), 0, 1),
        "element_matrix": draw_element_matrix(jax.random.fold_in(seeds[11], 71), 0),
        "iface_columns": draw_iface_columns(jax.random.fold_in(seeds[11], 71), 0),
        "iface_nodes": draw_iface_nodes(jax.random.fold_in(seeds[11], 71), 0),
    }


def cell_dx(plane):
    return 0.5 * ((plane[1:, :-1] + plane[1:, 1:]) - (plane[:-1, :-1] + plane[:-1, 1:]))


def cell_dy(plane):
    return 0.5 * ((plane[:-1, 1:] + plane[1:, 1:]) - (plane[:-1, :-1] + plane[1:, :-1]))


def shelf_residual(padded, friction, driving):
    u_field = padded[0]
    v_field = padded[1]
    h_field = padded[2]
    du_dx = cell_dx(u_field)
    du_dy = cell_dy(u_field)
    dv_dx = cell_dx(v_field)
    dv_dy = cell_dy(v_field)
    h_cell = 0.25 * (h_field[1:, :-1] + h_field[1:, 1:] + h_field[:-1, :-1] + h_field[:-1, 1:])
    tau_xx = h_cell * (4.0 * du_dx + 2.0 * dv_dy)
    tau_yy = h_cell * (4.0 * dv_dy + 2.0 * du_dx)
    tau_xy = h_cell * (du_dy + dv_dx)
    res_x = cell_dx(tau_xx) + cell_dy(tau_xy) - friction * u_field[1:-1, 1:-1] - driving[0]
    res_y = cell_dy(tau_yy) + cell_dx(tau_xy) - friction * v_field[1:-1, 1:-1] - driving[1]
    return jnp.stack([res_x, res_y])


def triangle(stiffness, lows, ups, weight):
    values = jnp.stack([plane[comp] for group in (lows, ups) for comp in range(3) for plane in group])
    viscous = (lows[0][3] + lows[1][3] + lows[2][3] + ups[0][3] + ups[1][3] + ups[2][3]) / 6.0 * weight
    response = jnp.einsum("ab,bxy->axy", stiffness, values, precision=lax.Precision.HIGHEST) * viscous
    return response.reshape((2, 3, 3) + response.shape[1:])


def cell_terms(lower, upper, flag_cells, stiffness, weight):
    low_a, low_b, low_c, low_d = lower[:, :-1, :-1], lower[:, 1:, :-1], lower[:, :-1, 1:], lower[:, 1:, 1:]
    up_a, up_b, up_c, up_d = upper[:, :-1, :-1], upper[:, 1:, :-1], upper[:, :-1, 1:], upper[:, 1:, 1:]
    main_diag = (flag_cells == 0)[None]
    low_far = jnp.where(main_diag, low_d, low_c)
    up_far = jnp.where(main_diag, up_d, up_c)
    low_near = jnp.where(main_diag, low_a, low_b)
    up_near = jnp.where(main_diag, up_a, up_b)
    tri_one = triangle(stiffness, (low_a, low_b, low_far), (up_a, up_b, up_far), weight)
    tri_two = triangle(stiffness, (low_near, low_d, low_c), (up_near, up_d, up_c), weight)
    result = []
    for height in range(2):
        resp_one = tri_one[height]
        resp_two = tri_two[height]
        corner_a = resp_one[:, 0] + jnp.where(main_diag, resp_two[:, 0], 0.0)
        corner_b = resp_one[:, 1] + jnp.where(main_diag, 0.0, resp_two[:, 0])
        corner_c = resp_two[:, 2] + jnp.where(main_diag, 0.0, resp_one[:, 2])
        corner_d = resp_two[:, 1] + jnp.where(main_diag, resp_one[:, 2], 0.0)
        result.append((corner_a, corner_b, corner_c, corner_d))
    return result[0], result[1]


def add_corners(total, extra):
    if total is None:
        return extra
    return tuple(first_term + other_term for first_term, other_term in zip(total, extra))


def to_nodes(corners):
    corner_a, corner_b, corner_c, corner_d = corners
    return (jnp.pad(corner_a, ((0, 0), (0, 1), (0, 1))) + jnp.pad(corner_b, ((0, 0), (1, 0), (0, 1)))
            + jnp.pad(corner_c, ((0, 0), (0, 1), (1, 0))) + jnp.pad(corner_d, ((0, 0), (1, 0), (1, 0))))


def reference(ssa_velocity, shelf_viscosity, basal_friction, driving_stress, stokes_velocity, ice_viscosity, body_force, diagonals, element_matrix, iface_columns, iface_nodes):
    stacked = jnp.concatenate([ssa_velocity, shelf_viscosity[None]], 0)
    padded = jnp.pad(stacked, ((0, 0), (1, 1), (1, 1)))
    shelf_res = shelf_residual(padded, basal_friction, driving_stress)

    direction = jnp.arange(9, dtype=jnp.int32)
    step_x = direction // 3 - 1
    step_y = direction % 3 - 1
    partition = jnp.arange(MAPS, dtype=jnp.int32)
    other_x = partition[:, None] // N_MY + step_x[None]
    other_y = partition[:, None] % N_MY + step_y[None]
    inside = (other_x >= 0) & (other_x < N_MX) & (other_y >= 0) & (other_y < N_MY)
    other = jnp.where(inside, other_x * N_MY + other_y, 0).astype(jnp.int32)
    mirrored = (8 - direction)[None, :]
    inside_f = inside.astype(jnp.float32)[None, :, :, None]

    node_live = iface_nodes >= 0
    node_safe = jnp.where(node_live, iface_nodes, 0)
    shelf_x = (partition // N_MY)[:, None, None] * SX + node_safe // SY
    shelf_y = (partition % N_MY)[:, None, None] * SY + node_safe % SY
    outgoing = ssa_velocity[:, shelf_x, shelf_y] * node_live.astype(jnp.float32)[None]
    iface_vel = outgoing[:, other, mirrored, :] * inside_f

    col_live = iface_columns >= 0
    col_safe = jnp.where(col_live, iface_columns, 0)
    stokes_x = (partition // N_MY)[:, None, None] * CGX + col_safe // CGY
    stokes_y = (partition % N_MY)[:, None, None] * CGY + col_safe % CGY
    flat_col = jnp.where(col_live, stokes_x * GY + stokes_y, GX * GY).astype(jnp.int32).reshape(-1)
    placed = jnp.zeros((2, GX * GY), jnp.float32).at[:, flat_col].add(iface_vel.reshape(2, -1), mode="drop")
    marked = jnp.zeros((GX * GY,), jnp.float32).at[flat_col].add(1.0, mode="drop") > 0.0
    uv_part = jnp.where(marked.reshape(1, 1, GX, GY), placed.reshape(2, 1, GX, GY), stokes_velocity[:2])
    stokes_field = jnp.concatenate([uv_part, stokes_velocity[2:3], ice_viscosity[None]], 0)

    flag_cells = diagonals[:-1, :-1]
    collected = [None for height in range(NL)]
    for height in range(NL - 1):
        lower_part, upper_part = cell_terms(stokes_field[:, height], stokes_field[:, height + 1], flag_cells, element_matrix, 1.0)
        collected[height] = add_corners(collected[height], lower_part)
        collected[height + 1] = add_corners(collected[height + 1], upper_part)
    assembled = jnp.stack([to_nodes(corners) for corners in collected], axis=1)
    stokes_residual = assembled - body_force

    depth_sum = jnp.sum(stokes_residual[:2], axis=1).reshape(2, GX * GY)
    col_index = jnp.where(col_live, stokes_x * GY + stokes_y, 0).astype(jnp.int32)
    iface_stress = depth_sum[:, col_index] * col_live.astype(jnp.float32)[None]
    at_owner = iface_stress[:, other, mirrored, :] * inside_f
    flat_node = jnp.where(node_live, shelf_x * NY + shelf_y, NX * NY).astype(jnp.int32).reshape(-1)
    node_force = jnp.zeros((2, NX * NY), jnp.float32).at[:, flat_node].add(at_owner.reshape(2, -1), mode="drop")
    coupled_residual = shelf_res - node_force.reshape(2, NX, NY)
    return coupled_residual, stokes_residual
```

```python
import jax
import jax.numpy as jnp
from jax import lax
from jax.sharding import PartitionSpec as P


def with_halo(array, sides, width):
    for axis, dim in sides:
        devices, length = (lax.axis_size(axis), array.shape[dim])
        up = [(i, (i + 1) % devices) for i in range(devices - 1)]
        down = [(j, i) for i, j in up]
        last = lax.slice_in_dim(array, length - width, length, axis=dim)
        initial = lax.slice_in_dim(array, 0, width, axis=dim)
        before = lax.ppermute(last, axis, up)
        after = lax.ppermute(initial, axis, down)
        array = jnp.concatenate([before, array, after], axis=dim)
    return array


HIGH = lax.Precision.HIGHEST


def slot_selectors(index, rows, cols):
    live = index >= 0
    row_of = jnp.where(live, index // cols, -1)
    col_of = jnp.where(live, index % cols, -1)
    pick_row = (row_of[:, None] == jnp.arange(rows, dtype=jnp.int32)[None]).astype(jnp.float32)
    pick_col = col_of[:, None] == jnp.arange(cols, dtype=jnp.int32)[None]
    return pick_row, pick_col


def gather_slots(field, pick_row, pick_col):
    rows_taken = jnp.einsum("sr,krc->ksc", pick_row, field, precision=HIGH)
    return jnp.sum(jnp.where(pick_col[None], rows_taken, 0.0), axis=-1)


def scatter_slots(values, pick_row, pick_col):
    spread = jnp.where(pick_col[None], values[:, :, None], 0.0)
    return jnp.einsum("sr,ksc->krc", pick_row, spread, precision=HIGH)


def layer_total(part):
    count = lax.axis_size("layer")
    place = lax.axis_index("layer")
    received = [part]
    for shift in range(1, count):
        pairs = [(i, (i + shift) % count) for i in range(count)]
        received.append(lax.ppermute(part, "layer", pairs))
    total = None
    for source in range(count):
        wanted = (place - source) % count
        value = received[0]
        for shift in range(1, count):
            value = jnp.where(wanted == shift, received[shift], value)
        total = value if total is None else total + value
    return total


def cell_dx(plane):
    return 0.5 * (plane[1:, :-1] + plane[1:, 1:] - (plane[:-1, :-1] + plane[:-1, 1:]))


def cell_dy(plane):
    return 0.5 * (plane[:-1, 1:] + plane[1:, 1:] - (plane[:-1, :-1] + plane[1:, :-1]))


def shelf_residual(padded, friction, driving):
    u_field = padded[0]
    v_field = padded[1]
    h_field = padded[2]
    du_dx = cell_dx(u_field)
    du_dy = cell_dy(u_field)
    dv_dx = cell_dx(v_field)
    dv_dy = cell_dy(v_field)
    h_cell = 0.25 * (h_field[1:, :-1] + h_field[1:, 1:] + h_field[:-1, :-1] + h_field[:-1, 1:])
    tau_xx = h_cell * (4.0 * du_dx + 2.0 * dv_dy)
    tau_yy = h_cell * (4.0 * dv_dy + 2.0 * du_dx)
    tau_xy = h_cell * (du_dy + dv_dx)
    res_x = cell_dx(tau_xx) + cell_dy(tau_xy) - friction * u_field[1:-1, 1:-1] - driving[0]
    res_y = cell_dy(tau_yy) + cell_dx(tau_xy) - friction * v_field[1:-1, 1:-1] - driving[1]
    return jnp.stack([res_x, res_y])


def triangle(stiffness, lows, ups, weight):
    values = jnp.stack(
        [plane[comp] for group in (lows, ups) for comp in range(3) for plane in group]
    )
    viscous = (
        (lows[0][3] + lows[1][3] + lows[2][3] + ups[0][3] + ups[1][3] + ups[2][3]) / 6.0 * weight
    )
    response = (
        jnp.einsum("ab,bxy->axy", stiffness, values, precision=lax.Precision.HIGHEST) * viscous
    )
    return response.reshape((2, 3, 3) + response.shape[1:])


def cell_terms(lower, upper, flag_cells, stiffness, weight):
    low_a, low_b, low_c, low_d = (
        lower[:, :-1, :-1],
        lower[:, 1:, :-1],
        lower[:, :-1, 1:],
        lower[:, 1:, 1:],
    )
    up_a, up_b, up_c, up_d = (
        upper[:, :-1, :-1],
        upper[:, 1:, :-1],
        upper[:, :-1, 1:],
        upper[:, 1:, 1:],
    )
    main_diag = (flag_cells == 0)[None]
    low_far = jnp.where(main_diag, low_d, low_c)
    up_far = jnp.where(main_diag, up_d, up_c)
    low_near = jnp.where(main_diag, low_a, low_b)
    up_near = jnp.where(main_diag, up_a, up_b)
    tri_one = triangle(stiffness, (low_a, low_b, low_far), (up_a, up_b, up_far), weight)
    tri_two = triangle(stiffness, (low_near, low_d, low_c), (up_near, up_d, up_c), weight)
    result = []
    for height in range(2):
        resp_one = tri_one[height]
        resp_two = tri_two[height]
        corner_a = resp_one[:, 0] + jnp.where(main_diag, resp_two[:, 0], 0.0)
        corner_b = resp_one[:, 1] + jnp.where(main_diag, 0.0, resp_two[:, 0])
        corner_c = resp_two[:, 2] + jnp.where(main_diag, 0.0, resp_one[:, 2])
        corner_d = resp_two[:, 1] + jnp.where(main_diag, resp_one[:, 2], 0.0)
        result.append((corner_a, corner_b, corner_c, corner_d))
    return (result[0], result[1])


def add_corners(total, extra):
    if total is None:
        return extra
    return tuple((first_term + other_term for first_term, other_term in zip(total, extra)))


def scaled_by(corners, factor):
    return tuple((member * factor for member in corners))


def own_nodes(corners):
    corner_a, corner_b, corner_c, corner_d = corners
    return corner_a[:, 1:, 1:] + corner_b[:, :-1, 1:] + corner_c[:, 1:, :-1] + corner_d[:, :-1, :-1]


def per_device(
    ssa_velocity,
    shelf_viscosity,
    basal_friction,
    driving_stress,
    stokes_velocity,
    ice_viscosity,
    body_force,
    diagonals,
    element_matrix,
    iface_columns,
    iface_nodes,
):
    row_count = ssa_velocity.shape[1]
    col_count = ssa_velocity.shape[2]
    stacked = jnp.concatenate([ssa_velocity, shelf_viscosity[None]], 0)
    padded = with_halo(stacked, (("mx", 1), ("my", 2)), 1)
    shelf_res = shelf_residual(padded, basal_friction, driving_stress)
    owner_nodes = iface_nodes[0]
    node_live = owner_nodes >= 0
    slot_count = owner_nodes.shape[1]
    node_row, node_col = slot_selectors(owner_nodes.reshape(-1), row_count, col_count)
    outgoing = gather_slots(ssa_velocity, node_row, node_col).reshape(2, 9, slot_count)
    grid_out = outgoing.reshape(2, 3, 3, slot_count)
    extended = with_halo(grid_out, (("mx", 1), ("my", 2)), 1)
    returned = extended[:, 0::2, 0::2].reshape(2, 9, slot_count)
    depth_count = stokes_velocity.shape[1]
    block_x = stokes_velocity.shape[2]
    block_y = stokes_velocity.shape[3]
    column_count = block_x * block_y
    columns = iface_columns[0]
    col_live = columns >= 0
    col_row, col_col = slot_selectors(columns.reshape(-1), block_x, block_y)
    placed = scatter_slots(returned.reshape(2, -1), col_row, col_col)
    marked = jnp.einsum("sr,sc->rc", col_row, col_col.astype(jnp.float32)) > 0.0
    uv_part = jnp.where(
        marked.reshape(1, 1, block_x, block_y),
        placed.reshape(2, 1, block_x, block_y),
        stokes_velocity[:2],
    )
    stokes_field = jnp.concatenate([uv_part, stokes_velocity[2:3], ice_viscosity[None]], 0)
    planes = jnp.concatenate(
        [
            stokes_field.reshape(4 * depth_count, block_x, block_y),
            diagonals.astype(jnp.float32)[None],
        ],
        0,
    )
    widened = with_halo(planes, (("mx", 1), ("my", 2)), 1)
    flag_cells = widened[-1, :-1, :-1]
    field_ext = widened[:-1].reshape(4, depth_count, block_x + 2, block_y + 2)
    count_x = lax.axis_size("mx")
    count_y = lax.axis_size("my")
    place_x = lax.axis_index("mx")
    place_y = lax.axis_index("my")
    global_x = place_x * block_x + jnp.arange(block_x + 1, dtype=jnp.int32) - 1
    global_y = place_y * block_y + jnp.arange(block_y + 1, dtype=jnp.int32) - 1
    valid_x = (global_x >= 0) & (global_x <= count_x * block_x - 2)
    valid_y = (global_y >= 0) & (global_y <= count_y * block_y - 2)
    weight = (valid_x[:, None] & valid_y[None, :]).astype(jnp.float32)
    layer_index = lax.axis_index("layer")
    layer_count = lax.axis_size("layer")
    below_live = (layer_index > 0).astype(jnp.float32)
    above_live = (layer_index < layer_count - 1).astype(jnp.float32)
    extended_layers = with_halo(field_ext, (("layer", 1),), 1)
    collected = [None for height in range(depth_count)]
    for height in range(depth_count + 1):
        lower_part, upper_part = cell_terms(
            extended_layers[:, height],
            extended_layers[:, height + 1],
            flag_cells,
            element_matrix,
            weight,
        )
        if height > 0:
            if height == depth_count:
                lower_part = scaled_by(lower_part, above_live)
            collected[height - 1] = add_corners(collected[height - 1], lower_part)
        if height < depth_count:
            if height == 0:
                upper_part = scaled_by(upper_part, below_live)
            collected[height] = add_corners(collected[height], upper_part)
    owned = [own_nodes(corners) for corners in collected]
    stokes_residual = jnp.stack(owned, axis=1) - body_force
    depth_sum = jnp.sum(stokes_residual[:2], axis=1)
    bucket = gather_slots(depth_sum, col_row, col_col).reshape(2, 9, slot_count)
    depth_total = layer_total(bucket)
    grid_back = depth_total.reshape(2, 3, 3, slot_count)
    extended_back = with_halo(grid_back, (("mx", 1), ("my", 2)), 1)
    at_owner = extended_back[:, 0::2, 0::2].reshape(2, 9, slot_count)
    node_force = scatter_slots(at_owner.reshape(2, -1), node_row, node_col)
    coupled_residual = shelf_res - node_force
    return (coupled_residual, stokes_residual)


def solution(mesh):
    return jax.shard_map(
        per_device,
        mesh=mesh,
        in_specs=(
            P(None, "mx", "my"),
            P("mx", "my"),
            P("mx", "my"),
            P(None, "mx", "my"),
            P(None, "layer", "mx", "my"),
            P("layer", "mx", "my"),
            P(None, "layer", "mx", "my"),
            P("mx", "my"),
            P(),
            P(("mx", "my"), None, None),
            P(("mx", "my"), None, None),
        ),
        out_specs=(P(None, "mx", "my"), P(None, "layer", "mx", "my")),
        check_vma=False,
    )
```

```python
import jax
import jax.numpy as jnp
from jax import lax
from jax.sharding import PartitionSpec as P
from jax.experimental import pallas as pl
from jax.experimental.pallas import tpu as pltpu

ROWS_PAD, LANES_PAD = 24, 384


def fem_kernel(fld_ref, main_ref, weight_ref, kmat_ref, live_ref, body_ref, out_ref, vals_ref, vis_ref, resp_ref):
    main = main_ref[...] > 0.5
    weight = weight_ref[...]
    zero = jnp.zeros((ROWS_PAD, LANES_PAD), jnp.float32)
    out_ref[...] = -body_ref[...]
    pairs = fld_ref.shape[1] - 1
    for pair in range(pairs):
        vis_parts = [[], []]
        for height in range(2):
            layer = pair + height
            for comp in range(4):
                plane = fld_ref[comp, layer]
                below = pltpu.roll(plane, ROWS_PAD - 1, 0)
                right = pltpu.roll(plane, LANES_PAD - 1, 1)
                diag = pltpu.roll(below, LANES_PAD - 1, 1)
                far = jnp.where(main, diag, right)
                near = jnp.where(main, plane, below)
                if comp < 3:
                    base = height * 9 + comp * 3
                    vals_ref[0, base] = plane
                    vals_ref[0, base + 1] = below
                    vals_ref[0, base + 2] = far
                    vals_ref[1, base] = near
                    vals_ref[1, base + 1] = diag
                    vals_ref[1, base + 2] = right
                else:
                    vis_parts[0] += [plane, below, far]
                    vis_parts[1] += [near, diag, right]
        for tri in range(2):
            total = vis_parts[tri][0]
            for term in vis_parts[tri][1:]:
                total = total + term
            vis_ref[tri] = total / 6.0 * weight

        def tile_body(tile, carry):
            row = pl.multiple_of((tile // 3) * 8, 8)
            lane = pl.multiple_of((tile % 3) * 128, 128)
            for tri in range(2):
                vals = [vals_ref[tri, beta, pl.ds(row, 8), pl.ds(lane, 128)] for beta in range(18)]
                vis = vis_ref[tri, pl.ds(row, 8), pl.ds(lane, 128)]
                for alpha in range(18):
                    acc = kmat_ref[alpha, 0] * vals[0]
                    for beta in range(1, 18):
                        acc = acc + kmat_ref[alpha, beta] * vals[beta]
                    resp_ref[tri, alpha, pl.ds(row, 8), pl.ds(lane, 128)] = acc * vis
            return carry

        lax.fori_loop(0, 9, tile_body, 0)
        for height in range(2):
            own_layer = pair + height - 1
            if own_layer < 0 or own_layer > pairs - 2:
                continue
            scale = None
            if pair == 0 and height == 1:
                scale = live_ref[0]
            if pair == pairs - 1 and height == 0:
                scale = live_ref[1]
            for comp in range(3):
                base = height * 9 + comp * 3
                one = [resp_ref[0, base + v] for v in range(3)]
                two = [resp_ref[1, base + v] for v in range(3)]
                corner_a = one[0] + jnp.where(main, two[0], zero)
                corner_b = one[1] + jnp.where(main, zero, two[0])
                corner_c = two[2] + jnp.where(main, zero, one[2])
                corner_d = two[1] + jnp.where(main, one[2], zero)
                node = (pltpu.roll(pltpu.roll(corner_a, ROWS_PAD - 1, 0), LANES_PAD - 1, 1)
                        + pltpu.roll(corner_b, LANES_PAD - 1, 1)
                        + pltpu.roll(corner_c, ROWS_PAD - 1, 0) + corner_d)
                part = node[0:16, 0:256]
                if scale is not None:
                    part = part * scale
                out_ref[comp, own_layer] = out_ref[comp, own_layer] + part


def fem_pallas(extended_layers, flag_cells, weight, element_matrix, below_live, above_live, body_force):
    comps, layers, rows, lanes = extended_layers.shape
    fld = jnp.pad(extended_layers, ((0, 0), (0, 0), (0, ROWS_PAD - rows), (0, LANES_PAD - lanes)))
    cell_rows, cell_lanes = flag_cells.shape
    main = jnp.pad((flag_cells == 0).astype(jnp.float32), ((0, ROWS_PAD - cell_rows), (0, LANES_PAD - cell_lanes)))
    wpad = jnp.pad(weight, ((0, ROWS_PAD - cell_rows), (0, LANES_PAD - cell_lanes)))
    live = jnp.stack([below_live, above_live]).astype(jnp.float32)
    return pl.pallas_call(
        fem_kernel,
        out_shape=jax.ShapeDtypeStruct(body_force.shape, jnp.float32),
        in_specs=[pl.BlockSpec(memory_space=pltpu.VMEM)] * 3
        + [pl.BlockSpec(memory_space=pltpu.SMEM)] * 2
        + [pl.BlockSpec(memory_space=pltpu.VMEM)],
        out_specs=pl.BlockSpec(memory_space=pltpu.VMEM),
        scratch_shapes=[
            pltpu.VMEM((2, 18, ROWS_PAD, LANES_PAD), jnp.float32),
            pltpu.VMEM((2, ROWS_PAD, LANES_PAD), jnp.float32),
            pltpu.VMEM((2, 18, ROWS_PAD, LANES_PAD), jnp.float32),
        ],
    )(fld, main, wpad, element_matrix, live, body_force)


def with_halo(array, sides, width):
    for axis, dim in sides:
        devices, length = (lax.axis_size(axis), array.shape[dim])
        up = [(i, (i + 1) % devices) for i in range(devices - 1)]
        down = [(j, i) for i, j in up]
        last = lax.slice_in_dim(array, length - width, length, axis=dim)
        initial = lax.slice_in_dim(array, 0, width, axis=dim)
        before = lax.ppermute(last, axis, up)
        after = lax.ppermute(initial, axis, down)
        array = jnp.concatenate([before, array, after], axis=dim)
    return array


HIGH = lax.Precision.HIGHEST


def slot_selectors(index, rows, cols):
    live = index >= 0
    row_of = jnp.where(live, index // cols, -1)
    col_of = jnp.where(live, index % cols, -1)
    pick_row = (row_of[:, None] == jnp.arange(rows, dtype=jnp.int32)[None]).astype(jnp.float32)
    pick_col = col_of[:, None] == jnp.arange(cols, dtype=jnp.int32)[None]
    return pick_row, pick_col


def gather_slots(field, pick_row, pick_col):
    rows_taken = jnp.einsum("sr,krc->ksc", pick_row, field, precision=HIGH)
    return jnp.sum(jnp.where(pick_col[None], rows_taken, 0.0), axis=-1)


def scatter_slots(values, pick_row, pick_col):
    spread = jnp.where(pick_col[None], values[:, :, None], 0.0)
    return jnp.einsum("sr,ksc->krc", pick_row, spread, precision=HIGH)


def layer_total(part):
    count = lax.axis_size("layer")
    place = lax.axis_index("layer")
    received = [part]
    for shift in range(1, count):
        pairs = [(i, (i + shift) % count) for i in range(count)]
        received.append(lax.ppermute(part, "layer", pairs))
    total = None
    for source in range(count):
        wanted = (place - source) % count
        value = received[0]
        for shift in range(1, count):
            value = jnp.where(wanted == shift, received[shift], value)
        total = value if total is None else total + value
    return total


def cell_dx(plane):
    return 0.5 * (plane[1:, :-1] + plane[1:, 1:] - (plane[:-1, :-1] + plane[:-1, 1:]))


def cell_dy(plane):
    return 0.5 * (plane[:-1, 1:] + plane[1:, 1:] - (plane[:-1, :-1] + plane[1:, :-1]))


def shelf_residual(padded, friction, driving):
    u_field = padded[0]
    v_field = padded[1]
    h_field = padded[2]
    du_dx = cell_dx(u_field)
    du_dy = cell_dy(u_field)
    dv_dx = cell_dx(v_field)
    dv_dy = cell_dy(v_field)
    h_cell = 0.25 * (h_field[1:, :-1] + h_field[1:, 1:] + h_field[:-1, :-1] + h_field[:-1, 1:])
    tau_xx = h_cell * (4.0 * du_dx + 2.0 * dv_dy)
    tau_yy = h_cell * (4.0 * dv_dy + 2.0 * du_dx)
    tau_xy = h_cell * (du_dy + dv_dx)
    res_x = cell_dx(tau_xx) + cell_dy(tau_xy) - friction * u_field[1:-1, 1:-1] - driving[0]
    res_y = cell_dy(tau_yy) + cell_dx(tau_xy) - friction * v_field[1:-1, 1:-1] - driving[1]
    return jnp.stack([res_x, res_y])


def triangle(stiffness, lows, ups, weight):
    values = jnp.stack(
        [plane[comp] for group in (lows, ups) for comp in range(3) for plane in group]
    )
    viscous = (
        (lows[0][3] + lows[1][3] + lows[2][3] + ups[0][3] + ups[1][3] + ups[2][3]) / 6.0 * weight
    )
    response = (
        jnp.einsum("ab,bxy->axy", stiffness, values, precision=lax.Precision.HIGHEST) * viscous
    )
    return response.reshape((2, 3, 3) + response.shape[1:])


def cell_terms(lower, upper, flag_cells, stiffness, weight):
    low_a, low_b, low_c, low_d = (
        lower[:, :-1, :-1],
        lower[:, 1:, :-1],
        lower[:, :-1, 1:],
        lower[:, 1:, 1:],
    )
    up_a, up_b, up_c, up_d = (
        upper[:, :-1, :-1],
        upper[:, 1:, :-1],
        upper[:, :-1, 1:],
        upper[:, 1:, 1:],
    )
    main_diag = (flag_cells == 0)[None]
    low_far = jnp.where(main_diag, low_d, low_c)
    up_far = jnp.where(main_diag, up_d, up_c)
    low_near = jnp.where(main_diag, low_a, low_b)
    up_near = jnp.where(main_diag, up_a, up_b)
    tri_one = triangle(stiffness, (low_a, low_b, low_far), (up_a, up_b, up_far), weight)
    tri_two = triangle(stiffness, (low_near, low_d, low_c), (up_near, up_d, up_c), weight)
    result = []
    for height in range(2):
        resp_one = tri_one[height]
        resp_two = tri_two[height]
        corner_a = resp_one[:, 0] + jnp.where(main_diag, resp_two[:, 0], 0.0)
        corner_b = resp_one[:, 1] + jnp.where(main_diag, 0.0, resp_two[:, 0])
        corner_c = resp_two[:, 2] + jnp.where(main_diag, 0.0, resp_one[:, 2])
        corner_d = resp_two[:, 1] + jnp.where(main_diag, resp_one[:, 2], 0.0)
        result.append((corner_a, corner_b, corner_c, corner_d))
    return (result[0], result[1])


def add_corners(total, extra):
    if total is None:
        return extra
    return tuple((first_term + other_term for first_term, other_term in zip(total, extra)))


def scaled_by(corners, factor):
    return tuple((member * factor for member in corners))


def own_nodes(corners):
    corner_a, corner_b, corner_c, corner_d = corners
    return corner_a[:, 1:, 1:] + corner_b[:, :-1, 1:] + corner_c[:, 1:, :-1] + corner_d[:, :-1, :-1]


def per_device(
    ssa_velocity,
    shelf_viscosity,
    basal_friction,
    driving_stress,
    stokes_velocity,
    ice_viscosity,
    body_force,
    diagonals,
    element_matrix,
    iface_columns,
    iface_nodes,
):
    row_count = ssa_velocity.shape[1]
    col_count = ssa_velocity.shape[2]
    stacked = jnp.concatenate([ssa_velocity, shelf_viscosity[None]], 0)
    padded = with_halo(stacked, (("mx", 1), ("my", 2)), 1)
    shelf_res = shelf_residual(padded, basal_friction, driving_stress)
    owner_nodes = iface_nodes[0]
    node_live = owner_nodes >= 0
    slot_count = owner_nodes.shape[1]
    node_row, node_col = slot_selectors(owner_nodes.reshape(-1), row_count, col_count)
    outgoing = gather_slots(ssa_velocity, node_row, node_col).reshape(2, 9, slot_count)
    grid_out = outgoing.reshape(2, 3, 3, slot_count)
    extended = with_halo(grid_out, (("mx", 1), ("my", 2)), 1)
    returned = extended[:, 0::2, 0::2].reshape(2, 9, slot_count)
    depth_count = stokes_velocity.shape[1]
    block_x = stokes_velocity.shape[2]
    block_y = stokes_velocity.shape[3]
    column_count = block_x * block_y
    columns = iface_columns[0]
    col_live = columns >= 0
    col_row, col_col = slot_selectors(columns.reshape(-1), block_x, block_y)
    placed = scatter_slots(returned.reshape(2, -1), col_row, col_col)
    marked = jnp.einsum("sr,sc->rc", col_row, col_col.astype(jnp.float32)) > 0.0
    uv_part = jnp.where(
        marked.reshape(1, 1, block_x, block_y),
        placed.reshape(2, 1, block_x, block_y),
        stokes_velocity[:2],
    )
    stokes_field = jnp.concatenate([uv_part, stokes_velocity[2:3], ice_viscosity[None]], 0)
    planes = jnp.concatenate(
        [
            stokes_field.reshape(4 * depth_count, block_x, block_y),
            diagonals.astype(jnp.float32)[None],
        ],
        0,
    )
    widened = with_halo(planes, (("mx", 1), ("my", 2)), 1)
    flag_cells = widened[-1, :-1, :-1]
    field_ext = widened[:-1].reshape(4, depth_count, block_x + 2, block_y + 2)
    count_x = lax.axis_size("mx")
    count_y = lax.axis_size("my")
    place_x = lax.axis_index("mx")
    place_y = lax.axis_index("my")
    global_x = place_x * block_x + jnp.arange(block_x + 1, dtype=jnp.int32) - 1
    global_y = place_y * block_y + jnp.arange(block_y + 1, dtype=jnp.int32) - 1
    valid_x = (global_x >= 0) & (global_x <= count_x * block_x - 2)
    valid_y = (global_y >= 0) & (global_y <= count_y * block_y - 2)
    weight = (valid_x[:, None] & valid_y[None, :]).astype(jnp.float32)
    layer_index = lax.axis_index("layer")
    layer_count = lax.axis_size("layer")
    below_live = (layer_index > 0).astype(jnp.float32)
    above_live = (layer_index < layer_count - 1).astype(jnp.float32)
    extended_layers = with_halo(field_ext, (("layer", 1),), 1)
    stokes_residual = fem_pallas(
        extended_layers, flag_cells, weight, element_matrix, below_live, above_live, body_force
    )
    depth_sum = jnp.sum(stokes_residual[:2], axis=1)
    bucket = gather_slots(depth_sum, col_row, col_col).reshape(2, 9, slot_count)
    depth_total = layer_total(bucket)
    grid_back = depth_total.reshape(2, 3, 3, slot_count)
    extended_back = with_halo(grid_back, (("mx", 1), ("my", 2)), 1)
    at_owner = extended_back[:, 0::2, 0::2].reshape(2, 9, slot_count)
    node_force = scatter_slots(at_owner.reshape(2, -1), node_row, node_col)
    coupled_residual = shelf_res - node_force
    return (coupled_residual, stokes_residual)


def solution(mesh):
    return jax.shard_map(
        per_device,
        mesh=mesh,
        in_specs=(
            P(None, "mx", "my"),
            P("mx", "my"),
            P("mx", "my"),
            P(None, "mx", "my"),
            P(None, "layer", "mx", "my"),
            P("layer", "mx", "my"),
            P(None, "layer", "mx", "my"),
            P("mx", "my"),
            P(),
            P(("mx", "my"), None, None),
            P(("mx", "my"), None, None),
        ),
        out_specs=(P(None, "mx", "my"), P(None, "layer", "mx", "my")),
        check_vma=False,
    )
```

```python
import jax
import jax.numpy as jnp
from jax import lax
from jax.sharding import PartitionSpec as P
from jax.experimental import pallas as pl
from jax.experimental.pallas import tpu as pltpu

ROWS_PAD, LANES_PAD = 24, 384


def fem_kernel(fld_ref, main_ref, weight_ref, kmat_ref, live_ref, body_ref, out_ref, vals_ref, vis_ref, resp_ref):
    main = main_ref[...] > 0.5
    weight = weight_ref[...]
    zero = jnp.zeros((ROWS_PAD, LANES_PAD), jnp.float32)
    out_ref[...] = -body_ref[...]
    pairs = fld_ref.shape[1] - 1
    for pair in range(pairs):
        vis_parts = [[], []]
        for height in range(2):
            layer = pair + height
            for comp in range(4):
                plane = fld_ref[comp, layer]
                below = pltpu.roll(plane, ROWS_PAD - 1, 0)
                right = pltpu.roll(plane, LANES_PAD - 1, 1)
                diag = pltpu.roll(below, LANES_PAD - 1, 1)
                far = jnp.where(main, diag, right)
                near = jnp.where(main, plane, below)
                if comp < 3:
                    base = height * 9 + comp * 3
                    vals_ref[0, base] = plane
                    vals_ref[0, base + 1] = below
                    vals_ref[0, base + 2] = far
                    vals_ref[1, base] = near
                    vals_ref[1, base + 1] = diag
                    vals_ref[1, base + 2] = right
                else:
                    vis_parts[0] += [plane, below, far]
                    vis_parts[1] += [near, diag, right]
        for tri in range(2):
            total = vis_parts[tri][0]
            for term in vis_parts[tri][1:]:
                total = total + term
            vis_ref[tri] = total / 6.0 * weight

        def tile_body(tile, carry):
            row = pl.multiple_of((tile // 3) * 8, 8)
            lane = pl.multiple_of((tile % 3) * 128, 128)
            for tri in range(2):
                vals = [vals_ref[tri, beta, pl.ds(row, 8), pl.ds(lane, 128)] for beta in range(18)]
                vis = vis_ref[tri, pl.ds(row, 8), pl.ds(lane, 128)]
                for alpha in range(18):
                    acc = kmat_ref[alpha, 0] * vals[0]
                    for beta in range(1, 18):
                        acc = acc + kmat_ref[alpha, beta] * vals[beta]
                    resp_ref[tri, alpha, pl.ds(row, 8), pl.ds(lane, 128)] = acc * vis
            return carry

        lax.fori_loop(0, 9, tile_body, 0)
        for height in range(2):
            own_layer = pair + height - 1
            if own_layer < 0 or own_layer > pairs - 2:
                continue
            scale = None
            if pair == 0 and height == 1:
                scale = live_ref[0]
            if pair == pairs - 1 and height == 0:
                scale = live_ref[1]
            for comp in range(3):
                base = height * 9 + comp * 3
                one = [resp_ref[0, base + v] for v in range(3)]
                two = [resp_ref[1, base + v] for v in range(3)]
                corner_a = one[0] + jnp.where(main, two[0], zero)
                corner_b = one[1] + jnp.where(main, zero, two[0])
                corner_c = two[2] + jnp.where(main, zero, one[2])
                corner_d = two[1] + jnp.where(main, one[2], zero)
                node = (pltpu.roll(pltpu.roll(corner_a, ROWS_PAD - 1, 0), LANES_PAD - 1, 1)
                        + pltpu.roll(corner_b, LANES_PAD - 1, 1)
                        + pltpu.roll(corner_c, ROWS_PAD - 1, 0) + corner_d)
                part = node[0:16, 0:256]
                if scale is not None:
                    part = part * scale
                out_ref[comp, own_layer] = out_ref[comp, own_layer] + part


def fem_pallas(extended_layers, flag_cells, weight, element_matrix, below_live, above_live, body_force):
    comps, layers, rows, lanes = extended_layers.shape
    fld = jnp.pad(extended_layers, ((0, 0), (0, 0), (0, ROWS_PAD - rows), (0, LANES_PAD - lanes)))
    cell_rows, cell_lanes = flag_cells.shape
    main = jnp.pad((flag_cells == 0).astype(jnp.float32), ((0, ROWS_PAD - cell_rows), (0, LANES_PAD - cell_lanes)))
    wpad = jnp.pad(weight, ((0, ROWS_PAD - cell_rows), (0, LANES_PAD - cell_lanes)))
    live = jnp.stack([below_live, above_live]).astype(jnp.float32)
    return pl.pallas_call(
        fem_kernel,
        out_shape=jax.ShapeDtypeStruct(body_force.shape, jnp.float32),
        in_specs=[pl.BlockSpec(memory_space=pltpu.VMEM)] * 3
        + [pl.BlockSpec(memory_space=pltpu.SMEM)] * 2
        + [pl.BlockSpec(memory_space=pltpu.VMEM)],
        out_specs=pl.BlockSpec(memory_space=pltpu.VMEM),
        scratch_shapes=[
            pltpu.VMEM((2, 18, ROWS_PAD, LANES_PAD), jnp.float32),
            pltpu.VMEM((2, ROWS_PAD, LANES_PAD), jnp.float32),
            pltpu.VMEM((2, 18, ROWS_PAD, LANES_PAD), jnp.float32),
        ],
    )(fld, main, wpad, element_matrix, live, body_force)


def with_halo(array, sides, width):
    for axis, dim in sides:
        devices, length = (lax.axis_size(axis), array.shape[dim])
        up = [(i, (i + 1) % devices) for i in range(devices - 1)]
        down = [(j, i) for i, j in up]
        last = lax.slice_in_dim(array, length - width, length, axis=dim)
        initial = lax.slice_in_dim(array, 0, width, axis=dim)
        before = lax.ppermute(last, axis, up)
        after = lax.ppermute(initial, axis, down)
        array = jnp.concatenate([before, array, after], axis=dim)
    return array


HIGH = lax.Precision.HIGHEST


def slot_selectors(index, rows, cols):
    live = index >= 0
    row_of = jnp.where(live, index // cols, -1)
    col_of = jnp.where(live, index % cols, -1)
    pick_row = (row_of[:, None] == jnp.arange(rows, dtype=jnp.int32)[None]).astype(jnp.float32)
    pick_col = col_of[:, None] == jnp.arange(cols, dtype=jnp.int32)[None]
    return pick_row, pick_col


def gather_slots(field, pick_row, pick_col):
    rows_taken = jnp.einsum("sr,krc->ksc", pick_row, field, precision=HIGH)
    return jnp.sum(jnp.where(pick_col[None], rows_taken, 0.0), axis=-1)


def scatter_slots(values, pick_row, pick_col):
    spread = jnp.where(pick_col[None], values[:, :, None], 0.0)
    return jnp.einsum("sr,ksc->krc", pick_row, spread, precision=HIGH)


def layer_total(part):
    count = lax.axis_size("layer")
    place = lax.axis_index("layer")
    received = [part]
    for shift in range(1, count):
        pairs = [(i, (i + shift) % count) for i in range(count)]
        received.append(lax.ppermute(part, "layer", pairs))
    total = None
    for source in range(count):
        wanted = (place - source) % count
        value = received[0]
        for shift in range(1, count):
            value = jnp.where(wanted == shift, received[shift], value)
        total = value if total is None else total + value
    return total


def cell_dx(plane):
    return 0.5 * (plane[1:, :-1] + plane[1:, 1:] - (plane[:-1, :-1] + plane[:-1, 1:]))


def cell_dy(plane):
    return 0.5 * (plane[:-1, 1:] + plane[1:, 1:] - (plane[:-1, :-1] + plane[1:, :-1]))


def shelf_residual(padded, friction, driving):
    u_field = padded[0]
    v_field = padded[1]
    h_field = padded[2]
    du_dx = cell_dx(u_field)
    du_dy = cell_dy(u_field)
    dv_dx = cell_dx(v_field)
    dv_dy = cell_dy(v_field)
    h_cell = 0.25 * (h_field[1:, :-1] + h_field[1:, 1:] + h_field[:-1, :-1] + h_field[:-1, 1:])
    tau_xx = h_cell * (4.0 * du_dx + 2.0 * dv_dy)
    tau_yy = h_cell * (4.0 * dv_dy + 2.0 * du_dx)
    tau_xy = h_cell * (du_dy + dv_dx)
    res_x = cell_dx(tau_xx) + cell_dy(tau_xy) - friction * u_field[1:-1, 1:-1] - driving[0]
    res_y = cell_dy(tau_yy) + cell_dx(tau_xy) - friction * v_field[1:-1, 1:-1] - driving[1]
    return jnp.stack([res_x, res_y])


def triangle(stiffness, lows, ups, weight):
    values = jnp.stack(
        [plane[comp] for group in (lows, ups) for comp in range(3) for plane in group]
    )
    viscous = (
        (lows[0][3] + lows[1][3] + lows[2][3] + ups[0][3] + ups[1][3] + ups[2][3]) / 6.0 * weight
    )
    response = (
        jnp.einsum("ab,bxy->axy", stiffness, values, precision=lax.Precision.HIGHEST) * viscous
    )
    return response.reshape((2, 3, 3) + response.shape[1:])


def cell_terms(lower, upper, flag_cells, stiffness, weight):
    low_a, low_b, low_c, low_d = (
        lower[:, :-1, :-1],
        lower[:, 1:, :-1],
        lower[:, :-1, 1:],
        lower[:, 1:, 1:],
    )
    up_a, up_b, up_c, up_d = (
        upper[:, :-1, :-1],
        upper[:, 1:, :-1],
        upper[:, :-1, 1:],
        upper[:, 1:, 1:],
    )
    main_diag = (flag_cells == 0)[None]
    low_far = jnp.where(main_diag, low_d, low_c)
    up_far = jnp.where(main_diag, up_d, up_c)
    low_near = jnp.where(main_diag, low_a, low_b)
    up_near = jnp.where(main_diag, up_a, up_b)
    tri_one = triangle(stiffness, (low_a, low_b, low_far), (up_a, up_b, up_far), weight)
    tri_two = triangle(stiffness, (low_near, low_d, low_c), (up_near, up_d, up_c), weight)
    result = []
    for height in range(2):
        resp_one = tri_one[height]
        resp_two = tri_two[height]
        corner_a = resp_one[:, 0] + jnp.where(main_diag, resp_two[:, 0], 0.0)
        corner_b = resp_one[:, 1] + jnp.where(main_diag, 0.0, resp_two[:, 0])
        corner_c = resp_two[:, 2] + jnp.where(main_diag, 0.0, resp_one[:, 2])
        corner_d = resp_two[:, 1] + jnp.where(main_diag, resp_one[:, 2], 0.0)
        result.append((corner_a, corner_b, corner_c, corner_d))
    return (result[0], result[1])


def add_corners(total, extra):
    if total is None:
        return extra
    return tuple((first_term + other_term for first_term, other_term in zip(total, extra)))


def scaled_by(corners, factor):
    return tuple((member * factor for member in corners))


def own_nodes(corners):
    corner_a, corner_b, corner_c, corner_d = corners
    return corner_a[:, 1:, 1:] + corner_b[:, :-1, 1:] + corner_c[:, 1:, :-1] + corner_d[:, :-1, :-1]


def exchange(axis, sent_up, sent_down):
    count = lax.axis_size(axis)
    up = [(i, i + 1) for i in range(count - 1)]
    down = [(i + 1, i) for i in range(count - 1)]
    return lax.ppermute(sent_up, axis, up), lax.ppermute(sent_down, axis, down)


def packed_halo(arrays, dims, axis):
    ups, downs, shapes = [], [], []
    for array, dim in zip(arrays, dims):
        length = array.shape[dim]
        last = lax.slice_in_dim(array, length - 1, length, axis=dim)
        first = lax.slice_in_dim(array, 0, 1, axis=dim)
        shapes.append(last.shape)
        ups.append(last.reshape(-1))
        downs.append(first.reshape(-1))
    before, after = exchange(axis, jnp.concatenate(ups), jnp.concatenate(downs))
    widened = []
    offset = 0
    for array, dim, shape in zip(arrays, dims, shapes):
        size = 1
        for extent in shape:
            size *= extent
        head = before[offset:offset + size].reshape(shape)
        tail = after[offset:offset + size].reshape(shape)
        offset += size
        widened.append(jnp.concatenate([head, array, tail], axis=dim))
    return widened


def per_device(
    ssa_velocity,
    shelf_viscosity,
    basal_friction,
    driving_stress,
    stokes_velocity,
    ice_viscosity,
    body_force,
    diagonals,
    element_matrix,
    iface_columns,
    iface_nodes,
):
    row_count = ssa_velocity.shape[1]
    col_count = ssa_velocity.shape[2]
    depth_count = stokes_velocity.shape[1]
    block_x = stokes_velocity.shape[2]
    block_y = stokes_velocity.shape[3]
    stacked = jnp.concatenate([ssa_velocity, shelf_viscosity[None]], 0)
    owner_nodes = iface_nodes[0]
    slot_count = owner_nodes.shape[1]
    node_row, node_col = slot_selectors(owner_nodes.reshape(-1), row_count, col_count)
    outgoing = gather_slots(ssa_velocity, node_row, node_col).reshape(2, 3, 3, slot_count)
    raw_planes = jnp.concatenate(
        [
            stokes_velocity.reshape(3 * depth_count, block_x, block_y),
            ice_viscosity,
            diagonals.astype(jnp.float32)[None],
        ],
        0,
    )
    shelf_x, planes_x, slots_x = packed_halo((stacked, raw_planes, outgoing), (1, 1, 1), "mx")
    padded, widened, extended = packed_halo((shelf_x, planes_x, slots_x), (2, 2, 2), "my")
    shelf_res = shelf_residual(padded, basal_friction, driving_stress)
    returned = extended[:, 0::2, 0::2].reshape(2, 9, slot_count)
    columns = iface_columns[0]
    col_row, col_col = slot_selectors(columns.reshape(-1), block_x, block_y)
    placed = scatter_slots(returned.reshape(2, -1), col_row, col_col)
    marked = jnp.einsum("sr,sc->rc", col_row, col_col.astype(jnp.float32))
    ring = jnp.concatenate([jnp.minimum(marked, 1.0)[None], placed], 0)
    field_ext = widened[:-1].reshape(4, depth_count, block_x + 2, block_y + 2)
    flag_cells = widened[-1, :-1, :-1]
    below_raw, above_raw = exchange("layer", field_ext[:, -1], field_ext[:, 0])
    (ring_x,) = packed_halo((ring,), (1,), "mx")
    (ring_ext,) = packed_halo((ring_x,), (2,), "my")
    imposed_at = ring_ext[0] > 0.5
    all_layers = jnp.concatenate([below_raw[:, None], field_ext, above_raw[:, None]], 1)
    uv_ext = jnp.where(imposed_at[None, None], ring_ext[1:3, None], all_layers[:2])
    extended_layers = jnp.concatenate([uv_ext, all_layers[2:]], 0)
    count_x = lax.axis_size("mx")
    count_y = lax.axis_size("my")
    place_x = lax.axis_index("mx")
    place_y = lax.axis_index("my")
    global_x = place_x * block_x + jnp.arange(block_x + 1, dtype=jnp.int32) - 1
    global_y = place_y * block_y + jnp.arange(block_y + 1, dtype=jnp.int32) - 1
    valid_x = (global_x >= 0) & (global_x <= count_x * block_x - 2)
    valid_y = (global_y >= 0) & (global_y <= count_y * block_y - 2)
    weight = (valid_x[:, None] & valid_y[None, :]).astype(jnp.float32)
    layer_index = lax.axis_index("layer")
    layer_count = lax.axis_size("layer")
    below_live = (layer_index > 0).astype(jnp.float32)
    above_live = (layer_index < layer_count - 1).astype(jnp.float32)
    stokes_residual = fem_pallas(
        extended_layers, flag_cells, weight, element_matrix, below_live, above_live, body_force
    )
    depth_sum = jnp.sum(stokes_residual[:2], axis=1)
    bucket = gather_slots(depth_sum, col_row, col_col).reshape(2, 9, slot_count)
    depth_total = layer_total(bucket)
    grid_back = depth_total.reshape(2, 3, 3, slot_count)
    (back_x,) = packed_halo((grid_back,), (1,), "mx")
    (extended_back,) = packed_halo((back_x,), (2,), "my")
    at_owner = extended_back[:, 0::2, 0::2].reshape(2, 9, slot_count)
    node_force = scatter_slots(at_owner.reshape(2, -1), node_row, node_col)
    coupled_residual = shelf_res - node_force
    return (coupled_residual, stokes_residual)


def solution(mesh):
    return jax.shard_map(
        per_device,
        mesh=mesh,
        in_specs=(
            P(None, "mx", "my"),
            P("mx", "my"),
            P("mx", "my"),
            P(None, "mx", "my"),
            P(None, "layer", "mx", "my"),
            P("layer", "mx", "my"),
            P(None, "layer", "mx", "my"),
            P("mx", "my"),
            P(),
            P(("mx", "my"), None, None),
            P(("mx", "my"), None, None),
        ),
        out_specs=(P(None, "mx", "my"), P(None, "layer", "mx", "my")),
        check_vma=False,
    )
```

```python
import jax
import jax.numpy as jnp
from jax import lax
from jax.sharding import PartitionSpec as P
from jax.experimental import pallas as pl
from jax.experimental.pallas import tpu as pltpu

ROWS_PAD, LANES_PAD = 24, 384


def fem_kernel(fld_ref, main_ref, weight_ref, kmat_ref, live_ref, body_ref, out_ref, vals_ref, vis_ref, resp_ref):
    main = main_ref[...] > 0.5
    weight = weight_ref[...]
    zero = jnp.zeros((ROWS_PAD, LANES_PAD), jnp.float32)
    out_ref[...] = -body_ref[...]
    pairs = fld_ref.shape[1] - 1
    for pair in range(pairs):
        vis_parts = [[], []]
        for height in range(2):
            layer = pair + height
            for comp in range(4):
                plane = fld_ref[comp, layer]
                below = pltpu.roll(plane, ROWS_PAD - 1, 0)
                right = pltpu.roll(plane, LANES_PAD - 1, 1)
                diag = pltpu.roll(below, LANES_PAD - 1, 1)
                far = jnp.where(main, diag, right)
                near = jnp.where(main, plane, below)
                if comp < 3:
                    base = height * 9 + comp * 3
                    vals_ref[0, base] = plane
                    vals_ref[0, base + 1] = below
                    vals_ref[0, base + 2] = far
                    vals_ref[1, base] = near
                    vals_ref[1, base + 1] = diag
                    vals_ref[1, base + 2] = right
                else:
                    vis_parts[0] += [plane, below, far]
                    vis_parts[1] += [near, diag, right]
        for tri in range(2):
            total = vis_parts[tri][0]
            for term in vis_parts[tri][1:]:
                total = total + term
            vis_ref[tri] = total / 6.0 * weight

        def tile_body(block, carry):
            row = pl.multiple_of(block * 8, 8)
            for tri in range(2):
                vis = vis_ref[tri, pl.ds(row, 8), :]
                for alpha in range(18):
                    acc = kmat_ref[alpha, 0] * vals_ref[tri, 0, pl.ds(row, 8), :]
                    for beta in range(1, 18):
                        acc = acc + kmat_ref[alpha, beta] * vals_ref[tri, beta, pl.ds(row, 8), :]
                    resp_ref[tri, alpha, pl.ds(row, 8), :] = acc * vis
            return carry

        lax.fori_loop(0, ROWS_PAD // 8, tile_body, 0)
        for height in range(2):
            own_layer = pair + height - 1
            if own_layer < 0 or own_layer > pairs - 2:
                continue
            scale = None
            if pair == 0 and height == 1:
                scale = live_ref[0]
            if pair == pairs - 1 and height == 0:
                scale = live_ref[1]
            for comp in range(3):
                base = height * 9 + comp * 3
                one = [resp_ref[0, base + v] for v in range(3)]
                two = [resp_ref[1, base + v] for v in range(3)]
                corner_a = one[0] + jnp.where(main, two[0], zero)
                corner_b = one[1] + jnp.where(main, zero, two[0])
                corner_c = two[2] + jnp.where(main, zero, one[2])
                corner_d = two[1] + jnp.where(main, one[2], zero)
                node = (pltpu.roll(pltpu.roll(corner_a, ROWS_PAD - 1, 0), LANES_PAD - 1, 1)
                        + pltpu.roll(corner_b, LANES_PAD - 1, 1)
                        + pltpu.roll(corner_c, ROWS_PAD - 1, 0) + corner_d)
                part = node[0:16, 0:256]
                if scale is not None:
                    part = part * scale
                out_ref[comp, own_layer] = out_ref[comp, own_layer] + part


def fem_pallas(extended_layers, flag_cells, weight, element_matrix, below_live, above_live, body_force):
    comps, layers, rows, lanes = extended_layers.shape
    fld = jnp.pad(extended_layers, ((0, 0), (0, 0), (0, ROWS_PAD - rows), (0, LANES_PAD - lanes)))
    cell_rows, cell_lanes = flag_cells.shape
    main = jnp.pad((flag_cells == 0).astype(jnp.float32), ((0, ROWS_PAD - cell_rows), (0, LANES_PAD - cell_lanes)))
    wpad = jnp.pad(weight, ((0, ROWS_PAD - cell_rows), (0, LANES_PAD - cell_lanes)))
    live = jnp.stack([below_live, above_live]).astype(jnp.float32)
    return pl.pallas_call(
        fem_kernel,
        out_shape=jax.ShapeDtypeStruct(body_force.shape, jnp.float32),
        in_specs=[pl.BlockSpec(memory_space=pltpu.VMEM)] * 3
        + [pl.BlockSpec(memory_space=pltpu.SMEM)] * 2
        + [pl.BlockSpec(memory_space=pltpu.VMEM)],
        out_specs=pl.BlockSpec(memory_space=pltpu.VMEM),
        scratch_shapes=[
            pltpu.VMEM((2, 18, ROWS_PAD, LANES_PAD), jnp.float32),
            pltpu.VMEM((2, ROWS_PAD, LANES_PAD), jnp.float32),
            pltpu.VMEM((2, 18, ROWS_PAD, LANES_PAD), jnp.float32),
        ],
    )(fld, main, wpad, element_matrix, live, body_force)


def with_halo(array, sides, width):
    for axis, dim in sides:
        devices, length = (lax.axis_size(axis), array.shape[dim])
        up = [(i, (i + 1) % devices) for i in range(devices - 1)]
        down = [(j, i) for i, j in up]
        last = lax.slice_in_dim(array, length - width, length, axis=dim)
        initial = lax.slice_in_dim(array, 0, width, axis=dim)
        before = lax.ppermute(last, axis, up)
        after = lax.ppermute(initial, axis, down)
        array = jnp.concatenate([before, array, after], axis=dim)
    return array


HIGH = lax.Precision.HIGHEST


def slot_selectors(index, rows, cols):
    live = index >= 0
    row_of = jnp.where(live, index // cols, -1)
    col_of = jnp.where(live, index % cols, -1)
    pick_row = (row_of[:, None] == jnp.arange(rows, dtype=jnp.int32)[None]).astype(jnp.float32)
    pick_col = (col_of[:, None] == jnp.arange(cols, dtype=jnp.int32)[None]).astype(jnp.float32)
    return pick_row, pick_col


def gather_slots(field, pick_row, pick_col):
    cols_taken = jnp.einsum("krc,sc->krs", field, pick_col, precision=HIGH)
    return jnp.sum(jnp.where(pick_row.T[None] > 0.5, cols_taken, 0.0), axis=1)


def scatter_slots(values, pick_row, pick_col):
    weighted = pick_row[None] * values[:, :, None]
    return jnp.einsum("ksr,sc->krc", weighted, pick_col, precision=HIGH)


def layer_total(part):
    count = lax.axis_size("layer")
    place = lax.axis_index("layer")
    received = [part]
    for shift in range(1, count):
        pairs = [(i, (i + shift) % count) for i in range(count)]
        received.append(lax.ppermute(part, "layer", pairs))
    total = None
    for source in range(count):
        wanted = (place - source) % count
        value = received[0]
        for shift in range(1, count):
            value = jnp.where(wanted == shift, received[shift], value)
        total = value if total is None else total + value
    return total


def cell_dx(plane):
    return 0.5 * (plane[1:, :-1] + plane[1:, 1:] - (plane[:-1, :-1] + plane[:-1, 1:]))


def cell_dy(plane):
    return 0.5 * (plane[:-1, 1:] + plane[1:, 1:] - (plane[:-1, :-1] + plane[1:, :-1]))


def shelf_residual(padded, friction, driving):
    u_field = padded[0]
    v_field = padded[1]
    h_field = padded[2]
    du_dx = cell_dx(u_field)
    du_dy = cell_dy(u_field)
    dv_dx = cell_dx(v_field)
    dv_dy = cell_dy(v_field)
    h_cell = 0.25 * (h_field[1:, :-1] + h_field[1:, 1:] + h_field[:-1, :-1] + h_field[:-1, 1:])
    tau_xx = h_cell * (4.0 * du_dx + 2.0 * dv_dy)
    tau_yy = h_cell * (4.0 * dv_dy + 2.0 * du_dx)
    tau_xy = h_cell * (du_dy + dv_dx)
    res_x = cell_dx(tau_xx) + cell_dy(tau_xy) - friction * u_field[1:-1, 1:-1] - driving[0]
    res_y = cell_dy(tau_yy) + cell_dx(tau_xy) - friction * v_field[1:-1, 1:-1] - driving[1]
    return jnp.stack([res_x, res_y])


def triangle(stiffness, lows, ups, weight):
    values = jnp.stack(
        [plane[comp] for group in (lows, ups) for comp in range(3) for plane in group]
    )
    viscous = (
        (lows[0][3] + lows[1][3] + lows[2][3] + ups[0][3] + ups[1][3] + ups[2][3]) / 6.0 * weight
    )
    response = (
        jnp.einsum("ab,bxy->axy", stiffness, values, precision=lax.Precision.HIGHEST) * viscous
    )
    return response.reshape((2, 3, 3) + response.shape[1:])


def cell_terms(lower, upper, flag_cells, stiffness, weight):
    low_a, low_b, low_c, low_d = (
        lower[:, :-1, :-1],
        lower[:, 1:, :-1],
        lower[:, :-1, 1:],
        lower[:, 1:, 1:],
    )
    up_a, up_b, up_c, up_d = (
        upper[:, :-1, :-1],
        upper[:, 1:, :-1],
        upper[:, :-1, 1:],
        upper[:, 1:, 1:],
    )
    main_diag = (flag_cells == 0)[None]
    low_far = jnp.where(main_diag, low_d, low_c)
    up_far = jnp.where(main_diag, up_d, up_c)
    low_near = jnp.where(main_diag, low_a, low_b)
    up_near = jnp.where(main_diag, up_a, up_b)
    tri_one = triangle(stiffness, (low_a, low_b, low_far), (up_a, up_b, up_far), weight)
    tri_two = triangle(stiffness, (low_near, low_d, low_c), (up_near, up_d, up_c), weight)
    result = []
    for height in range(2):
        resp_one = tri_one[height]
        resp_two = tri_two[height]
        corner_a = resp_one[:, 0] + jnp.where(main_diag, resp_two[:, 0], 0.0)
        corner_b = resp_one[:, 1] + jnp.where(main_diag, 0.0, resp_two[:, 0])
        corner_c = resp_two[:, 2] + jnp.where(main_diag, 0.0, resp_one[:, 2])
        corner_d = resp_two[:, 1] + jnp.where(main_diag, resp_one[:, 2], 0.0)
        result.append((corner_a, corner_b, corner_c, corner_d))
    return (result[0], result[1])


def add_corners(total, extra):
    if total is None:
        return extra
    return tuple((first_term + other_term for first_term, other_term in zip(total, extra)))


def scaled_by(corners, factor):
    return tuple((member * factor for member in corners))


def own_nodes(corners):
    corner_a, corner_b, corner_c, corner_d = corners
    return corner_a[:, 1:, 1:] + corner_b[:, :-1, 1:] + corner_c[:, 1:, :-1] + corner_d[:, :-1, :-1]


def exchange(axis, sent_up, sent_down):
    count = lax.axis_size(axis)
    up = [(i, i + 1) for i in range(count - 1)]
    down = [(i + 1, i) for i in range(count - 1)]
    return lax.ppermute(sent_up, axis, up), lax.ppermute(sent_down, axis, down)


def packed_halo(arrays, dims, axis):
    ups, downs, shapes = [], [], []
    for array, dim in zip(arrays, dims):
        length = array.shape[dim]
        last = lax.slice_in_dim(array, length - 1, length, axis=dim)
        first = lax.slice_in_dim(array, 0, 1, axis=dim)
        shapes.append(last.shape)
        ups.append(last.reshape(-1))
        downs.append(first.reshape(-1))
    before, after = exchange(axis, jnp.concatenate(ups), jnp.concatenate(downs))
    widened = []
    offset = 0
    for array, dim, shape in zip(arrays, dims, shapes):
        size = 1
        for extent in shape:
            size *= extent
        head = before[offset:offset + size].reshape(shape)
        tail = after[offset:offset + size].reshape(shape)
        offset += size
        widened.append(jnp.concatenate([head, array, tail], axis=dim))
    return widened


def per_device(
    ssa_velocity,
    shelf_viscosity,
    basal_friction,
    driving_stress,
    stokes_velocity,
    ice_viscosity,
    body_force,
    diagonals,
    element_matrix,
    iface_columns,
    iface_nodes,
):
    row_count = ssa_velocity.shape[1]
    col_count = ssa_velocity.shape[2]
    depth_count = stokes_velocity.shape[1]
    block_x = stokes_velocity.shape[2]
    block_y = stokes_velocity.shape[3]
    stacked = jnp.concatenate([ssa_velocity, shelf_viscosity[None]], 0)
    owner_nodes = iface_nodes[0]
    slot_count = owner_nodes.shape[1]
    node_row, node_col = slot_selectors(owner_nodes.reshape(-1), row_count, col_count)
    outgoing = gather_slots(ssa_velocity, node_row, node_col).reshape(2, 3, 3, slot_count)
    raw_planes = jnp.concatenate(
        [
            stokes_velocity.reshape(3 * depth_count, block_x, block_y),
            ice_viscosity,
            diagonals.astype(jnp.float32)[None],
        ],
        0,
    )
    shelf_x, planes_x, slots_x = packed_halo((stacked, raw_planes, outgoing), (1, 1, 1), "mx")
    padded, widened, extended = packed_halo((shelf_x, planes_x, slots_x), (2, 2, 2), "my")
    shelf_res = shelf_residual(padded, basal_friction, driving_stress)
    returned = extended[:, 0::2, 0::2].reshape(2, 9, slot_count)
    columns = iface_columns[0]
    col_row, col_col = slot_selectors(columns.reshape(-1), block_x, block_y)
    placed = scatter_slots(returned.reshape(2, -1), col_row, col_col)
    marked = jnp.einsum("sr,sc->rc", col_row, col_col)
    ring = jnp.concatenate([jnp.minimum(marked, 1.0)[None], placed], 0)
    field_ext = widened[:-1].reshape(4, depth_count, block_x + 2, block_y + 2)
    flag_cells = widened[-1, :-1, :-1]
    below_raw, above_raw = exchange("layer", field_ext[:, -1], field_ext[:, 0])
    (ring_x,) = packed_halo((ring,), (1,), "mx")
    (ring_ext,) = packed_halo((ring_x,), (2,), "my")
    imposed_at = ring_ext[0] > 0.5
    all_layers = jnp.concatenate([below_raw[:, None], field_ext, above_raw[:, None]], 1)
    uv_ext = jnp.where(imposed_at[None, None], ring_ext[1:3, None], all_layers[:2])
    extended_layers = jnp.concatenate([uv_ext, all_layers[2:]], 0)
    count_x = lax.axis_size("mx")
    count_y = lax.axis_size("my")
    place_x = lax.axis_index("mx")
    place_y = lax.axis_index("my")
    global_x = place_x * block_x + jnp.arange(block_x + 1, dtype=jnp.int32) - 1
    global_y = place_y * block_y + jnp.arange(block_y + 1, dtype=jnp.int32) - 1
    valid_x = (global_x >= 0) & (global_x <= count_x * block_x - 2)
    valid_y = (global_y >= 0) & (global_y <= count_y * block_y - 2)
    weight = (valid_x[:, None] & valid_y[None, :]).astype(jnp.float32)
    layer_index = lax.axis_index("layer")
    layer_count = lax.axis_size("layer")
    below_live = (layer_index > 0).astype(jnp.float32)
    above_live = (layer_index < layer_count - 1).astype(jnp.float32)
    stokes_residual = fem_pallas(
        extended_layers, flag_cells, weight, element_matrix, below_live, above_live, body_force
    )
    depth_sum = jnp.sum(stokes_residual[:2], axis=1)
    bucket = gather_slots(depth_sum, col_row, col_col).reshape(2, 9, slot_count)
    depth_total = layer_total(bucket)
    grid_back = depth_total.reshape(2, 3, 3, slot_count)
    (back_x,) = packed_halo((grid_back,), (1,), "mx")
    (extended_back,) = packed_halo((back_x,), (2,), "my")
    at_owner = extended_back[:, 0::2, 0::2].reshape(2, 9, slot_count)
    node_force = scatter_slots(at_owner.reshape(2, -1), node_row, node_col)
    coupled_residual = shelf_res - node_force
    return (coupled_residual, stokes_residual)


def solution(mesh):
    return jax.shard_map(
        per_device,
        mesh=mesh,
        in_specs=(
            P(None, "mx", "my"),
            P("mx", "my"),
            P("mx", "my"),
            P(None, "mx", "my"),
            P(None, "layer", "mx", "my"),
            P("layer", "mx", "my"),
            P(None, "layer", "mx", "my"),
            P("mx", "my"),
            P(),
            P(("mx", "my"), None, None),
            P(("mx", "my"), None, None),
        ),
        out_specs=(P(None, "mx", "my"), P(None, "layer", "mx", "my")),
        check_vma=False,
    )
```

```python
import jax
import jax.numpy as jnp
from jax import lax
from jax.sharding import PartitionSpec as P
from jax.experimental import pallas as pl
from jax.experimental.pallas import tpu as pltpu

ROWS_PAD, LANES_PAD = 24, 384


def fem_kernel(fld_ref, main_ref, weight_ref, kmat_ref, live_ref, body_ref, out_ref, vals_ref, vis_ref, resp_ref):
    main = main_ref[...] > 0.5
    weight = weight_ref[...]
    zero = jnp.zeros((ROWS_PAD, LANES_PAD), jnp.float32)
    out_ref[...] = -body_ref[...]
    pairs = fld_ref.shape[1] - 1
    for pair in range(pairs):
        vis_parts = [[], []]
        for height in range(2):
            layer = pair + height
            for comp in range(4):
                plane = fld_ref[comp, layer]
                below = pltpu.roll(plane, ROWS_PAD - 1, 0)
                right = pltpu.roll(plane, LANES_PAD - 1, 1)
                diag = pltpu.roll(below, LANES_PAD - 1, 1)
                far = jnp.where(main, diag, right)
                near = jnp.where(main, plane, below)
                if comp < 3:
                    base = height * 9 + comp * 3
                    vals_ref[0, base] = plane
                    vals_ref[0, base + 1] = below
                    vals_ref[0, base + 2] = far
                    vals_ref[1, base] = near
                    vals_ref[1, base + 1] = diag
                    vals_ref[1, base + 2] = right
                else:
                    vis_parts[0] += [plane, below, far]
                    vis_parts[1] += [near, diag, right]
        for tri in range(2):
            total = vis_parts[tri][0]
            for term in vis_parts[tri][1:]:
                total = total + term
            vis_ref[tri] = total / 6.0 * weight

        def tile_body(block, carry):
            row = pl.multiple_of(block * 8, 8)
            for tri in range(2):
                vis = vis_ref[tri, pl.ds(row, 8), :]
                for alpha in range(18):
                    acc = kmat_ref[alpha, 0] * vals_ref[tri, 0, pl.ds(row, 8), :]
                    for beta in range(1, 18):
                        acc = acc + kmat_ref[alpha, beta] * vals_ref[tri, beta, pl.ds(row, 8), :]
                    resp_ref[tri, alpha, pl.ds(row, 8), :] = acc * vis
            return carry

        lax.fori_loop(0, ROWS_PAD // 8, tile_body, 0)
        for height in range(2):
            own_layer = pair + height - 1
            if own_layer < 0 or own_layer > pairs - 2:
                continue
            scale = None
            if pair == 0 and height == 1:
                scale = live_ref[0]
            if pair == pairs - 1 and height == 0:
                scale = live_ref[1]
            for comp in range(3):
                base = height * 9 + comp * 3
                one = [resp_ref[0, base + v] for v in range(3)]
                two = [resp_ref[1, base + v] for v in range(3)]
                corner_a = one[0] + jnp.where(main, two[0], zero)
                corner_b = one[1] + jnp.where(main, zero, two[0])
                corner_c = two[2] + jnp.where(main, zero, one[2])
                corner_d = two[1] + jnp.where(main, one[2], zero)
                node = (pltpu.roll(pltpu.roll(corner_a, ROWS_PAD - 1, 0), LANES_PAD - 1, 1)
                        + pltpu.roll(corner_b, LANES_PAD - 1, 1)
                        + pltpu.roll(corner_c, ROWS_PAD - 1, 0) + corner_d)
                part = node[0:16, 0:256]
                if scale is not None:
                    part = part * scale
                out_ref[comp, own_layer] = out_ref[comp, own_layer] + part


def fem_pallas(extended_layers, flag_cells, weight, element_matrix, below_live, above_live, body_force):
    comps, layers, rows, lanes = extended_layers.shape
    fld = jnp.pad(extended_layers, ((0, 0), (0, 0), (0, ROWS_PAD - rows), (0, LANES_PAD - lanes)))
    cell_rows, cell_lanes = flag_cells.shape
    main = jnp.pad((flag_cells == 0).astype(jnp.float32), ((0, ROWS_PAD - cell_rows), (0, LANES_PAD - cell_lanes)))
    wpad = jnp.pad(weight, ((0, ROWS_PAD - cell_rows), (0, LANES_PAD - cell_lanes)))
    live = jnp.stack([below_live, above_live]).astype(jnp.float32)
    return pl.pallas_call(
        fem_kernel,
        out_shape=jax.ShapeDtypeStruct(body_force.shape, jnp.float32),
        in_specs=[pl.BlockSpec(memory_space=pltpu.VMEM)] * 3
        + [pl.BlockSpec(memory_space=pltpu.SMEM)] * 2
        + [pl.BlockSpec(memory_space=pltpu.VMEM)],
        out_specs=pl.BlockSpec(memory_space=pltpu.VMEM),
        scratch_shapes=[
            pltpu.VMEM((2, 18, ROWS_PAD, LANES_PAD), jnp.float32),
            pltpu.VMEM((2, ROWS_PAD, LANES_PAD), jnp.float32),
            pltpu.VMEM((2, 18, ROWS_PAD, LANES_PAD), jnp.float32),
        ],
    )(fld, main, wpad, element_matrix, live, body_force)


def with_halo(array, sides, width):
    for axis, dim in sides:
        devices, length = (lax.axis_size(axis), array.shape[dim])
        up = [(i, (i + 1) % devices) for i in range(devices - 1)]
        down = [(j, i) for i, j in up]
        last = lax.slice_in_dim(array, length - width, length, axis=dim)
        initial = lax.slice_in_dim(array, 0, width, axis=dim)
        before = lax.ppermute(last, axis, up)
        after = lax.ppermute(initial, axis, down)
        array = jnp.concatenate([before, array, after], axis=dim)
    return array


HIGH = lax.Precision.HIGHEST


def slot_selectors(index, rows, cols):
    live = index >= 0
    row_of = jnp.where(live, index // cols, -1)
    col_of = jnp.where(live, index % cols, -1)
    pick_row = (row_of[:, None] == jnp.arange(rows, dtype=jnp.int32)[None]).astype(jnp.float32)
    pick_col = (col_of[:, None] == jnp.arange(cols, dtype=jnp.int32)[None]).astype(jnp.float32)
    return pick_row, pick_col


def gather_slots(field, pick_row, pick_col):
    cols_taken = jnp.einsum("krc,sc->krs", field, pick_col, precision=HIGH)
    return jnp.sum(jnp.where(pick_row.T[None] > 0.5, cols_taken, 0.0), axis=1)


def scatter_slots(values, pick_row, pick_col):
    weighted = pick_row[None] * values[:, :, None]
    return jnp.einsum("ksr,sc->krc", weighted, pick_col, precision=HIGH)


def layer_total(part):
    count = lax.axis_size("layer")
    place = lax.axis_index("layer")
    total = part
    step = 1
    while step < count:
        pairs = [(i, i ^ step) for i in range(count)]
        other = lax.ppermute(total, "layer", pairs)
        total = jnp.where((place & step) == 0, total + other, other + total)
        step *= 2
    return total


def cell_dx(plane):
    return 0.5 * (plane[1:, :-1] + plane[1:, 1:] - (plane[:-1, :-1] + plane[:-1, 1:]))


def cell_dy(plane):
    return 0.5 * (plane[:-1, 1:] + plane[1:, 1:] - (plane[:-1, :-1] + plane[1:, :-1]))


def shelf_residual(padded, friction, driving):
    u_field = padded[0]
    v_field = padded[1]
    h_field = padded[2]
    du_dx = cell_dx(u_field)
    du_dy = cell_dy(u_field)
    dv_dx = cell_dx(v_field)
    dv_dy = cell_dy(v_field)
    h_cell = 0.25 * (h_field[1:, :-1] + h_field[1:, 1:] + h_field[:-1, :-1] + h_field[:-1, 1:])
    tau_xx = h_cell * (4.0 * du_dx + 2.0 * dv_dy)
    tau_yy = h_cell * (4.0 * dv_dy + 2.0 * du_dx)
    tau_xy = h_cell * (du_dy + dv_dx)
    res_x = cell_dx(tau_xx) + cell_dy(tau_xy) - friction * u_field[1:-1, 1:-1] - driving[0]
    res_y = cell_dy(tau_yy) + cell_dx(tau_xy) - friction * v_field[1:-1, 1:-1] - driving[1]
    return jnp.stack([res_x, res_y])


def triangle(stiffness, lows, ups, weight):
    values = jnp.stack(
        [plane[comp] for group in (lows, ups) for comp in range(3) for plane in group]
    )
    viscous = (
        (lows[0][3] + lows[1][3] + lows[2][3] + ups[0][3] + ups[1][3] + ups[2][3]) / 6.0 * weight
    )
    response = (
        jnp.einsum("ab,bxy->axy", stiffness, values, precision=lax.Precision.HIGHEST) * viscous
    )
    return response.reshape((2, 3, 3) + response.shape[1:])


def cell_terms(lower, upper, flag_cells, stiffness, weight):
    low_a, low_b, low_c, low_d = (
        lower[:, :-1, :-1],
        lower[:, 1:, :-1],
        lower[:, :-1, 1:],
        lower[:, 1:, 1:],
    )
    up_a, up_b, up_c, up_d = (
        upper[:, :-1, :-1],
        upper[:, 1:, :-1],
        upper[:, :-1, 1:],
        upper[:, 1:, 1:],
    )
    main_diag = (flag_cells == 0)[None]
    low_far = jnp.where(main_diag, low_d, low_c)
    up_far = jnp.where(main_diag, up_d, up_c)
    low_near = jnp.where(main_diag, low_a, low_b)
    up_near = jnp.where(main_diag, up_a, up_b)
    tri_one = triangle(stiffness, (low_a, low_b, low_far), (up_a, up_b, up_far), weight)
    tri_two = triangle(stiffness, (low_near, low_d, low_c), (up_near, up_d, up_c), weight)
    result = []
    for height in range(2):
        resp_one = tri_one[height]
        resp_two = tri_two[height]
        corner_a = resp_one[:, 0] + jnp.where(main_diag, resp_two[:, 0], 0.0)
        corner_b = resp_one[:, 1] + jnp.where(main_diag, 0.0, resp_two[:, 0])
        corner_c = resp_two[:, 2] + jnp.where(main_diag, 0.0, resp_one[:, 2])
        corner_d = resp_two[:, 1] + jnp.where(main_diag, resp_one[:, 2], 0.0)
        result.append((corner_a, corner_b, corner_c, corner_d))
    return (result[0], result[1])


def add_corners(total, extra):
    if total is None:
        return extra
    return tuple((first_term + other_term for first_term, other_term in zip(total, extra)))


def scaled_by(corners, factor):
    return tuple((member * factor for member in corners))


def own_nodes(corners):
    corner_a, corner_b, corner_c, corner_d = corners
    return corner_a[:, 1:, 1:] + corner_b[:, :-1, 1:] + corner_c[:, 1:, :-1] + corner_d[:, :-1, :-1]


def exchange(axis, sent_up, sent_down):
    count = lax.axis_size(axis)
    up = [(i, i + 1) for i in range(count - 1)]
    down = [(i + 1, i) for i in range(count - 1)]
    return lax.ppermute(sent_up, axis, up), lax.ppermute(sent_down, axis, down)


def packed_halo(arrays, dims, axis):
    ups, downs, shapes = [], [], []
    for array, dim in zip(arrays, dims):
        length = array.shape[dim]
        last = lax.slice_in_dim(array, length - 1, length, axis=dim)
        first = lax.slice_in_dim(array, 0, 1, axis=dim)
        shapes.append(last.shape)
        ups.append(last.reshape(-1))
        downs.append(first.reshape(-1))
    before, after = exchange(axis, jnp.concatenate(ups), jnp.concatenate(downs))
    widened = []
    offset = 0
    for array, dim, shape in zip(arrays, dims, shapes):
        size = 1
        for extent in shape:
            size *= extent
        head = before[offset:offset + size].reshape(shape)
        tail = after[offset:offset + size].reshape(shape)
        offset += size
        widened.append(jnp.concatenate([head, array, tail], axis=dim))
    return widened


def per_device(
    ssa_velocity,
    shelf_viscosity,
    basal_friction,
    driving_stress,
    stokes_velocity,
    ice_viscosity,
    body_force,
    diagonals,
    element_matrix,
    iface_columns,
    iface_nodes,
):
    row_count = ssa_velocity.shape[1]
    col_count = ssa_velocity.shape[2]
    depth_count = stokes_velocity.shape[1]
    block_x = stokes_velocity.shape[2]
    block_y = stokes_velocity.shape[3]
    stacked = jnp.concatenate([ssa_velocity, shelf_viscosity[None]], 0)
    owner_nodes = iface_nodes[0]
    slot_count = owner_nodes.shape[1]
    node_row, node_col = slot_selectors(owner_nodes.reshape(-1), row_count, col_count)
    outgoing = gather_slots(ssa_velocity, node_row, node_col).reshape(2, 3, 3, slot_count)
    raw_planes = jnp.concatenate(
        [
            stokes_velocity.reshape(3 * depth_count, block_x, block_y),
            ice_viscosity,
            diagonals.astype(jnp.float32)[None],
        ],
        0,
    )
    shelf_x, planes_x, slots_x = packed_halo((stacked, raw_planes, outgoing), (1, 1, 1), "mx")
    padded, widened, extended = packed_halo((shelf_x, planes_x, slots_x), (2, 2, 2), "my")
    shelf_res = shelf_residual(padded, basal_friction, driving_stress)
    returned = extended[:, 0::2, 0::2].reshape(2, 9, slot_count)
    columns = iface_columns[0]
    col_row, col_col = slot_selectors(columns.reshape(-1), block_x, block_y)
    placed = scatter_slots(returned.reshape(2, -1), col_row, col_col)
    marked = jnp.einsum("sr,sc->rc", col_row, col_col)
    ring = jnp.concatenate([jnp.minimum(marked, 1.0)[None], placed], 0)
    field_ext = widened[:-1].reshape(4, depth_count, block_x + 2, block_y + 2)
    flag_cells = widened[-1, :-1, :-1]
    below_raw, above_raw = exchange("layer", field_ext[:, -1], field_ext[:, 0])
    (ring_x,) = packed_halo((ring,), (1,), "mx")
    (ring_ext,) = packed_halo((ring_x,), (2,), "my")
    imposed_at = ring_ext[0] > 0.5
    all_layers = jnp.concatenate([below_raw[:, None], field_ext, above_raw[:, None]], 1)
    uv_ext = jnp.where(imposed_at[None, None], ring_ext[1:3, None], all_layers[:2])
    extended_layers = jnp.concatenate([uv_ext, all_layers[2:]], 0)
    count_x = lax.axis_size("mx")
    count_y = lax.axis_size("my")
    place_x = lax.axis_index("mx")
    place_y = lax.axis_index("my")
    global_x = place_x * block_x + jnp.arange(block_x + 1, dtype=jnp.int32) - 1
    global_y = place_y * block_y + jnp.arange(block_y + 1, dtype=jnp.int32) - 1
    valid_x = (global_x >= 0) & (global_x <= count_x * block_x - 2)
    valid_y = (global_y >= 0) & (global_y <= count_y * block_y - 2)
    weight = (valid_x[:, None] & valid_y[None, :]).astype(jnp.float32)
    layer_index = lax.axis_index("layer")
    layer_count = lax.axis_size("layer")
    below_live = (layer_index > 0).astype(jnp.float32)
    above_live = (layer_index < layer_count - 1).astype(jnp.float32)
    stokes_residual = fem_pallas(
        extended_layers, flag_cells, weight, element_matrix, below_live, above_live, body_force
    )
    depth_sum = jnp.sum(stokes_residual[:2], axis=1)
    bucket = gather_slots(depth_sum, col_row, col_col).reshape(2, 9, slot_count)
    depth_total = layer_total(bucket)
    grid_back = depth_total.reshape(2, 3, 3, slot_count)
    (back_x,) = packed_halo((grid_back,), (1,), "mx")
    (extended_back,) = packed_halo((back_x,), (2,), "my")
    at_owner = extended_back[:, 0::2, 0::2].reshape(2, 9, slot_count)
    node_force = scatter_slots(at_owner.reshape(2, -1), node_row, node_col)
    coupled_residual = shelf_res - node_force
    return (coupled_residual, stokes_residual)


def solution(mesh):
    return jax.shard_map(
        per_device,
        mesh=mesh,
        in_specs=(
            P(None, "mx", "my"),
            P("mx", "my"),
            P("mx", "my"),
            P(None, "mx", "my"),
            P(None, "layer", "mx", "my"),
            P("layer", "mx", "my"),
            P(None, "layer", "mx", "my"),
            P("mx", "my"),
            P(),
            P(("mx", "my"), None, None),
            P(("mx", "my"), None, None),
        ),
        out_specs=(P(None, "mx", "my"), P(None, "layer", "mx", "my")),
        check_vma=False,
    )
```

```python
import jax
import jax.numpy as jnp
from jax import lax
from jax.sharding import PartitionSpec as P
from jax.experimental import pallas as pl
from jax.experimental.pallas import tpu as pltpu

ROWS_PAD, LANES_PAD = 24, 384


def fem_kernel(fld_ref, main_ref, weight_ref, kmat_ref, live_ref, body_ref, out_ref, vals_ref, vis_ref, resp_ref):
    main = main_ref[...] > 0.5
    weight = weight_ref[...]
    zero = jnp.zeros((ROWS_PAD, LANES_PAD), jnp.float32)
    out_ref[...] = -body_ref[...]
    pairs = fld_ref.shape[1] - 1
    for pair in range(pairs):
        vis_parts = [[], []]
        for height in range(2):
            layer = pair + height
            for comp in range(4):
                plane = fld_ref[comp, layer]
                below = pltpu.roll(plane, ROWS_PAD - 1, 0)
                right = pltpu.roll(plane, LANES_PAD - 1, 1)
                diag = pltpu.roll(below, LANES_PAD - 1, 1)
                far = jnp.where(main, diag, right)
                near = jnp.where(main, plane, below)
                if comp < 3:
                    base = height * 9 + comp * 3
                    vals_ref[0, base] = plane
                    vals_ref[0, base + 1] = below
                    vals_ref[0, base + 2] = far
                    vals_ref[1, base] = near
                    vals_ref[1, base + 1] = diag
                    vals_ref[1, base + 2] = right
                else:
                    vis_parts[0] += [plane, below, far]
                    vis_parts[1] += [near, diag, right]
        for tri in range(2):
            total = vis_parts[tri][0]
            for term in vis_parts[tri][1:]:
                total = total + term
            vis_ref[tri] = total / 6.0 * weight

        def tile_body(block, carry):
            row = pl.multiple_of(block * 8, 8)
            for tri in range(2):
                vis = vis_ref[tri, pl.ds(row, 8), :]
                for alpha in range(18):
                    acc = kmat_ref[alpha, 0] * vals_ref[tri, 0, pl.ds(row, 8), :]
                    for beta in range(1, 18):
                        acc = acc + kmat_ref[alpha, beta] * vals_ref[tri, beta, pl.ds(row, 8), :]
                    resp_ref[tri, alpha, pl.ds(row, 8), :] = acc * vis
            return carry

        lax.fori_loop(0, ROWS_PAD // 8, tile_body, 0)
        for height in range(2):
            own_layer = pair + height - 1
            if own_layer < 0 or own_layer > pairs - 2:
                continue
            scale = None
            if pair == 0 and height == 1:
                scale = live_ref[0]
            if pair == pairs - 1 and height == 0:
                scale = live_ref[1]
            for comp in range(3):
                base = height * 9 + comp * 3
                one = [resp_ref[0, base + v] for v in range(3)]
                two = [resp_ref[1, base + v] for v in range(3)]
                corner_a = one[0] + jnp.where(main, two[0], zero)
                corner_b = one[1] + jnp.where(main, zero, two[0])
                corner_c = two[2] + jnp.where(main, zero, one[2])
                corner_d = two[1] + jnp.where(main, one[2], zero)
                node = (pltpu.roll(pltpu.roll(corner_a, ROWS_PAD - 1, 0), LANES_PAD - 1, 1)
                        + pltpu.roll(corner_b, LANES_PAD - 1, 1)
                        + pltpu.roll(corner_c, ROWS_PAD - 1, 0) + corner_d)
                part = node[0:16, 0:256]
                if scale is not None:
                    part = part * scale
                out_ref[comp, own_layer] = out_ref[comp, own_layer] + part


def fem_pallas(extended_layers, flag_cells, weight, element_matrix, below_live, above_live, body_force):
    comps, layers, rows, lanes = extended_layers.shape
    fld = jnp.pad(extended_layers, ((0, 0), (0, 0), (0, ROWS_PAD - rows), (0, LANES_PAD - lanes)))
    cell_rows, cell_lanes = flag_cells.shape
    main = jnp.pad((flag_cells == 0).astype(jnp.float32), ((0, ROWS_PAD - cell_rows), (0, LANES_PAD - cell_lanes)))
    wpad = jnp.pad(weight, ((0, ROWS_PAD - cell_rows), (0, LANES_PAD - cell_lanes)))
    live = jnp.stack([below_live, above_live]).astype(jnp.float32)
    return pl.pallas_call(
        fem_kernel,
        out_shape=jax.ShapeDtypeStruct(body_force.shape, jnp.float32),
        in_specs=[pl.BlockSpec(memory_space=pltpu.VMEM)] * 3
        + [pl.BlockSpec(memory_space=pltpu.SMEM)] * 2
        + [pl.BlockSpec(memory_space=pltpu.VMEM)],
        out_specs=pl.BlockSpec(memory_space=pltpu.VMEM),
        scratch_shapes=[
            pltpu.VMEM((2, 18, ROWS_PAD, LANES_PAD), jnp.float32),
            pltpu.VMEM((2, ROWS_PAD, LANES_PAD), jnp.float32),
            pltpu.VMEM((2, 18, ROWS_PAD, LANES_PAD), jnp.float32),
        ],
    )(fld, main, wpad, element_matrix, live, body_force)


def with_halo(array, sides, width):
    for axis, dim in sides:
        devices, length = (lax.axis_size(axis), array.shape[dim])
        up = [(i, (i + 1) % devices) for i in range(devices - 1)]
        down = [(j, i) for i, j in up]
        last = lax.slice_in_dim(array, length - width, length, axis=dim)
        initial = lax.slice_in_dim(array, 0, width, axis=dim)
        before = lax.ppermute(last, axis, up)
        after = lax.ppermute(initial, axis, down)
        array = jnp.concatenate([before, array, after], axis=dim)
    return array


HIGH = lax.Precision.HIGHEST


def slot_selectors(index, rows, cols):
    live = index >= 0
    row_of = jnp.where(live, index // cols, -1)
    col_of = jnp.where(live, index % cols, -1)
    pick_row = (row_of[:, None] == jnp.arange(rows, dtype=jnp.int32)[None]).astype(jnp.float32)
    pick_col = (col_of[:, None] == jnp.arange(cols, dtype=jnp.int32)[None]).astype(jnp.float32)
    return pick_row, pick_col


def gather_slots(field, pick_row, pick_col):
    cols_taken = jnp.einsum("krc,sc->krs", field, pick_col, precision=HIGH)
    return jnp.sum(jnp.where(pick_row.T[None] > 0.5, cols_taken, 0.0), axis=1)


def scatter_slots(values, pick_row, pick_col):
    weighted = pick_row[None] * values[:, :, None]
    return jnp.einsum("ksr,sc->krc", weighted, pick_col, precision=HIGH)


def layer_total(part):
    count = lax.axis_size("layer")
    copies = jnp.broadcast_to(part[None], (count,) + part.shape)
    gathered = lax.all_to_all(copies, "layer", 0, 0, tiled=True)
    total = gathered[0]
    for source in range(1, count):
        total = total + gathered[source]
    return total


def layer_neighbours(top, bottom):
    count = lax.axis_size("layer")
    place = lax.axis_index("layer")
    chunks = []
    for target in range(count):
        chunk = jnp.where(target == place + 1, top, jnp.where(target == place - 1, bottom, 0.0))
        chunks.append(chunk[None])
    received = lax.all_to_all(jnp.concatenate(chunks, 0), "layer", 0, 0, tiled=True)
    below = jnp.zeros_like(top)
    above = jnp.zeros_like(top)
    for source in range(count):
        below = jnp.where(source == place - 1, received[source], below)
        above = jnp.where(source == place + 1, received[source], above)
    return below, above


def cell_dx(plane):
    return 0.5 * (plane[1:, :-1] + plane[1:, 1:] - (plane[:-1, :-1] + plane[:-1, 1:]))


def cell_dy(plane):
    return 0.5 * (plane[:-1, 1:] + plane[1:, 1:] - (plane[:-1, :-1] + plane[1:, :-1]))


def shelf_residual(padded, friction, driving):
    u_field = padded[0]
    v_field = padded[1]
    h_field = padded[2]
    du_dx = cell_dx(u_field)
    du_dy = cell_dy(u_field)
    dv_dx = cell_dx(v_field)
    dv_dy = cell_dy(v_field)
    h_cell = 0.25 * (h_field[1:, :-1] + h_field[1:, 1:] + h_field[:-1, :-1] + h_field[:-1, 1:])
    tau_xx = h_cell * (4.0 * du_dx + 2.0 * dv_dy)
    tau_yy = h_cell * (4.0 * dv_dy + 2.0 * du_dx)
    tau_xy = h_cell * (du_dy + dv_dx)
    res_x = cell_dx(tau_xx) + cell_dy(tau_xy) - friction * u_field[1:-1, 1:-1] - driving[0]
    res_y = cell_dy(tau_yy) + cell_dx(tau_xy) - friction * v_field[1:-1, 1:-1] - driving[1]
    return jnp.stack([res_x, res_y])


def triangle(stiffness, lows, ups, weight):
    values = jnp.stack(
        [plane[comp] for group in (lows, ups) for comp in range(3) for plane in group]
    )
    viscous = (
        (lows[0][3] + lows[1][3] + lows[2][3] + ups[0][3] + ups[1][3] + ups[2][3]) / 6.0 * weight
    )
    response = (
        jnp.einsum("ab,bxy->axy", stiffness, values, precision=lax.Precision.HIGHEST) * viscous
    )
    return response.reshape((2, 3, 3) + response.shape[1:])


def cell_terms(lower, upper, flag_cells, stiffness, weight):
    low_a, low_b, low_c, low_d = (
        lower[:, :-1, :-1],
        lower[:, 1:, :-1],
        lower[:, :-1, 1:],
        lower[:, 1:, 1:],
    )
    up_a, up_b, up_c, up_d = (
        upper[:, :-1, :-1],
        upper[:, 1:, :-1],
        upper[:, :-1, 1:],
        upper[:, 1:, 1:],
    )
    main_diag = (flag_cells == 0)[None]
    low_far = jnp.where(main_diag, low_d, low_c)
    up_far = jnp.where(main_diag, up_d, up_c)
    low_near = jnp.where(main_diag, low_a, low_b)
    up_near = jnp.where(main_diag, up_a, up_b)
    tri_one = triangle(stiffness, (low_a, low_b, low_far), (up_a, up_b, up_far), weight)
    tri_two = triangle(stiffness, (low_near, low_d, low_c), (up_near, up_d, up_c), weight)
    result = []
    for height in range(2):
        resp_one = tri_one[height]
        resp_two = tri_two[height]
        corner_a = resp_one[:, 0] + jnp.where(main_diag, resp_two[:, 0], 0.0)
        corner_b = resp_one[:, 1] + jnp.where(main_diag, 0.0, resp_two[:, 0])
        corner_c = resp_two[:, 2] + jnp.where(main_diag, 0.0, resp_one[:, 2])
        corner_d = resp_two[:, 1] + jnp.where(main_diag, resp_one[:, 2], 0.0)
        result.append((corner_a, corner_b, corner_c, corner_d))
    return (result[0], result[1])


def add_corners(total, extra):
    if total is None:
        return extra
    return tuple((first_term + other_term for first_term, other_term in zip(total, extra)))


def scaled_by(corners, factor):
    return tuple((member * factor for member in corners))


def own_nodes(corners):
    corner_a, corner_b, corner_c, corner_d = corners
    return corner_a[:, 1:, 1:] + corner_b[:, :-1, 1:] + corner_c[:, 1:, :-1] + corner_d[:, :-1, :-1]


def exchange(axis, sent_up, sent_down):
    count = lax.axis_size(axis)
    up = [(i, i + 1) for i in range(count - 1)]
    down = [(i + 1, i) for i in range(count - 1)]
    return lax.ppermute(sent_up, axis, up), lax.ppermute(sent_down, axis, down)


def packed_halo(arrays, dims, axis):
    ups, downs, shapes = [], [], []
    for array, dim in zip(arrays, dims):
        length = array.shape[dim]
        last = lax.slice_in_dim(array, length - 1, length, axis=dim)
        first = lax.slice_in_dim(array, 0, 1, axis=dim)
        shapes.append(last.shape)
        ups.append(last.reshape(-1))
        downs.append(first.reshape(-1))
    before, after = exchange(axis, jnp.concatenate(ups), jnp.concatenate(downs))
    widened = []
    offset = 0
    for array, dim, shape in zip(arrays, dims, shapes):
        size = 1
        for extent in shape:
            size *= extent
        head = before[offset:offset + size].reshape(shape)
        tail = after[offset:offset + size].reshape(shape)
        offset += size
        widened.append(jnp.concatenate([head, array, tail], axis=dim))
    return widened


def per_device(
    ssa_velocity,
    shelf_viscosity,
    basal_friction,
    driving_stress,
    stokes_velocity,
    ice_viscosity,
    body_force,
    diagonals,
    element_matrix,
    iface_columns,
    iface_nodes,
):
    row_count = ssa_velocity.shape[1]
    col_count = ssa_velocity.shape[2]
    depth_count = stokes_velocity.shape[1]
    block_x = stokes_velocity.shape[2]
    block_y = stokes_velocity.shape[3]
    stacked = jnp.concatenate([ssa_velocity, shelf_viscosity[None]], 0)
    owner_nodes = iface_nodes[0]
    slot_count = owner_nodes.shape[1]
    node_row, node_col = slot_selectors(owner_nodes.reshape(-1), row_count, col_count)
    outgoing = gather_slots(ssa_velocity, node_row, node_col).reshape(2, 3, 3, slot_count)
    raw_planes = jnp.concatenate(
        [
            stokes_velocity.reshape(3 * depth_count, block_x, block_y),
            ice_viscosity,
            diagonals.astype(jnp.float32)[None],
        ],
        0,
    )
    shelf_x, planes_x, slots_x = packed_halo((stacked, raw_planes, outgoing), (1, 1, 1), "mx")
    padded, widened, extended = packed_halo((shelf_x, planes_x, slots_x), (2, 2, 2), "my")
    shelf_res = shelf_residual(padded, basal_friction, driving_stress)
    returned = extended[:, 0::2, 0::2].reshape(2, 9, slot_count)
    columns = iface_columns[0]
    col_row, col_col = slot_selectors(columns.reshape(-1), block_x, block_y)
    placed = scatter_slots(returned.reshape(2, -1), col_row, col_col)
    marked = jnp.einsum("sr,sc->rc", col_row, col_col)
    ring = jnp.concatenate([jnp.minimum(marked, 1.0)[None], placed], 0)
    field_ext = widened[:-1].reshape(4, depth_count, block_x + 2, block_y + 2)
    flag_cells = widened[-1, :-1, :-1]
    below_raw, above_raw = layer_neighbours(field_ext[:, -1], field_ext[:, 0])
    (ring_x,) = packed_halo((ring,), (1,), "mx")
    (ring_ext,) = packed_halo((ring_x,), (2,), "my")
    imposed_at = ring_ext[0] > 0.5
    all_layers = jnp.concatenate([below_raw[:, None], field_ext, above_raw[:, None]], 1)
    uv_ext = jnp.where(imposed_at[None, None], ring_ext[1:3, None], all_layers[:2])
    extended_layers = jnp.concatenate([uv_ext, all_layers[2:]], 0)
    count_x = lax.axis_size("mx")
    count_y = lax.axis_size("my")
    place_x = lax.axis_index("mx")
    place_y = lax.axis_index("my")
    global_x = place_x * block_x + jnp.arange(block_x + 1, dtype=jnp.int32) - 1
    global_y = place_y * block_y + jnp.arange(block_y + 1, dtype=jnp.int32) - 1
    valid_x = (global_x >= 0) & (global_x <= count_x * block_x - 2)
    valid_y = (global_y >= 0) & (global_y <= count_y * block_y - 2)
    weight = (valid_x[:, None] & valid_y[None, :]).astype(jnp.float32)
    layer_index = lax.axis_index("layer")
    layer_count = lax.axis_size("layer")
    below_live = (layer_index > 0).astype(jnp.float32)
    above_live = (layer_index < layer_count - 1).astype(jnp.float32)
    stokes_residual = fem_pallas(
        extended_layers, flag_cells, weight, element_matrix, below_live, above_live, body_force
    )
    depth_sum = jnp.sum(stokes_residual[:2], axis=1)
    bucket = gather_slots(depth_sum, col_row, col_col).reshape(2, 9, slot_count)
    depth_total = layer_total(bucket)
    grid_back = depth_total.reshape(2, 3, 3, slot_count)
    (back_x,) = packed_halo((grid_back,), (1,), "mx")
    (extended_back,) = packed_halo((back_x,), (2,), "my")
    at_owner = extended_back[:, 0::2, 0::2].reshape(2, 9, slot_count)
    node_force = scatter_slots(at_owner.reshape(2, -1), node_row, node_col)
    coupled_residual = shelf_res - node_force
    return (coupled_residual, stokes_residual)


def solution(mesh):
    return jax.shard_map(
        per_device,
        mesh=mesh,
        in_specs=(
            P(None, "mx", "my"),
            P("mx", "my"),
            P("mx", "my"),
            P(None, "mx", "my"),
            P(None, "layer", "mx", "my"),
            P("layer", "mx", "my"),
            P(None, "layer", "mx", "my"),
            P("mx", "my"),
            P(),
            P(("mx", "my"), None, None),
            P(("mx", "my"), None, None),
        ),
        out_specs=(P(None, "mx", "my"), P(None, "layer", "mx", "my")),
        check_vma=False,
    )
```

```python
import jax
import jax.numpy as jnp
from jax import lax
from jax.sharding import PartitionSpec as P
from jax.experimental import pallas as pl
from jax.experimental.pallas import tpu as pltpu

ROWS_PAD, LANES_PAD = 24, 384


def fem_kernel(fld_ref, main_ref, weight_ref, kmat_ref, live_ref, body_ref, out_ref, vals_ref, vis_ref, resp_ref):
    main = main_ref[...] > 0.5
    weight = weight_ref[...]
    zero = jnp.zeros((ROWS_PAD, LANES_PAD), jnp.float32)
    out_ref[...] = -body_ref[...]
    pairs = fld_ref.shape[1] - 1
    for pair in range(pairs):
        vis_parts = [[], []]
        for height in range(2):
            layer = pair + height
            for comp in range(4):
                plane = fld_ref[comp, layer]
                below = pltpu.roll(plane, ROWS_PAD - 1, 0)
                right = pltpu.roll(plane, LANES_PAD - 1, 1)
                diag = pltpu.roll(below, LANES_PAD - 1, 1)
                far = jnp.where(main, diag, right)
                near = jnp.where(main, plane, below)
                if comp < 3:
                    base = height * 9 + comp * 3
                    vals_ref[0, base] = plane
                    vals_ref[0, base + 1] = below
                    vals_ref[0, base + 2] = far
                    vals_ref[1, base] = near
                    vals_ref[1, base + 1] = diag
                    vals_ref[1, base + 2] = right
                else:
                    vis_parts[0] += [plane, below, far]
                    vis_parts[1] += [near, diag, right]
        for tri in range(2):
            total = vis_parts[tri][0]
            for term in vis_parts[tri][1:]:
                total = total + term
            vis_ref[tri] = total / 6.0 * weight

        def tile_body(block, carry):
            row = pl.multiple_of(block * 8, 8)
            for tri in range(2):
                vis = vis_ref[tri, pl.ds(row, 8), :]
                for alpha in range(18):
                    acc = kmat_ref[alpha, 0] * vals_ref[tri, 0, pl.ds(row, 8), :]
                    for beta in range(1, 18):
                        acc = acc + kmat_ref[alpha, beta] * vals_ref[tri, beta, pl.ds(row, 8), :]
                    resp_ref[tri, alpha, pl.ds(row, 8), :] = acc * vis
            return carry

        lax.fori_loop(0, ROWS_PAD // 8, tile_body, 0)
        for height in range(2):
            own_layer = pair + height - 1
            if own_layer < 0 or own_layer > pairs - 2:
                continue
            scale = None
            if pair == 0 and height == 1:
                scale = live_ref[0]
            if pair == pairs - 1 and height == 0:
                scale = live_ref[1]
            for comp in range(3):
                base = height * 9 + comp * 3
                one = [resp_ref[0, base + v] for v in range(3)]
                two = [resp_ref[1, base + v] for v in range(3)]
                corner_a = one[0] + jnp.where(main, two[0], zero)
                corner_b = one[1] + jnp.where(main, zero, two[0])
                corner_c = two[2] + jnp.where(main, zero, one[2])
                corner_d = two[1] + jnp.where(main, one[2], zero)
                node = (pltpu.roll(pltpu.roll(corner_a, ROWS_PAD - 1, 0), LANES_PAD - 1, 1)
                        + pltpu.roll(corner_b, LANES_PAD - 1, 1)
                        + pltpu.roll(corner_c, ROWS_PAD - 1, 0) + corner_d)
                part = node[0:16, 0:256]
                if scale is not None:
                    part = part * scale
                out_ref[comp, own_layer] = out_ref[comp, own_layer] + part


def fem_pallas(extended_layers, flag_cells, weight, element_matrix, below_live, above_live, body_force):
    comps, layers, rows, lanes = extended_layers.shape
    fld = jnp.pad(extended_layers, ((0, 0), (0, 0), (0, ROWS_PAD - rows), (0, LANES_PAD - lanes)))
    cell_rows, cell_lanes = flag_cells.shape
    main = jnp.pad((flag_cells == 0).astype(jnp.float32), ((0, ROWS_PAD - cell_rows), (0, LANES_PAD - cell_lanes)))
    wpad = jnp.pad(weight, ((0, ROWS_PAD - cell_rows), (0, LANES_PAD - cell_lanes)))
    live = jnp.stack([below_live, above_live]).astype(jnp.float32)
    return pl.pallas_call(
        fem_kernel,
        out_shape=jax.ShapeDtypeStruct(body_force.shape, jnp.float32),
        in_specs=[pl.BlockSpec(memory_space=pltpu.VMEM)] * 3
        + [pl.BlockSpec(memory_space=pltpu.SMEM)] * 2
        + [pl.BlockSpec(memory_space=pltpu.VMEM)],
        out_specs=pl.BlockSpec(memory_space=pltpu.VMEM),
        scratch_shapes=[
            pltpu.VMEM((2, 18, ROWS_PAD, LANES_PAD), jnp.float32),
            pltpu.VMEM((2, ROWS_PAD, LANES_PAD), jnp.float32),
            pltpu.VMEM((2, 18, ROWS_PAD, LANES_PAD), jnp.float32),
        ],
    )(fld, main, wpad, element_matrix, live, body_force)


def with_halo(array, sides, width):
    for axis, dim in sides:
        devices, length = (lax.axis_size(axis), array.shape[dim])
        up = [(i, (i + 1) % devices) for i in range(devices - 1)]
        down = [(j, i) for i, j in up]
        last = lax.slice_in_dim(array, length - width, length, axis=dim)
        initial = lax.slice_in_dim(array, 0, width, axis=dim)
        before = lax.ppermute(last, axis, up)
        after = lax.ppermute(initial, axis, down)
        array = jnp.concatenate([before, array, after], axis=dim)
    return array


HIGH = lax.Precision.HIGHEST


def slot_selectors(index, rows, cols):
    live = index >= 0
    row_of = jnp.where(live, index // cols, -1)
    col_of = jnp.where(live, index % cols, -1)
    pick_row = (row_of[:, None] == jnp.arange(rows, dtype=jnp.int32)[None]).astype(jnp.float32)
    pick_col = (col_of[:, None] == jnp.arange(cols, dtype=jnp.int32)[None]).astype(jnp.float32)
    return pick_row, pick_col


def gather_slots(field, pick_row, pick_col):
    cols_taken = jnp.einsum("krc,sc->krs", field, pick_col, precision=HIGH)
    return jnp.sum(jnp.where(pick_row.T[None] > 0.5, cols_taken, 0.0), axis=1)


def scatter_slots(values, pick_row, pick_col):
    weighted = pick_row[None] * values[:, :, None]
    return jnp.einsum("ksr,sc->krc", weighted, pick_col, precision=HIGH)


def layer_total(part):
    count = lax.axis_size("layer")
    copies = jnp.broadcast_to(part[None], (count,) + part.shape)
    gathered = lax.all_to_all(copies, "layer", 0, 0, tiled=True)
    total = gathered[0]
    for source in range(1, count):
        total = total + gathered[source]
    return total


def cell_dx(plane):
    return 0.5 * (plane[1:, :-1] + plane[1:, 1:] - (plane[:-1, :-1] + plane[:-1, 1:]))


def cell_dy(plane):
    return 0.5 * (plane[:-1, 1:] + plane[1:, 1:] - (plane[:-1, :-1] + plane[1:, :-1]))


def shelf_residual(padded, friction, driving):
    u_field = padded[0]
    v_field = padded[1]
    h_field = padded[2]
    du_dx = cell_dx(u_field)
    du_dy = cell_dy(u_field)
    dv_dx = cell_dx(v_field)
    dv_dy = cell_dy(v_field)
    h_cell = 0.25 * (h_field[1:, :-1] + h_field[1:, 1:] + h_field[:-1, :-1] + h_field[:-1, 1:])
    tau_xx = h_cell * (4.0 * du_dx + 2.0 * dv_dy)
    tau_yy = h_cell * (4.0 * dv_dy + 2.0 * du_dx)
    tau_xy = h_cell * (du_dy + dv_dx)
    res_x = cell_dx(tau_xx) + cell_dy(tau_xy) - friction * u_field[1:-1, 1:-1] - driving[0]
    res_y = cell_dy(tau_yy) + cell_dx(tau_xy) - friction * v_field[1:-1, 1:-1] - driving[1]
    return jnp.stack([res_x, res_y])


def triangle(stiffness, lows, ups, weight):
    values = jnp.stack(
        [plane[comp] for group in (lows, ups) for comp in range(3) for plane in group]
    )
    viscous = (
        (lows[0][3] + lows[1][3] + lows[2][3] + ups[0][3] + ups[1][3] + ups[2][3]) / 6.0 * weight
    )
    response = (
        jnp.einsum("ab,bxy->axy", stiffness, values, precision=lax.Precision.HIGHEST) * viscous
    )
    return response.reshape((2, 3, 3) + response.shape[1:])


def cell_terms(lower, upper, flag_cells, stiffness, weight):
    low_a, low_b, low_c, low_d = (
        lower[:, :-1, :-1],
        lower[:, 1:, :-1],
        lower[:, :-1, 1:],
        lower[:, 1:, 1:],
    )
    up_a, up_b, up_c, up_d = (
        upper[:, :-1, :-1],
        upper[:, 1:, :-1],
        upper[:, :-1, 1:],
        upper[:, 1:, 1:],
    )
    main_diag = (flag_cells == 0)[None]
    low_far = jnp.where(main_diag, low_d, low_c)
    up_far = jnp.where(main_diag, up_d, up_c)
    low_near = jnp.where(main_diag, low_a, low_b)
    up_near = jnp.where(main_diag, up_a, up_b)
    tri_one = triangle(stiffness, (low_a, low_b, low_far), (up_a, up_b, up_far), weight)
    tri_two = triangle(stiffness, (low_near, low_d, low_c), (up_near, up_d, up_c), weight)
    result = []
    for height in range(2):
        resp_one = tri_one[height]
        resp_two = tri_two[height]
        corner_a = resp_one[:, 0] + jnp.where(main_diag, resp_two[:, 0], 0.0)
        corner_b = resp_one[:, 1] + jnp.where(main_diag, 0.0, resp_two[:, 0])
        corner_c = resp_two[:, 2] + jnp.where(main_diag, 0.0, resp_one[:, 2])
        corner_d = resp_two[:, 1] + jnp.where(main_diag, resp_one[:, 2], 0.0)
        result.append((corner_a, corner_b, corner_c, corner_d))
    return (result[0], result[1])


def add_corners(total, extra):
    if total is None:
        return extra
    return tuple((first_term + other_term for first_term, other_term in zip(total, extra)))


def scaled_by(corners, factor):
    return tuple((member * factor for member in corners))


def own_nodes(corners):
    corner_a, corner_b, corner_c, corner_d = corners
    return corner_a[:, 1:, 1:] + corner_b[:, :-1, 1:] + corner_c[:, 1:, :-1] + corner_d[:, :-1, :-1]


def exchange(axis, sent_up, sent_down):
    count = lax.axis_size(axis)
    if count > 4:
        up = [(i, i + 1) for i in range(count - 1)]
        down = [(i + 1, i) for i in range(count - 1)]
        return lax.ppermute(sent_up, axis, up), lax.ppermute(sent_down, axis, down)
    place = lax.axis_index(axis)
    chunks = []
    for target in range(count):
        chunk = jnp.where(target == place + 1, sent_up, jnp.where(target == place - 1, sent_down, 0.0))
        chunks.append(chunk[None])
    received = lax.all_to_all(jnp.concatenate(chunks, 0), axis, 0, 0, tiled=True)
    before = jnp.zeros_like(sent_up)
    after = jnp.zeros_like(sent_down)
    for source in range(count):
        before = jnp.where(source == place - 1, received[source], before)
        after = jnp.where(source == place + 1, received[source], after)
    return before, after


def packed_halo(arrays, dims, axis):
    ups, downs, shapes = [], [], []
    for array, dim in zip(arrays, dims):
        length = array.shape[dim]
        last = lax.slice_in_dim(array, length - 1, length, axis=dim)
        first = lax.slice_in_dim(array, 0, 1, axis=dim)
        shapes.append(last.shape)
        ups.append(last.reshape(-1))
        downs.append(first.reshape(-1))
    before, after = exchange(axis, jnp.concatenate(ups), jnp.concatenate(downs))
    widened = []
    offset = 0
    for array, dim, shape in zip(arrays, dims, shapes):
        size = 1
        for extent in shape:
            size *= extent
        head = before[offset:offset + size].reshape(shape)
        tail = after[offset:offset + size].reshape(shape)
        offset += size
        widened.append(jnp.concatenate([head, array, tail], axis=dim))
    return widened


def per_device(
    ssa_velocity,
    shelf_viscosity,
    basal_friction,
    driving_stress,
    stokes_velocity,
    ice_viscosity,
    body_force,
    diagonals,
    element_matrix,
    iface_columns,
    iface_nodes,
):
    row_count = ssa_velocity.shape[1]
    col_count = ssa_velocity.shape[2]
    depth_count = stokes_velocity.shape[1]
    block_x = stokes_velocity.shape[2]
    block_y = stokes_velocity.shape[3]
    stacked = jnp.concatenate([ssa_velocity, shelf_viscosity[None]], 0)
    owner_nodes = iface_nodes[0]
    slot_count = owner_nodes.shape[1]
    node_row, node_col = slot_selectors(owner_nodes.reshape(-1), row_count, col_count)
    outgoing = gather_slots(ssa_velocity, node_row, node_col).reshape(2, 3, 3, slot_count)
    raw_planes = jnp.concatenate(
        [
            stokes_velocity.reshape(3 * depth_count, block_x, block_y),
            ice_viscosity,
            diagonals.astype(jnp.float32)[None],
        ],
        0,
    )
    shelf_x, planes_x, slots_x = packed_halo((stacked, raw_planes, outgoing), (1, 1, 1), "mx")
    padded, widened, extended = packed_halo((shelf_x, planes_x, slots_x), (2, 2, 2), "my")
    shelf_res = shelf_residual(padded, basal_friction, driving_stress)
    returned = extended[:, 0::2, 0::2].reshape(2, 9, slot_count)
    columns = iface_columns[0]
    col_row, col_col = slot_selectors(columns.reshape(-1), block_x, block_y)
    placed = scatter_slots(returned.reshape(2, -1), col_row, col_col)
    marked = jnp.einsum("sr,sc->rc", col_row, col_col)
    ring = jnp.concatenate([jnp.minimum(marked, 1.0)[None], placed], 0)
    field_ext = widened[:-1].reshape(4, depth_count, block_x + 2, block_y + 2)
    flag_cells = widened[-1, :-1, :-1]
    below_raw, above_raw = exchange("layer", field_ext[:, -1], field_ext[:, 0])
    (ring_x,) = packed_halo((ring,), (1,), "mx")
    (ring_ext,) = packed_halo((ring_x,), (2,), "my")
    imposed_at = ring_ext[0] > 0.5
    all_layers = jnp.concatenate([below_raw[:, None], field_ext, above_raw[:, None]], 1)
    uv_ext = jnp.where(imposed_at[None, None], ring_ext[1:3, None], all_layers[:2])
    extended_layers = jnp.concatenate([uv_ext, all_layers[2:]], 0)
    count_x = lax.axis_size("mx")
    count_y = lax.axis_size("my")
    place_x = lax.axis_index("mx")
    place_y = lax.axis_index("my")
    global_x = place_x * block_x + jnp.arange(block_x + 1, dtype=jnp.int32) - 1
    global_y = place_y * block_y + jnp.arange(block_y + 1, dtype=jnp.int32) - 1
    valid_x = (global_x >= 0) & (global_x <= count_x * block_x - 2)
    valid_y = (global_y >= 0) & (global_y <= count_y * block_y - 2)
    weight = (valid_x[:, None] & valid_y[None, :]).astype(jnp.float32)
    layer_index = lax.axis_index("layer")
    layer_count = lax.axis_size("layer")
    below_live = (layer_index > 0).astype(jnp.float32)
    above_live = (layer_index < layer_count - 1).astype(jnp.float32)
    stokes_residual = fem_pallas(
        extended_layers, flag_cells, weight, element_matrix, below_live, above_live, body_force
    )
    depth_sum = jnp.sum(stokes_residual[:2], axis=1)
    bucket = gather_slots(depth_sum, col_row, col_col).reshape(2, 9, slot_count)
    depth_total = layer_total(bucket)
    grid_back = depth_total.reshape(2, 3, 3, slot_count)
    (back_x,) = packed_halo((grid_back,), (1,), "mx")
    (extended_back,) = packed_halo((back_x,), (2,), "my")
    at_owner = extended_back[:, 0::2, 0::2].reshape(2, 9, slot_count)
    node_force = scatter_slots(at_owner.reshape(2, -1), node_row, node_col)
    coupled_residual = shelf_res - node_force
    return (coupled_residual, stokes_residual)


def solution(mesh):
    return jax.shard_map(
        per_device,
        mesh=mesh,
        in_specs=(
            P(None, "mx", "my"),
            P("mx", "my"),
            P("mx", "my"),
            P(None, "mx", "my"),
            P(None, "layer", "mx", "my"),
            P("layer", "mx", "my"),
            P(None, "layer", "mx", "my"),
            P("mx", "my"),
            P(),
            P(("mx", "my"), None, None),
            P(("mx", "my"), None, None),
        ),
        out_specs=(P(None, "mx", "my"), P(None, "layer", "mx", "my")),
        check_vma=False,
    )
```

```python
import jax
import jax.numpy as jnp
from jax import lax
from jax.sharding import PartitionSpec as P
from jax.experimental import pallas as pl
from jax.experimental.pallas import tpu as pltpu

ROWS_PAD, LANES_PAD = 24, 384


def fem_body(comps, fld_ref, main_ref, weight_ref, kmat_ref, live_ref, body_ref, out_ref, vals_ref, vis_ref, resp_ref):
    main = main_ref[...] > 0.5
    weight = weight_ref[...]
    zero = jnp.zeros((ROWS_PAD, LANES_PAD), jnp.float32)
    for comp in comps:
        out_ref[comp] = -body_ref[comp]
    rows_out = [height * 9 + comp * 3 + vertex for height in range(2) for comp in comps for vertex in range(3)]
    pairs = fld_ref.shape[1] - 1
    for pair in range(pairs):
        vis_parts = [[], []]
        for height in range(2):
            layer = pair + height
            for comp in range(4):
                plane = fld_ref[comp, layer]
                below = pltpu.roll(plane, ROWS_PAD - 1, 0)
                right = pltpu.roll(plane, LANES_PAD - 1, 1)
                diag = pltpu.roll(below, LANES_PAD - 1, 1)
                far = jnp.where(main, diag, right)
                near = jnp.where(main, plane, below)
                if comp < 3:
                    base = height * 9 + comp * 3
                    vals_ref[0, base] = plane
                    vals_ref[0, base + 1] = below
                    vals_ref[0, base + 2] = far
                    vals_ref[1, base] = near
                    vals_ref[1, base + 1] = diag
                    vals_ref[1, base + 2] = right
                else:
                    vis_parts[0] += [plane, below, far]
                    vis_parts[1] += [near, diag, right]
        for tri in range(2):
            total = vis_parts[tri][0]
            for term in vis_parts[tri][1:]:
                total = total + term
            vis_ref[tri] = total / 6.0 * weight

        def tile_body(block, carry):
            row = pl.multiple_of(block * 8, 8)
            for tri in range(2):
                vis = vis_ref[tri, pl.ds(row, 8), :]
                for alpha in rows_out:
                    acc = kmat_ref[alpha, 0] * vals_ref[tri, 0, pl.ds(row, 8), :]
                    for beta in range(1, 18):
                        acc = acc + kmat_ref[alpha, beta] * vals_ref[tri, beta, pl.ds(row, 8), :]
                    resp_ref[tri, alpha, pl.ds(row, 8), :] = acc * vis
            return carry

        lax.fori_loop(0, ROWS_PAD // 8, tile_body, 0)
        for height in range(2):
            own_layer = pair + height - 1
            if own_layer < 0 or own_layer > pairs - 2:
                continue
            scale = None
            if pair == 0 and height == 1:
                scale = live_ref[0]
            if pair == pairs - 1 and height == 0:
                scale = live_ref[1]
            for comp in comps:
                base = height * 9 + comp * 3
                one = [resp_ref[0, base + v] for v in range(3)]
                two = [resp_ref[1, base + v] for v in range(3)]
                corner_a = one[0] + jnp.where(main, two[0], zero)
                corner_b = one[1] + jnp.where(main, zero, two[0])
                corner_c = two[2] + jnp.where(main, zero, one[2])
                corner_d = two[1] + jnp.where(main, one[2], zero)
                node = (pltpu.roll(pltpu.roll(corner_a, ROWS_PAD - 1, 0), LANES_PAD - 1, 1)
                        + pltpu.roll(corner_b, LANES_PAD - 1, 1)
                        + pltpu.roll(corner_c, ROWS_PAD - 1, 0) + corner_d)
                part = node[0:16, 0:256]
                if scale is not None:
                    part = part * scale
                out_ref[comp, own_layer] = out_ref[comp, own_layer] + part


def fem_horizontal(fld_ref, main_ref, weight_ref, kmat_ref, live_ref, body_ref, out_ref, depth_ref, vals_ref, vis_ref, resp_ref):
    fem_body((0, 1), fld_ref, main_ref, weight_ref, kmat_ref, live_ref, body_ref, out_ref, vals_ref, vis_ref, resp_ref)
    for comp in range(2):
        total = out_ref[comp, 0]
        for layer in range(1, out_ref.shape[1]):
            total = total + out_ref[comp, layer]
        depth_ref[comp] = total


def fem_vertical(fld_ref, main_ref, weight_ref, kmat_ref, live_ref, body_ref, prev_ref, out_ref, vals_ref, vis_ref, resp_ref):
    out_ref[0:2] = prev_ref[0:2]
    fem_body((2,), fld_ref, main_ref, weight_ref, kmat_ref, live_ref, body_ref, out_ref, vals_ref, vis_ref, resp_ref)


def fem_inputs(extended_layers, flag_cells, weight, below_live, above_live):
    comps, layers, rows, lanes = extended_layers.shape
    fld = jnp.pad(extended_layers, ((0, 0), (0, 0), (0, ROWS_PAD - rows), (0, LANES_PAD - lanes)))
    cell_rows, cell_lanes = flag_cells.shape
    main = jnp.pad((flag_cells == 0).astype(jnp.float32), ((0, ROWS_PAD - cell_rows), (0, LANES_PAD - cell_lanes)))
    wpad = jnp.pad(weight, ((0, ROWS_PAD - cell_rows), (0, LANES_PAD - cell_lanes)))
    live = jnp.stack([below_live, above_live]).astype(jnp.float32)
    return fld, main, wpad, live


def fem_scratch():
    return [
        pltpu.VMEM((2, 18, ROWS_PAD, LANES_PAD), jnp.float32),
        pltpu.VMEM((2, ROWS_PAD, LANES_PAD), jnp.float32),
        pltpu.VMEM((2, 18, ROWS_PAD, LANES_PAD), jnp.float32),
    ]


def fem_first(fld, main, wpad, element_matrix, live, body_force):
    vmem = pl.BlockSpec(memory_space=pltpu.VMEM)
    smem = pl.BlockSpec(memory_space=pltpu.SMEM)
    depth_shape = (2,) + body_force.shape[2:]
    return pl.pallas_call(
        fem_horizontal,
        out_shape=(
            jax.ShapeDtypeStruct(body_force.shape, jnp.float32),
            jax.ShapeDtypeStruct(depth_shape, jnp.float32),
        ),
        in_specs=[vmem, vmem, vmem, smem, smem, vmem],
        out_specs=(vmem, vmem),
        scratch_shapes=fem_scratch(),
    )(fld, main, wpad, element_matrix, live, body_force)


def fem_second(fld, main, wpad, element_matrix, live, body_force, previous):
    vmem = pl.BlockSpec(memory_space=pltpu.VMEM)
    smem = pl.BlockSpec(memory_space=pltpu.SMEM)
    return pl.pallas_call(
        fem_vertical,
        out_shape=jax.ShapeDtypeStruct(body_force.shape, jnp.float32),
        in_specs=[vmem, vmem, vmem, smem, smem, vmem, vmem],
        out_specs=vmem,
        scratch_shapes=fem_scratch(),
    )(fld, main, wpad, element_matrix, live, body_force, previous)


HIGH = lax.Precision.HIGHEST


def slot_selectors(index, rows, cols):
    live = index >= 0
    row_of = jnp.where(live, index // cols, -1)
    col_of = jnp.where(live, index % cols, -1)
    pick_row = (row_of[:, None] == jnp.arange(rows, dtype=jnp.int32)[None]).astype(jnp.float32)
    pick_col = (col_of[:, None] == jnp.arange(cols, dtype=jnp.int32)[None]).astype(jnp.float32)
    return pick_row, pick_col


def gather_slots(field, pick_row, pick_col):
    cols_taken = jnp.einsum("krc,sc->krs", field, pick_col, precision=HIGH)
    return jnp.sum(jnp.where(pick_row.T[None] > 0.5, cols_taken, 0.0), axis=1)


def scatter_slots(values, pick_row, pick_col):
    weighted = pick_row[None] * values[:, :, None]
    return jnp.einsum("ksr,sc->krc", weighted, pick_col, precision=HIGH)


def layer_total(part):
    count = lax.axis_size("layer")
    copies = jnp.broadcast_to(part[None], (count,) + part.shape)
    gathered = lax.all_to_all(copies, "layer", 0, 0, tiled=True)
    total = gathered[0]
    for source in range(1, count):
        total = total + gathered[source]
    return total


def layer_neighbours(top, bottom):
    count = lax.axis_size("layer")
    place = lax.axis_index("layer")
    chunks = []
    for target in range(count):
        chunk = jnp.where(target == place + 1, top, jnp.where(target == place - 1, bottom, 0.0))
        chunks.append(chunk[None])
    received = lax.all_to_all(jnp.concatenate(chunks, 0), "layer", 0, 0, tiled=True)
    below = jnp.zeros_like(top)
    above = jnp.zeros_like(top)
    for source in range(count):
        below = jnp.where(source == place - 1, received[source], below)
        above = jnp.where(source == place + 1, received[source], above)
    return below, above


def cell_dx(plane):
    return 0.5 * (plane[1:, :-1] + plane[1:, 1:] - (plane[:-1, :-1] + plane[:-1, 1:]))


def cell_dy(plane):
    return 0.5 * (plane[:-1, 1:] + plane[1:, 1:] - (plane[:-1, :-1] + plane[1:, :-1]))


def shelf_residual(padded, friction, driving):
    u_field = padded[0]
    v_field = padded[1]
    h_field = padded[2]
    du_dx = cell_dx(u_field)
    du_dy = cell_dy(u_field)
    dv_dx = cell_dx(v_field)
    dv_dy = cell_dy(v_field)
    h_cell = 0.25 * (h_field[1:, :-1] + h_field[1:, 1:] + h_field[:-1, :-1] + h_field[:-1, 1:])
    tau_xx = h_cell * (4.0 * du_dx + 2.0 * dv_dy)
    tau_yy = h_cell * (4.0 * dv_dy + 2.0 * du_dx)
    tau_xy = h_cell * (du_dy + dv_dx)
    res_x = cell_dx(tau_xx) + cell_dy(tau_xy) - friction * u_field[1:-1, 1:-1] - driving[0]
    res_y = cell_dy(tau_yy) + cell_dx(tau_xy) - friction * v_field[1:-1, 1:-1] - driving[1]
    return jnp.stack([res_x, res_y])


def triangle(stiffness, lows, ups, weight):
    values = jnp.stack(
        [plane[comp] for group in (lows, ups) for comp in range(3) for plane in group]
    )
    viscous = (
        (lows[0][3] + lows[1][3] + lows[2][3] + ups[0][3] + ups[1][3] + ups[2][3]) / 6.0 * weight
    )
    response = (
        jnp.einsum("ab,bxy->axy", stiffness, values, precision=lax.Precision.HIGHEST) * viscous
    )
    return response.reshape((2, 3, 3) + response.shape[1:])


def cell_terms(lower, upper, flag_cells, stiffness, weight):
    low_a, low_b, low_c, low_d = (
        lower[:, :-1, :-1],
        lower[:, 1:, :-1],
        lower[:, :-1, 1:],
        lower[:, 1:, 1:],
    )
    up_a, up_b, up_c, up_d = (
        upper[:, :-1, :-1],
        upper[:, 1:, :-1],
        upper[:, :-1, 1:],
        upper[:, 1:, 1:],
    )
    main_diag = (flag_cells == 0)[None]
    low_far = jnp.where(main_diag, low_d, low_c)
    up_far = jnp.where(main_diag, up_d, up_c)
    low_near = jnp.where(main_diag, low_a, low_b)
    up_near = jnp.where(main_diag, up_a, up_b)
    tri_one = triangle(stiffness, (low_a, low_b, low_far), (up_a, up_b, up_far), weight)
    tri_two = triangle(stiffness, (low_near, low_d, low_c), (up_near, up_d, up_c), weight)
    result = []
    for height in range(2):
        resp_one = tri_one[height]
        resp_two = tri_two[height]
        corner_a = resp_one[:, 0] + jnp.where(main_diag, resp_two[:, 0], 0.0)
        corner_b = resp_one[:, 1] + jnp.where(main_diag, 0.0, resp_two[:, 0])
        corner_c = resp_two[:, 2] + jnp.where(main_diag, 0.0, resp_one[:, 2])
        corner_d = resp_two[:, 1] + jnp.where(main_diag, resp_one[:, 2], 0.0)
        result.append((corner_a, corner_b, corner_c, corner_d))
    return (result[0], result[1])


def add_corners(total, extra):
    if total is None:
        return extra
    return tuple((first_term + other_term for first_term, other_term in zip(total, extra)))


def scaled_by(corners, factor):
    return tuple((member * factor for member in corners))


def own_nodes(corners):
    corner_a, corner_b, corner_c, corner_d = corners
    return corner_a[:, 1:, 1:] + corner_b[:, :-1, 1:] + corner_c[:, 1:, :-1] + corner_d[:, :-1, :-1]


def exchange(axis, sent_up, sent_down):
    count = lax.axis_size(axis)
    up = [(i, i + 1) for i in range(count - 1)]
    down = [(i + 1, i) for i in range(count - 1)]
    return lax.ppermute(sent_up, axis, up), lax.ppermute(sent_down, axis, down)


def packed_halo(arrays, dims, axis):
    ups, downs, shapes = [], [], []
    for array, dim in zip(arrays, dims):
        length = array.shape[dim]
        last = lax.slice_in_dim(array, length - 1, length, axis=dim)
        first = lax.slice_in_dim(array, 0, 1, axis=dim)
        shapes.append(last.shape)
        ups.append(last.reshape(-1))
        downs.append(first.reshape(-1))
    before, after = exchange(axis, jnp.concatenate(ups), jnp.concatenate(downs))
    widened = []
    offset = 0
    for array, dim, shape in zip(arrays, dims, shapes):
        size = 1
        for extent in shape:
            size *= extent
        head = before[offset:offset + size].reshape(shape)
        tail = after[offset:offset + size].reshape(shape)
        offset += size
        widened.append(jnp.concatenate([head, array, tail], axis=dim))
    return widened


def per_device(
    ssa_velocity,
    shelf_viscosity,
    basal_friction,
    driving_stress,
    stokes_velocity,
    ice_viscosity,
    body_force,
    diagonals,
    element_matrix,
    iface_columns,
    iface_nodes,
):
    row_count = ssa_velocity.shape[1]
    col_count = ssa_velocity.shape[2]
    depth_count = stokes_velocity.shape[1]
    block_x = stokes_velocity.shape[2]
    block_y = stokes_velocity.shape[3]
    stacked = jnp.concatenate([ssa_velocity, shelf_viscosity[None]], 0)
    owner_nodes = iface_nodes[0]
    slot_count = owner_nodes.shape[1]
    node_row, node_col = slot_selectors(owner_nodes.reshape(-1), row_count, col_count)
    outgoing = gather_slots(ssa_velocity, node_row, node_col).reshape(2, 3, 3, slot_count)
    raw_planes = jnp.concatenate(
        [
            stokes_velocity.reshape(3 * depth_count, block_x, block_y),
            ice_viscosity,
            diagonals.astype(jnp.float32)[None],
        ],
        0,
    )
    shelf_x, planes_x, slots_x = packed_halo((stacked, raw_planes, outgoing), (1, 1, 1), "mx")
    padded, widened, extended = packed_halo((shelf_x, planes_x, slots_x), (2, 2, 2), "my")
    shelf_res = shelf_residual(padded, basal_friction, driving_stress)
    returned = extended[:, 0::2, 0::2].reshape(2, 9, slot_count)
    columns = iface_columns[0]
    col_row, col_col = slot_selectors(columns.reshape(-1), block_x, block_y)
    placed = scatter_slots(returned.reshape(2, -1), col_row, col_col)
    marked = jnp.einsum("sr,sc->rc", col_row, col_col)
    ring = jnp.concatenate([jnp.minimum(marked, 1.0)[None], placed], 0)
    field_ext = widened[:-1].reshape(4, depth_count, block_x + 2, block_y + 2)
    flag_cells = widened[-1, :-1, :-1]
    below_raw, above_raw = layer_neighbours(field_ext[:, -1], field_ext[:, 0])
    (ring_x,) = packed_halo((ring,), (1,), "mx")
    (ring_ext,) = packed_halo((ring_x,), (2,), "my")
    imposed_at = ring_ext[0] > 0.5
    all_layers = jnp.concatenate([below_raw[:, None], field_ext, above_raw[:, None]], 1)
    uv_ext = jnp.where(imposed_at[None, None], ring_ext[1:3, None], all_layers[:2])
    extended_layers = jnp.concatenate([uv_ext, all_layers[2:]], 0)
    count_x = lax.axis_size("mx")
    count_y = lax.axis_size("my")
    place_x = lax.axis_index("mx")
    place_y = lax.axis_index("my")
    global_x = place_x * block_x + jnp.arange(block_x + 1, dtype=jnp.int32) - 1
    global_y = place_y * block_y + jnp.arange(block_y + 1, dtype=jnp.int32) - 1
    valid_x = (global_x >= 0) & (global_x <= count_x * block_x - 2)
    valid_y = (global_y >= 0) & (global_y <= count_y * block_y - 2)
    weight = (valid_x[:, None] & valid_y[None, :]).astype(jnp.float32)
    layer_index = lax.axis_index("layer")
    layer_count = lax.axis_size("layer")
    below_live = (layer_index > 0).astype(jnp.float32)
    above_live = (layer_index < layer_count - 1).astype(jnp.float32)
    fld, main, wpad, live = fem_inputs(extended_layers, flag_cells, weight, below_live, above_live)
    partial_residual, depth_sum = fem_first(fld, main, wpad, element_matrix, live, body_force)
    stokes_residual = fem_second(fld, main, wpad, element_matrix, live, body_force, partial_residual)
    bucket = gather_slots(depth_sum, col_row, col_col).reshape(2, 9, slot_count)
    depth_total = layer_total(bucket)
    grid_back = depth_total.reshape(2, 3, 3, slot_count)
    (back_x,) = packed_halo((grid_back,), (1,), "mx")
    (extended_back,) = packed_halo((back_x,), (2,), "my")
    at_owner = extended_back[:, 0::2, 0::2].reshape(2, 9, slot_count)
    node_force = scatter_slots(at_owner.reshape(2, -1), node_row, node_col)
    coupled_residual = shelf_res - node_force
    return (coupled_residual, stokes_residual)


def solution(mesh):
    return jax.shard_map(
        per_device,
        mesh=mesh,
        in_specs=(
            P(None, "mx", "my"),
            P("mx", "my"),
            P("mx", "my"),
            P(None, "mx", "my"),
            P(None, "layer", "mx", "my"),
            P("layer", "mx", "my"),
            P(None, "layer", "mx", "my"),
            P("mx", "my"),
            P(),
            P(("mx", "my"), None, None),
            P(("mx", "my"), None, None),
        ),
        out_specs=(P(None, "mx", "my"), P(None, "layer", "mx", "my")),
        check_vma=False,
    )
```

```python
import jax
import jax.numpy as jnp
from jax import lax
from jax.sharding import PartitionSpec as P
from jax.experimental import pallas as pl
from jax.experimental.pallas import tpu as pltpu

ROWS_PAD, LANES_PAD = 24, 384


def fem_body(comps, fld_ref, main_ref, weight_ref, kmat_ref, live_ref, body_ref, out_ref, vals_ref, vis_ref, resp_ref):
    main = main_ref[...] > 0.5
    weight = weight_ref[...]
    zero = jnp.zeros((ROWS_PAD, LANES_PAD), jnp.float32)
    for comp in comps:
        out_ref[comp] = -body_ref[comp]
    rows_out = [height * 9 + comp * 3 + vertex for height in range(2) for comp in comps for vertex in range(3)]
    pairs = fld_ref.shape[1] - 1
    for pair in range(pairs):
        vis_parts = [[], []]
        for height in range(2):
            layer = pair + height
            for comp in range(4):
                plane = fld_ref[comp, layer]
                below = pltpu.roll(plane, ROWS_PAD - 1, 0)
                right = pltpu.roll(plane, LANES_PAD - 1, 1)
                diag = pltpu.roll(below, LANES_PAD - 1, 1)
                far = jnp.where(main, diag, right)
                near = jnp.where(main, plane, below)
                if comp < 3:
                    base = height * 9 + comp * 3
                    vals_ref[0, base] = plane
                    vals_ref[0, base + 1] = below
                    vals_ref[0, base + 2] = far
                    vals_ref[1, base] = near
                    vals_ref[1, base + 1] = diag
                    vals_ref[1, base + 2] = right
                else:
                    vis_parts[0] += [plane, below, far]
                    vis_parts[1] += [near, diag, right]
        for tri in range(2):
            total = vis_parts[tri][0]
            for term in vis_parts[tri][1:]:
                total = total + term
            vis_ref[tri] = total / 6.0 * weight

        def tile_body(block, carry):
            row = pl.multiple_of(block * 8, 8)
            for tri in range(2):
                vis = vis_ref[tri, pl.ds(row, 8), :]
                for alpha in rows_out:
                    acc = kmat_ref[alpha, 0] * vals_ref[tri, 0, pl.ds(row, 8), :]
                    for beta in range(1, 18):
                        acc = acc + kmat_ref[alpha, beta] * vals_ref[tri, beta, pl.ds(row, 8), :]
                    resp_ref[tri, alpha, pl.ds(row, 8), :] = acc * vis
            return carry

        lax.fori_loop(0, ROWS_PAD // 8, tile_body, 0)
        for height in range(2):
            own_layer = pair + height - 1
            if own_layer < 0 or own_layer > pairs - 2:
                continue
            scale = None
            if pair == 0 and height == 1:
                scale = live_ref[0]
            if pair == pairs - 1 and height == 0:
                scale = live_ref[1]
            for comp in comps:
                base = height * 9 + comp * 3
                one = [resp_ref[0, base + v] for v in range(3)]
                two = [resp_ref[1, base + v] for v in range(3)]
                corner_a = one[0] + jnp.where(main, two[0], zero)
                corner_b = one[1] + jnp.where(main, zero, two[0])
                corner_c = two[2] + jnp.where(main, zero, one[2])
                corner_d = two[1] + jnp.where(main, one[2], zero)
                node = (pltpu.roll(pltpu.roll(corner_a, ROWS_PAD - 1, 0), LANES_PAD - 1, 1)
                        + pltpu.roll(corner_b, LANES_PAD - 1, 1)
                        + pltpu.roll(corner_c, ROWS_PAD - 1, 0) + corner_d)
                part = node[0:16, 0:256]
                if scale is not None:
                    part = part * scale
                out_ref[comp, own_layer] = out_ref[comp, own_layer] + part


def fem_horizontal(fld_ref, main_ref, weight_ref, kmat_ref, live_ref, body_ref, out_ref, depth_ref, vals_ref, vis_ref, resp_ref):
    fem_body((0, 1), fld_ref, main_ref, weight_ref, kmat_ref, live_ref, body_ref, out_ref, vals_ref, vis_ref, resp_ref)
    for comp in range(2):
        total = out_ref[comp, 0]
        for layer in range(1, out_ref.shape[1]):
            total = total + out_ref[comp, layer]
        depth_ref[comp] = total


def fem_vertical(fld_ref, main_ref, weight_ref, kmat_ref, live_ref, body_ref, prev_ref, out_ref, vals_ref, vis_ref, resp_ref):
    out_ref[0:2] = prev_ref[0:2]
    fem_body((2,), fld_ref, main_ref, weight_ref, kmat_ref, live_ref, body_ref, out_ref, vals_ref, vis_ref, resp_ref)


def fem_inputs(extended_layers, flag_cells, weight, below_live, above_live):
    comps, layers, rows, lanes = extended_layers.shape
    fld = jnp.pad(extended_layers, ((0, 0), (0, 0), (0, ROWS_PAD - rows), (0, LANES_PAD - lanes)))
    cell_rows, cell_lanes = flag_cells.shape
    main = jnp.pad((flag_cells == 0).astype(jnp.float32), ((0, ROWS_PAD - cell_rows), (0, LANES_PAD - cell_lanes)))
    wpad = jnp.pad(weight, ((0, ROWS_PAD - cell_rows), (0, LANES_PAD - cell_lanes)))
    live = jnp.stack([below_live, above_live]).astype(jnp.float32)
    return fld, main, wpad, live


def fem_scratch():
    return [
        pltpu.VMEM((2, 18, ROWS_PAD, LANES_PAD), jnp.float32),
        pltpu.VMEM((2, ROWS_PAD, LANES_PAD), jnp.float32),
        pltpu.VMEM((2, 18, ROWS_PAD, LANES_PAD), jnp.float32),
    ]


def fem_first(fld, main, wpad, element_matrix, live, body_force):
    vmem = pl.BlockSpec(memory_space=pltpu.VMEM)
    smem = pl.BlockSpec(memory_space=pltpu.SMEM)
    depth_shape = (2,) + body_force.shape[2:]
    return pl.pallas_call(
        fem_horizontal,
        out_shape=(
            jax.ShapeDtypeStruct(body_force.shape, jnp.float32),
            jax.ShapeDtypeStruct(depth_shape, jnp.float32),
        ),
        in_specs=[vmem, vmem, vmem, smem, smem, vmem],
        out_specs=(vmem, vmem),
        scratch_shapes=fem_scratch(),
    )(fld, main, wpad, element_matrix, live, body_force)


def fem_second(fld, main, wpad, element_matrix, live, body_force, previous):
    vmem = pl.BlockSpec(memory_space=pltpu.VMEM)
    smem = pl.BlockSpec(memory_space=pltpu.SMEM)
    return pl.pallas_call(
        fem_vertical,
        out_shape=jax.ShapeDtypeStruct(body_force.shape, jnp.float32),
        in_specs=[vmem, vmem, vmem, smem, smem, vmem, vmem],
        out_specs=vmem,
        scratch_shapes=fem_scratch(),
    )(fld, main, wpad, element_matrix, live, body_force, previous)


HIGH = lax.Precision.HIGHEST


def slot_selectors(index, rows, cols):
    live = index >= 0
    row_of = jnp.where(live, index // cols, -1)
    col_of = jnp.where(live, index % cols, -1)
    pick_row = (row_of[:, None] == jnp.arange(rows, dtype=jnp.int32)[None]).astype(jnp.float32)
    pick_col = (col_of[:, None] == jnp.arange(cols, dtype=jnp.int32)[None]).astype(jnp.float32)
    return pick_row, pick_col


def gather_slots(field, pick_row, pick_col):
    cols_taken = jnp.einsum("krc,sc->krs", field, pick_col, precision=HIGH)
    return jnp.sum(jnp.where(pick_row.T[None] > 0.5, cols_taken, 0.0), axis=1)


def scatter_slots(values, pick_row, pick_col):
    weighted = pick_row[None] * values[:, :, None]
    return jnp.einsum("ksr,sc->krc", weighted, pick_col, precision=HIGH)


def layer_total(part):
    count = lax.axis_size("layer")
    copies = jnp.broadcast_to(part[None], (count,) + part.shape)
    gathered = lax.all_to_all(copies, "layer", 0, 0, tiled=True)
    total = gathered[0]
    for source in range(1, count):
        total = total + gathered[source]
    return total


def layer_neighbours(top, bottom):
    count = lax.axis_size("layer")
    place = lax.axis_index("layer")
    chunks = []
    for target in range(count):
        chunk = jnp.where(target == place + 1, top, jnp.where(target == place - 1, bottom, 0.0))
        chunks.append(chunk[None])
    received = lax.all_to_all(jnp.concatenate(chunks, 0), "layer", 0, 0, tiled=True)
    below = jnp.zeros_like(top)
    above = jnp.zeros_like(top)
    for source in range(count):
        below = jnp.where(source == place - 1, received[source], below)
        above = jnp.where(source == place + 1, received[source], above)
    return below, above


def cell_dx(plane):
    return 0.5 * (plane[1:, :-1] + plane[1:, 1:] - (plane[:-1, :-1] + plane[:-1, 1:]))


def cell_dy(plane):
    return 0.5 * (plane[:-1, 1:] + plane[1:, 1:] - (plane[:-1, :-1] + plane[1:, :-1]))


def shelf_residual(padded, friction, driving):
    u_field = padded[0]
    v_field = padded[1]
    h_field = padded[2]
    du_dx = cell_dx(u_field)
    du_dy = cell_dy(u_field)
    dv_dx = cell_dx(v_field)
    dv_dy = cell_dy(v_field)
    h_cell = 0.25 * (h_field[1:, :-1] + h_field[1:, 1:] + h_field[:-1, :-1] + h_field[:-1, 1:])
    tau_xx = h_cell * (4.0 * du_dx + 2.0 * dv_dy)
    tau_yy = h_cell * (4.0 * dv_dy + 2.0 * du_dx)
    tau_xy = h_cell * (du_dy + dv_dx)
    res_x = cell_dx(tau_xx) + cell_dy(tau_xy) - friction * u_field[1:-1, 1:-1] - driving[0]
    res_y = cell_dy(tau_yy) + cell_dx(tau_xy) - friction * v_field[1:-1, 1:-1] - driving[1]
    return jnp.stack([res_x, res_y])


def triangle(stiffness, lows, ups, weight):
    values = jnp.stack(
        [plane[comp] for group in (lows, ups) for comp in range(3) for plane in group]
    )
    viscous = (
        (lows[0][3] + lows[1][3] + lows[2][3] + ups[0][3] + ups[1][3] + ups[2][3]) / 6.0 * weight
    )
    response = (
        jnp.einsum("ab,bxy->axy", stiffness, values, precision=lax.Precision.HIGHEST) * viscous
    )
    return response.reshape((2, 3, 3) + response.shape[1:])


def cell_terms(lower, upper, flag_cells, stiffness, weight):
    low_a, low_b, low_c, low_d = (
        lower[:, :-1, :-1],
        lower[:, 1:, :-1],
        lower[:, :-1, 1:],
        lower[:, 1:, 1:],
    )
    up_a, up_b, up_c, up_d = (
        upper[:, :-1, :-1],
        upper[:, 1:, :-1],
        upper[:, :-1, 1:],
        upper[:, 1:, 1:],
    )
    main_diag = (flag_cells == 0)[None]
    low_far = jnp.where(main_diag, low_d, low_c)
    up_far = jnp.where(main_diag, up_d, up_c)
    low_near = jnp.where(main_diag, low_a, low_b)
    up_near = jnp.where(main_diag, up_a, up_b)
    tri_one = triangle(stiffness, (low_a, low_b, low_far), (up_a, up_b, up_far), weight)
    tri_two = triangle(stiffness, (low_near, low_d, low_c), (up_near, up_d, up_c), weight)
    result = []
    for height in range(2):
        resp_one = tri_one[height]
        resp_two = tri_two[height]
        corner_a = resp_one[:, 0] + jnp.where(main_diag, resp_two[:, 0], 0.0)
        corner_b = resp_one[:, 1] + jnp.where(main_diag, 0.0, resp_two[:, 0])
        corner_c = resp_two[:, 2] + jnp.where(main_diag, 0.0, resp_one[:, 2])
        corner_d = resp_two[:, 1] + jnp.where(main_diag, resp_one[:, 2], 0.0)
        result.append((corner_a, corner_b, corner_c, corner_d))
    return (result[0], result[1])


def add_corners(total, extra):
    if total is None:
        return extra
    return tuple((first_term + other_term for first_term, other_term in zip(total, extra)))


def scaled_by(corners, factor):
    return tuple((member * factor for member in corners))


def own_nodes(corners):
    corner_a, corner_b, corner_c, corner_d = corners
    return corner_a[:, 1:, 1:] + corner_b[:, :-1, 1:] + corner_c[:, 1:, :-1] + corner_d[:, :-1, :-1]


def exchange(axis, sent_up, sent_down):
    count = lax.axis_size(axis)
    up = [(i, i + 1) for i in range(count - 1)]
    down = [(i + 1, i) for i in range(count - 1)]
    return lax.ppermute(sent_up, axis, up), lax.ppermute(sent_down, axis, down)


def packed_halo(arrays, dims, axis):
    ups, downs, shapes = [], [], []
    for array, dim in zip(arrays, dims):
        length = array.shape[dim]
        last = lax.slice_in_dim(array, length - 1, length, axis=dim)
        first = lax.slice_in_dim(array, 0, 1, axis=dim)
        shapes.append(last.shape)
        ups.append(last.reshape(-1))
        downs.append(first.reshape(-1))
    before, after = exchange(axis, jnp.concatenate(ups), jnp.concatenate(downs))
    widened = []
    offset = 0
    for array, dim, shape in zip(arrays, dims, shapes):
        size = 1
        for extent in shape:
            size *= extent
        head = before[offset:offset + size].reshape(shape)
        tail = after[offset:offset + size].reshape(shape)
        offset += size
        widened.append(jnp.concatenate([head, array, tail], axis=dim))
    return widened


def per_device(
    ssa_velocity,
    shelf_viscosity,
    basal_friction,
    driving_stress,
    stokes_velocity,
    ice_viscosity,
    body_force,
    diagonals,
    element_matrix,
    iface_columns,
    iface_nodes,
):
    row_count = ssa_velocity.shape[1]
    col_count = ssa_velocity.shape[2]
    depth_count = stokes_velocity.shape[1]
    block_x = stokes_velocity.shape[2]
    block_y = stokes_velocity.shape[3]
    stacked = jnp.concatenate([ssa_velocity, shelf_viscosity[None]], 0)
    owner_nodes = iface_nodes[0]
    slot_count = owner_nodes.shape[1]
    node_row, node_col = slot_selectors(owner_nodes.reshape(-1), row_count, col_count)
    outgoing = gather_slots(ssa_velocity, node_row, node_col).reshape(2, 3, 3, slot_count)
    raw_planes = jnp.concatenate(
        [
            stokes_velocity.reshape(3 * depth_count, block_x, block_y),
            ice_viscosity,
            diagonals.astype(jnp.float32)[None],
        ],
        0,
    )
    shelf_x, planes_x, slots_x = packed_halo((stacked, raw_planes, outgoing), (1, 1, 1), "mx")
    padded, widened, extended = packed_halo((shelf_x, planes_x, slots_x), (2, 2, 2), "my")
    shelf_res = shelf_residual(padded, basal_friction, driving_stress)
    returned = extended[:, 0::2, 0::2].reshape(2, 9, slot_count)
    columns = iface_columns[0]
    col_row, col_col = slot_selectors(columns.reshape(-1), block_x, block_y)
    placed = scatter_slots(returned.reshape(2, -1), col_row, col_col)
    marked = jnp.einsum("sr,sc->rc", col_row, col_col)
    ring = jnp.concatenate([jnp.minimum(marked, 1.0)[None], placed], 0)
    field_ext = widened[:-1].reshape(4, depth_count, block_x + 2, block_y + 2)
    flag_cells = widened[-1, :-1, :-1]
    below_raw, above_raw = layer_neighbours(field_ext[:, -1], field_ext[:, 0])
    (ring_x,) = packed_halo((ring,), (1,), "mx")
    (ring_ext,) = packed_halo((ring_x,), (2,), "my")
    imposed_at = ring_ext[0] > 0.5
    all_layers = jnp.concatenate([below_raw[:, None], field_ext, above_raw[:, None]], 1)
    uv_ext = jnp.where(imposed_at[None, None], ring_ext[1:3, None], all_layers[:2])
    extended_layers = jnp.concatenate([uv_ext, all_layers[2:]], 0)
    count_x = lax.axis_size("mx")
    count_y = lax.axis_size("my")
    place_x = lax.axis_index("mx")
    place_y = lax.axis_index("my")
    global_x = place_x * block_x + jnp.arange(block_x + 1, dtype=jnp.int32) - 1
    global_y = place_y * block_y + jnp.arange(block_y + 1, dtype=jnp.int32) - 1
    valid_x = (global_x >= 0) & (global_x <= count_x * block_x - 2)
    valid_y = (global_y >= 0) & (global_y <= count_y * block_y - 2)
    weight = (valid_x[:, None] & valid_y[None, :]).astype(jnp.float32)
    layer_index = lax.axis_index("layer")
    layer_count = lax.axis_size("layer")
    below_live = (layer_index > 0).astype(jnp.float32)
    above_live = (layer_index < layer_count - 1).astype(jnp.float32)
    fld, main, wpad, live = fem_inputs(extended_layers, flag_cells, weight, below_live, above_live)
    partial_residual, depth_sum = fem_first(fld, main, wpad, element_matrix, live, body_force)
    stokes_residual = fem_second(fld, main, wpad, element_matrix, live, body_force, partial_residual)
    bucket = gather_slots(depth_sum, col_row, col_col).reshape(2, 9, slot_count)
    depth_total = layer_total(bucket)
    depth_total, stokes_residual = lax.optimization_barrier((depth_total, stokes_residual))
    grid_back = depth_total.reshape(2, 3, 3, slot_count)
    (back_x,) = packed_halo((grid_back,), (1,), "mx")
    (extended_back,) = packed_halo((back_x,), (2,), "my")
    at_owner = extended_back[:, 0::2, 0::2].reshape(2, 9, slot_count)
    node_force = scatter_slots(at_owner.reshape(2, -1), node_row, node_col)
    coupled_residual = shelf_res - node_force
    return (coupled_residual, stokes_residual)


def solution(mesh):
    return jax.shard_map(
        per_device,
        mesh=mesh,
        in_specs=(
            P(None, "mx", "my"),
            P("mx", "my"),
            P("mx", "my"),
            P(None, "mx", "my"),
            P(None, "layer", "mx", "my"),
            P("layer", "mx", "my"),
            P(None, "layer", "mx", "my"),
            P("mx", "my"),
            P(),
            P(("mx", "my"), None, None),
            P(("mx", "my"), None, None),
        ),
        out_specs=(P(None, "mx", "my"), P(None, "layer", "mx", "my")),
        check_vma=False,
    )
```

```python
import functools

import jax
import jax.numpy as jnp
from jax import lax
from jax.sharding import PartitionSpec as P
from jax.experimental import pallas as pl
from jax.experimental.pallas import tpu as pltpu

ROWS_PAD, LANES_PAD = 24, 384


def cell_weight(grid):
    block_x, block_y, count_x, count_y = grid
    rows = lax.broadcasted_iota(jnp.int32, (ROWS_PAD, LANES_PAD), 0)
    lanes = lax.broadcasted_iota(jnp.int32, (ROWS_PAD, LANES_PAD), 1)
    global_x = lax.axis_index("mx") * block_x + rows - 1
    global_y = lax.axis_index("my") * block_y + lanes - 1
    valid = (global_x >= 0) & (global_x <= count_x * block_x - 2) & (rows <= block_x)
    valid = valid & (global_y >= 0) & (global_y <= count_y * block_y - 2) & (lanes <= block_y)
    return valid.astype(jnp.float32)


def fem_body(comps, grid, fld_ref, kmat_ref, body_ref, out_ref, vals_ref, vis_ref, resp_ref):
    layers = (fld_ref.shape[0] - 1) // 4
    main = fld_ref[4 * layers] == 0.0
    weight = cell_weight(grid)
    layer_index = lax.axis_index("layer")
    below_live = (layer_index > 0).astype(jnp.float32)
    above_live = (layer_index < lax.axis_size("layer") - 1).astype(jnp.float32)
    zero = jnp.zeros((ROWS_PAD, LANES_PAD), jnp.float32)
    for comp in comps:
        out_ref[comp] = -body_ref[comp]
    rows_out = [height * 9 + comp * 3 + vertex for height in range(2) for comp in comps for vertex in range(3)]
    pairs = layers - 1
    for pair in range(pairs):
        vis_parts = [[], []]
        for height in range(2):
            layer = pair + height
            for comp in range(4):
                plane = fld_ref[comp * layers + layer]
                below = pltpu.roll(plane, ROWS_PAD - 1, 0)
                right = pltpu.roll(plane, LANES_PAD - 1, 1)
                diag = pltpu.roll(below, LANES_PAD - 1, 1)
                far = jnp.where(main, diag, right)
                near = jnp.where(main, plane, below)
                if comp < 3:
                    base = height * 9 + comp * 3
                    vals_ref[0, base] = plane
                    vals_ref[0, base + 1] = below
                    vals_ref[0, base + 2] = far
                    vals_ref[1, base] = near
                    vals_ref[1, base + 1] = diag
                    vals_ref[1, base + 2] = right
                else:
                    vis_parts[0] += [plane, below, far]
                    vis_parts[1] += [near, diag, right]
        for tri in range(2):
            total = vis_parts[tri][0]
            for term in vis_parts[tri][1:]:
                total = total + term
            vis_ref[tri] = total / 6.0 * weight

        def tile_body(block, carry):
            row = pl.multiple_of(block * 8, 8)
            for tri in range(2):
                vis = vis_ref[tri, pl.ds(row, 8), :]
                for alpha in rows_out:
                    acc = kmat_ref[alpha, 0] * vals_ref[tri, 0, pl.ds(row, 8), :]
                    for beta in range(1, 18):
                        acc = acc + kmat_ref[alpha, beta] * vals_ref[tri, beta, pl.ds(row, 8), :]
                    resp_ref[tri, alpha, pl.ds(row, 8), :] = acc * vis
            return carry

        lax.fori_loop(0, ROWS_PAD // 8, tile_body, 0)
        for height in range(2):
            own_layer = pair + height - 1
            if own_layer < 0 or own_layer > pairs - 2:
                continue
            scale = None
            if pair == 0 and height == 1:
                scale = below_live
            if pair == pairs - 1 and height == 0:
                scale = above_live
            for comp in comps:
                base = height * 9 + comp * 3
                one = [resp_ref[0, base + v] for v in range(3)]
                two = [resp_ref[1, base + v] for v in range(3)]
                corner_a = one[0] + jnp.where(main, two[0], zero)
                corner_b = one[1] + jnp.where(main, zero, two[0])
                corner_c = two[2] + jnp.where(main, zero, one[2])
                corner_d = two[1] + jnp.where(main, one[2], zero)
                node = (pltpu.roll(pltpu.roll(corner_a, ROWS_PAD - 1, 0), LANES_PAD - 1, 1)
                        + pltpu.roll(corner_b, LANES_PAD - 1, 1)
                        + pltpu.roll(corner_c, ROWS_PAD - 1, 0) + corner_d)
                part = node[0:16, 0:256]
                if scale is not None:
                    part = part * scale
                out_ref[comp, own_layer] = out_ref[comp, own_layer] + part


def fem_horizontal(grid, fld_ref, kmat_ref, body_ref, out_ref, depth_ref, vals_ref, vis_ref, resp_ref):
    fem_body((0, 1), grid, fld_ref, kmat_ref, body_ref, out_ref, vals_ref, vis_ref, resp_ref)
    for comp in range(2):
        total = out_ref[comp, 0]
        for layer in range(1, out_ref.shape[1]):
            total = total + out_ref[comp, layer]
        depth_ref[comp] = total


def fem_vertical(grid, fld_ref, kmat_ref, body_ref, prev_ref, out_ref, vals_ref, vis_ref, resp_ref):
    out_ref[0:2] = prev_ref[0:2]
    fem_body((2,), grid, fld_ref, kmat_ref, body_ref, out_ref, vals_ref, vis_ref, resp_ref)


def fem_inputs(extended_layers, diag_ext):
    comps, layers, rows, lanes = extended_layers.shape
    planes = jnp.concatenate([extended_layers.reshape(comps * layers, rows, lanes), diag_ext[None]], 0)
    return jnp.pad(planes, ((0, 0), (0, ROWS_PAD - rows), (0, LANES_PAD - lanes)))


def fem_scratch():
    return [
        pltpu.VMEM((2, 18, ROWS_PAD, LANES_PAD), jnp.float32),
        pltpu.VMEM((2, ROWS_PAD, LANES_PAD), jnp.float32),
        pltpu.VMEM((2, 18, ROWS_PAD, LANES_PAD), jnp.float32),
    ]


def fem_first(grid, fld, element_matrix, body_force):
    vmem = pl.BlockSpec(memory_space=pltpu.VMEM)
    smem = pl.BlockSpec(memory_space=pltpu.SMEM)
    depth_shape = (2,) + body_force.shape[2:]
    return pl.pallas_call(
        functools.partial(fem_horizontal, grid),
        out_shape=(
            jax.ShapeDtypeStruct(body_force.shape, jnp.float32),
            jax.ShapeDtypeStruct(depth_shape, jnp.float32),
        ),
        in_specs=[vmem, smem, vmem],
        out_specs=(vmem, vmem),
        scratch_shapes=fem_scratch(),
    )(fld, element_matrix, body_force)


def fem_second(grid, fld, element_matrix, body_force, previous):
    vmem = pl.BlockSpec(memory_space=pltpu.VMEM)
    smem = pl.BlockSpec(memory_space=pltpu.SMEM)
    return pl.pallas_call(
        functools.partial(fem_vertical, grid),
        out_shape=jax.ShapeDtypeStruct(body_force.shape, jnp.float32),
        in_specs=[vmem, smem, vmem, vmem],
        out_specs=vmem,
        scratch_shapes=fem_scratch(),
    )(fld, element_matrix, body_force, previous)


HIGH = lax.Precision.HIGHEST


def slot_selectors(index, rows, cols):
    live = index >= 0
    row_of = jnp.where(live, index // cols, -1)
    col_of = jnp.where(live, index % cols, -1)
    pick_row = (row_of[:, None] == jnp.arange(rows, dtype=jnp.int32)[None]).astype(jnp.float32)
    pick_col = (col_of[:, None] == jnp.arange(cols, dtype=jnp.int32)[None]).astype(jnp.float32)
    return pick_row, pick_col


def gather_slots(field, pick_row, pick_col):
    cols_taken = jnp.einsum("krc,sc->krs", field, pick_col, precision=HIGH)
    return jnp.sum(jnp.where(pick_row.T[None] > 0.5, cols_taken, 0.0), axis=1)


def scatter_slots(values, pick_row, pick_col):
    weighted = pick_row[None] * values[:, :, None]
    return jnp.einsum("ksr,sc->krc", weighted, pick_col, precision=HIGH)


def layer_total(part):
    count = lax.axis_size("layer")
    copies = jnp.broadcast_to(part[None], (count,) + part.shape)
    gathered = lax.all_to_all(copies, "layer", 0, 0, tiled=True)
    total = gathered[0]
    for source in range(1, count):
        total = total + gathered[source]
    return total


def layer_neighbours(top, bottom):
    count = lax.axis_size("layer")
    place = lax.axis_index("layer")
    chunks = []
    for target in range(count):
        chunk = jnp.where(target == place + 1, top, jnp.where(target == place - 1, bottom, 0.0))
        chunks.append(chunk[None])
    received = lax.all_to_all(jnp.concatenate(chunks, 0), "layer", 0, 0, tiled=True)
    below = jnp.zeros_like(top)
    above = jnp.zeros_like(top)
    for source in range(count):
        below = jnp.where(source == place - 1, received[source], below)
        above = jnp.where(source == place + 1, received[source], above)
    return below, above


def cell_dx(plane):
    return 0.5 * (plane[1:, :-1] + plane[1:, 1:] - (plane[:-1, :-1] + plane[:-1, 1:]))


def cell_dy(plane):
    return 0.5 * (plane[:-1, 1:] + plane[1:, 1:] - (plane[:-1, :-1] + plane[1:, :-1]))


def shelf_residual(padded, friction, driving):
    u_field = padded[0]
    v_field = padded[1]
    h_field = padded[2]
    du_dx = cell_dx(u_field)
    du_dy = cell_dy(u_field)
    dv_dx = cell_dx(v_field)
    dv_dy = cell_dy(v_field)
    h_cell = 0.25 * (h_field[1:, :-1] + h_field[1:, 1:] + h_field[:-1, :-1] + h_field[:-1, 1:])
    tau_xx = h_cell * (4.0 * du_dx + 2.0 * dv_dy)
    tau_yy = h_cell * (4.0 * dv_dy + 2.0 * du_dx)
    tau_xy = h_cell * (du_dy + dv_dx)
    res_x = cell_dx(tau_xx) + cell_dy(tau_xy) - friction * u_field[1:-1, 1:-1] - driving[0]
    res_y = cell_dy(tau_yy) + cell_dx(tau_xy) - friction * v_field[1:-1, 1:-1] - driving[1]
    return jnp.stack([res_x, res_y])


def triangle(stiffness, lows, ups, weight):
    values = jnp.stack(
        [plane[comp] for group in (lows, ups) for comp in range(3) for plane in group]
    )
    viscous = (
        (lows[0][3] + lows[1][3] + lows[2][3] + ups[0][3] + ups[1][3] + ups[2][3]) / 6.0 * weight
    )
    response = (
        jnp.einsum("ab,bxy->axy", stiffness, values, precision=lax.Precision.HIGHEST) * viscous
    )
    return response.reshape((2, 3, 3) + response.shape[1:])


def cell_terms(lower, upper, flag_cells, stiffness, weight):
    low_a, low_b, low_c, low_d = (
        lower[:, :-1, :-1],
        lower[:, 1:, :-1],
        lower[:, :-1, 1:],
        lower[:, 1:, 1:],
    )
    up_a, up_b, up_c, up_d = (
        upper[:, :-1, :-1],
        upper[:, 1:, :-1],
        upper[:, :-1, 1:],
        upper[:, 1:, 1:],
    )
    main_diag = (flag_cells == 0)[None]
    low_far = jnp.where(main_diag, low_d, low_c)
    up_far = jnp.where(main_diag, up_d, up_c)
    low_near = jnp.where(main_diag, low_a, low_b)
    up_near = jnp.where(main_diag, up_a, up_b)
    tri_one = triangle(stiffness, (low_a, low_b, low_far), (up_a, up_b, up_far), weight)
    tri_two = triangle(stiffness, (low_near, low_d, low_c), (up_near, up_d, up_c), weight)
    result = []
    for height in range(2):
        resp_one = tri_one[height]
        resp_two = tri_two[height]
        corner_a = resp_one[:, 0] + jnp.where(main_diag, resp_two[:, 0], 0.0)
        corner_b = resp_one[:, 1] + jnp.where(main_diag, 0.0, resp_two[:, 0])
        corner_c = resp_two[:, 2] + jnp.where(main_diag, 0.0, resp_one[:, 2])
        corner_d = resp_two[:, 1] + jnp.where(main_diag, resp_one[:, 2], 0.0)
        result.append((corner_a, corner_b, corner_c, corner_d))
    return (result[0], result[1])


def add_corners(total, extra):
    if total is None:
        return extra
    return tuple((first_term + other_term for first_term, other_term in zip(total, extra)))


def scaled_by(corners, factor):
    return tuple((member * factor for member in corners))


def own_nodes(corners):
    corner_a, corner_b, corner_c, corner_d = corners
    return corner_a[:, 1:, 1:] + corner_b[:, :-1, 1:] + corner_c[:, 1:, :-1] + corner_d[:, :-1, :-1]


def exchange(axis, sent_up, sent_down):
    count = lax.axis_size(axis)
    up = [(i, i + 1) for i in range(count - 1)]
    down = [(i + 1, i) for i in range(count - 1)]
    return lax.ppermute(sent_up, axis, up), lax.ppermute(sent_down, axis, down)


def packed_halo(arrays, dims, axis):
    ups, downs, shapes = [], [], []
    for array, dim in zip(arrays, dims):
        length = array.shape[dim]
        last = lax.slice_in_dim(array, length - 1, length, axis=dim)
        first = lax.slice_in_dim(array, 0, 1, axis=dim)
        shapes.append(last.shape)
        ups.append(last.reshape(-1))
        downs.append(first.reshape(-1))
    before, after = exchange(axis, jnp.concatenate(ups), jnp.concatenate(downs))
    widened = []
    offset = 0
    for array, dim, shape in zip(arrays, dims, shapes):
        size = 1
        for extent in shape:
            size *= extent
        head = before[offset:offset + size].reshape(shape)
        tail = after[offset:offset + size].reshape(shape)
        offset += size
        widened.append(jnp.concatenate([head, array, tail], axis=dim))
    return widened


def per_device(
    ssa_velocity,
    shelf_viscosity,
    basal_friction,
    driving_stress,
    stokes_velocity,
    ice_viscosity,
    body_force,
    diagonals,
    element_matrix,
    iface_columns,
    iface_nodes,
):
    row_count = ssa_velocity.shape[1]
    col_count = ssa_velocity.shape[2]
    depth_count = stokes_velocity.shape[1]
    block_x = stokes_velocity.shape[2]
    block_y = stokes_velocity.shape[3]
    stacked = jnp.concatenate([ssa_velocity, shelf_viscosity[None]], 0)
    owner_nodes = iface_nodes[0]
    slot_count = owner_nodes.shape[1]
    node_row, node_col = slot_selectors(owner_nodes.reshape(-1), row_count, col_count)
    outgoing = gather_slots(ssa_velocity, node_row, node_col).reshape(2, 3, 3, slot_count)
    raw_planes = jnp.concatenate(
        [
            stokes_velocity.reshape(3 * depth_count, block_x, block_y),
            ice_viscosity,
            diagonals.astype(jnp.float32)[None],
        ],
        0,
    )
    shelf_x, planes_x, slots_x = packed_halo((stacked, raw_planes, outgoing), (1, 1, 1), "mx")
    padded, widened, extended = packed_halo((shelf_x, planes_x, slots_x), (2, 2, 2), "my")
    shelf_res = shelf_residual(padded, basal_friction, driving_stress)
    returned = extended[:, 0::2, 0::2].reshape(2, 9, slot_count)
    columns = iface_columns[0]
    col_row, col_col = slot_selectors(columns.reshape(-1), block_x, block_y)
    placed = scatter_slots(returned.reshape(2, -1), col_row, col_col)
    marked = jnp.einsum("sr,sc->rc", col_row, col_col)
    ring = jnp.concatenate([jnp.minimum(marked, 1.0)[None], placed], 0)
    field_ext = widened[:-1].reshape(4, depth_count, block_x + 2, block_y + 2)
    below_raw, above_raw = layer_neighbours(field_ext[:, -1], field_ext[:, 0])
    (ring_x,) = packed_halo((ring,), (1,), "mx")
    (ring_ext,) = packed_halo((ring_x,), (2,), "my")
    imposed_at = ring_ext[0] > 0.5
    all_layers = jnp.concatenate([below_raw[:, None], field_ext, above_raw[:, None]], 1)
    uv_ext = jnp.where(imposed_at[None, None], ring_ext[1:3, None], all_layers[:2])
    extended_layers = jnp.concatenate([uv_ext, all_layers[2:]], 0)
    grid = (block_x, block_y, lax.axis_size("mx"), lax.axis_size("my"))
    fld = fem_inputs(extended_layers, widened[-1])
    partial_residual, depth_sum = fem_first(grid, fld, element_matrix, body_force)
    stokes_residual = fem_second(grid, fld, element_matrix, body_force, partial_residual)
    bucket = gather_slots(depth_sum, col_row, col_col).reshape(2, 9, slot_count)
    depth_total = layer_total(bucket)
    depth_total, stokes_residual = lax.optimization_barrier((depth_total, stokes_residual))
    grid_back = depth_total.reshape(2, 3, 3, slot_count)
    (back_x,) = packed_halo((grid_back,), (1,), "mx")
    (extended_back,) = packed_halo((back_x,), (2,), "my")
    at_owner = extended_back[:, 0::2, 0::2].reshape(2, 9, slot_count)
    node_force = scatter_slots(at_owner.reshape(2, -1), node_row, node_col)
    coupled_residual = shelf_res - node_force
    return (coupled_residual, stokes_residual)


def solution(mesh):
    return jax.shard_map(
        per_device,
        mesh=mesh,
        in_specs=(
            P(None, "mx", "my"),
            P("mx", "my"),
            P("mx", "my"),
            P(None, "mx", "my"),
            P(None, "layer", "mx", "my"),
            P("layer", "mx", "my"),
            P(None, "layer", "mx", "my"),
            P("mx", "my"),
            P(),
            P(("mx", "my"), None, None),
            P(("mx", "my"), None, None),
        ),
        out_specs=(P(None, "mx", "my"), P(None, "layer", "mx", "my")),
        check_vma=False,
    )
```

```python
import functools

import jax
import jax.numpy as jnp
from jax import lax
from jax.sharding import PartitionSpec as P
from jax.experimental import pallas as pl
from jax.experimental.pallas import tpu as pltpu

ROWS_PAD, LANES_PAD = 24, 384


def cell_weight(grid):
    block_x, block_y, count_x, count_y = grid
    rows = lax.broadcasted_iota(jnp.int32, (ROWS_PAD, LANES_PAD), 0)
    lanes = lax.broadcasted_iota(jnp.int32, (ROWS_PAD, LANES_PAD), 1)
    global_x = lax.axis_index("mx") * block_x + rows - 1
    global_y = lax.axis_index("my") * block_y + lanes - 1
    valid = (global_x >= 0) & (global_x <= count_x * block_x - 2) & (rows <= block_x)
    valid = valid & (global_y >= 0) & (global_y <= count_y * block_y - 2) & (lanes <= block_y)
    return valid.astype(jnp.float32)


def fem_body(comps, grid, fld_ref, kmat_ref, body_ref, out_ref, vals_ref, vis_ref, resp_ref):
    layers = (fld_ref.shape[0] - 1) // 4
    main = fld_ref[4 * layers] == 0.0
    weight = cell_weight(grid)
    layer_index = lax.axis_index("layer")
    below_live = (layer_index > 0).astype(jnp.float32)
    above_live = (layer_index < lax.axis_size("layer") - 1).astype(jnp.float32)
    zero = jnp.zeros((ROWS_PAD, LANES_PAD), jnp.float32)
    for comp in comps:
        out_ref[comp] = -body_ref[comp]
    rows_out = [height * 9 + comp * 3 + vertex for height in range(2) for comp in comps for vertex in range(3)]
    pairs = layers - 1

    def layer_views(layer):
        slot = layer % 2
        for comp in range(4):
            plane = fld_ref[comp * layers + layer]
            below = pltpu.roll(plane, ROWS_PAD - 1, 0)
            right = pltpu.roll(plane, LANES_PAD - 1, 1)
            diag = pltpu.roll(below, LANES_PAD - 1, 1)
            far = jnp.where(main, diag, right)
            near = jnp.where(main, plane, below)
            for tri, views in enumerate(((plane, below, far), (near, diag, right))):
                for vertex in range(3):
                    vals_ref[slot, tri, comp * 3 + vertex] = views[vertex]

    layer_views(0)
    for pair in range(pairs):
        layer_views(pair + 1)
        slots = (pair % 2, (pair + 1) % 2)
        for tri in range(2):
            total = None
            for height in range(2):
                for vertex in range(3):
                    term = vals_ref[slots[height], tri, 9 + vertex]
                    total = term if total is None else total + term
            vis_ref[tri] = total / 6.0 * weight

        def tile_body(block, carry):
            row = pl.multiple_of(block * 8, 8)
            for tri in range(2):
                vis = vis_ref[tri, pl.ds(row, 8), :]
                values = [vals_ref[slots[beta // 9], tri, beta % 9, pl.ds(row, 8), :] for beta in range(18)]
                for alpha in rows_out:
                    acc = kmat_ref[alpha, 0] * values[0]
                    for beta in range(1, 18):
                        acc = acc + kmat_ref[alpha, beta] * values[beta]
                    resp_ref[tri, alpha, pl.ds(row, 8), :] = acc * vis
            return carry

        lax.fori_loop(0, ROWS_PAD // 8, tile_body, 0)
        for height in range(2):
            own_layer = pair + height - 1
            if own_layer < 0 or own_layer > pairs - 2:
                continue
            scale = None
            if pair == 0 and height == 1:
                scale = below_live
            if pair == pairs - 1 and height == 0:
                scale = above_live
            for comp in comps:
                base = height * 9 + comp * 3
                one = [resp_ref[0, base + v] for v in range(3)]
                two = [resp_ref[1, base + v] for v in range(3)]
                corner_a = one[0] + jnp.where(main, two[0], zero)
                corner_b = one[1] + jnp.where(main, zero, two[0])
                corner_c = two[2] + jnp.where(main, zero, one[2])
                corner_d = two[1] + jnp.where(main, one[2], zero)
                node = (pltpu.roll(pltpu.roll(corner_a, ROWS_PAD - 1, 0), LANES_PAD - 1, 1)
                        + pltpu.roll(corner_b, LANES_PAD - 1, 1)
                        + pltpu.roll(corner_c, ROWS_PAD - 1, 0) + corner_d)
                part = node[0:16, 0:256]
                if scale is not None:
                    part = part * scale
                out_ref[comp, own_layer] = out_ref[comp, own_layer] + part


def fem_horizontal(grid, fld_ref, kmat_ref, body_ref, out_ref, depth_ref, vals_ref, vis_ref, resp_ref):
    fem_body((0, 1), grid, fld_ref, kmat_ref, body_ref, out_ref, vals_ref, vis_ref, resp_ref)
    for comp in range(2):
        total = out_ref[comp, 0]
        for layer in range(1, out_ref.shape[1]):
            total = total + out_ref[comp, layer]
        depth_ref[comp] = total


def fem_vertical(grid, fld_ref, kmat_ref, body_ref, prev_ref, out_ref, vals_ref, vis_ref, resp_ref):
    out_ref[0:2] = prev_ref[0:2]
    fem_body((2,), grid, fld_ref, kmat_ref, body_ref, out_ref, vals_ref, vis_ref, resp_ref)


def fem_inputs(extended_layers, diag_ext):
    comps, layers, rows, lanes = extended_layers.shape
    planes = jnp.concatenate([extended_layers.reshape(comps * layers, rows, lanes), diag_ext[None]], 0)
    return jnp.pad(planes, ((0, 0), (0, ROWS_PAD - rows), (0, LANES_PAD - lanes)))


def fem_scratch():
    return [
        pltpu.VMEM((2, 2, 12, ROWS_PAD, LANES_PAD), jnp.float32),
        pltpu.VMEM((2, ROWS_PAD, LANES_PAD), jnp.float32),
        pltpu.VMEM((2, 18, ROWS_PAD, LANES_PAD), jnp.float32),
    ]


def fem_first(grid, fld, element_matrix, body_force):
    vmem = pl.BlockSpec(memory_space=pltpu.VMEM)
    smem = pl.BlockSpec(memory_space=pltpu.SMEM)
    depth_shape = (2,) + body_force.shape[2:]
    return pl.pallas_call(
        functools.partial(fem_horizontal, grid),
        out_shape=(
            jax.ShapeDtypeStruct(body_force.shape, jnp.float32),
            jax.ShapeDtypeStruct(depth_shape, jnp.float32),
        ),
        in_specs=[vmem, smem, vmem],
        out_specs=(vmem, vmem),
        scratch_shapes=fem_scratch(),
    )(fld, element_matrix, body_force)


def fem_second(grid, fld, element_matrix, body_force, previous):
    vmem = pl.BlockSpec(memory_space=pltpu.VMEM)
    smem = pl.BlockSpec(memory_space=pltpu.SMEM)
    return pl.pallas_call(
        functools.partial(fem_vertical, grid),
        out_shape=jax.ShapeDtypeStruct(body_force.shape, jnp.float32),
        in_specs=[vmem, smem, vmem, vmem],
        out_specs=vmem,
        scratch_shapes=fem_scratch(),
    )(fld, element_matrix, body_force, previous)


HIGH = lax.Precision.HIGHEST


def slot_selectors(index, rows, cols):
    live = index >= 0
    row_of = jnp.where(live, index // cols, -1)
    col_of = jnp.where(live, index % cols, -1)
    pick_row = (row_of[:, None] == jnp.arange(rows, dtype=jnp.int32)[None]).astype(jnp.float32)
    pick_col = (col_of[:, None] == jnp.arange(cols, dtype=jnp.int32)[None]).astype(jnp.float32)
    return pick_row, pick_col


def gather_slots(field, pick_row, pick_col):
    cols_taken = jnp.einsum("krc,sc->krs", field, pick_col, precision=HIGH)
    return jnp.sum(jnp.where(pick_row.T[None] > 0.5, cols_taken, 0.0), axis=1)


def scatter_slots(values, pick_row, pick_col):
    weighted = pick_row[None] * values[:, :, None]
    return jnp.einsum("ksr,sc->krc", weighted, pick_col, precision=HIGH)


def layer_total(part):
    count = lax.axis_size("layer")
    copies = jnp.broadcast_to(part[None], (count,) + part.shape)
    gathered = lax.all_to_all(copies, "layer", 0, 0, tiled=True)
    total = gathered[0]
    for source in range(1, count):
        total = total + gathered[source]
    return total


def layer_neighbours(top, bottom):
    count = lax.axis_size("layer")
    place = lax.axis_index("layer")
    chunks = []
    for target in range(count):
        chunk = jnp.where(target == place + 1, top, jnp.where(target == place - 1, bottom, 0.0))
        chunks.append(chunk[None])
    received = lax.all_to_all(jnp.concatenate(chunks, 0), "layer", 0, 0, tiled=True)
    below = jnp.zeros_like(top)
    above = jnp.zeros_like(top)
    for source in range(count):
        below = jnp.where(source == place - 1, received[source], below)
        above = jnp.where(source == place + 1, received[source], above)
    return below, above


def cell_dx(plane):
    return 0.5 * (plane[1:, :-1] + plane[1:, 1:] - (plane[:-1, :-1] + plane[:-1, 1:]))


def cell_dy(plane):
    return 0.5 * (plane[:-1, 1:] + plane[1:, 1:] - (plane[:-1, :-1] + plane[1:, :-1]))


def shelf_residual(padded, friction, driving):
    u_field = padded[0]
    v_field = padded[1]
    h_field = padded[2]
    du_dx = cell_dx(u_field)
    du_dy = cell_dy(u_field)
    dv_dx = cell_dx(v_field)
    dv_dy = cell_dy(v_field)
    h_cell = 0.25 * (h_field[1:, :-1] + h_field[1:, 1:] + h_field[:-1, :-1] + h_field[:-1, 1:])
    tau_xx = h_cell * (4.0 * du_dx + 2.0 * dv_dy)
    tau_yy = h_cell * (4.0 * dv_dy + 2.0 * du_dx)
    tau_xy = h_cell * (du_dy + dv_dx)
    res_x = cell_dx(tau_xx) + cell_dy(tau_xy) - friction * u_field[1:-1, 1:-1] - driving[0]
    res_y = cell_dy(tau_yy) + cell_dx(tau_xy) - friction * v_field[1:-1, 1:-1] - driving[1]
    return jnp.stack([res_x, res_y])


def triangle(stiffness, lows, ups, weight):
    values = jnp.stack(
        [plane[comp] for group in (lows, ups) for comp in range(3) for plane in group]
    )
    viscous = (
        (lows[0][3] + lows[1][3] + lows[2][3] + ups[0][3] + ups[1][3] + ups[2][3]) / 6.0 * weight
    )
    response = (
        jnp.einsum("ab,bxy->axy", stiffness, values, precision=lax.Precision.HIGHEST) * viscous
    )
    return response.reshape((2, 3, 3) + response.shape[1:])


def cell_terms(lower, upper, flag_cells, stiffness, weight):
    low_a, low_b, low_c, low_d = (
        lower[:, :-1, :-1],
        lower[:, 1:, :-1],
        lower[:, :-1, 1:],
        lower[:, 1:, 1:],
    )
    up_a, up_b, up_c, up_d = (
        upper[:, :-1, :-1],
        upper[:, 1:, :-1],
        upper[:, :-1, 1:],
        upper[:, 1:, 1:],
    )
    main_diag = (flag_cells == 0)[None]
    low_far = jnp.where(main_diag, low_d, low_c)
    up_far = jnp.where(main_diag, up_d, up_c)
    low_near = jnp.where(main_diag, low_a, low_b)
    up_near = jnp.where(main_diag, up_a, up_b)
    tri_one = triangle(stiffness, (low_a, low_b, low_far), (up_a, up_b, up_far), weight)
    tri_two = triangle(stiffness, (low_near, low_d, low_c), (up_near, up_d, up_c), weight)
    result = []
    for height in range(2):
        resp_one = tri_one[height]
        resp_two = tri_two[height]
        corner_a = resp_one[:, 0] + jnp.where(main_diag, resp_two[:, 0], 0.0)
        corner_b = resp_one[:, 1] + jnp.where(main_diag, 0.0, resp_two[:, 0])
        corner_c = resp_two[:, 2] + jnp.where(main_diag, 0.0, resp_one[:, 2])
        corner_d = resp_two[:, 1] + jnp.where(main_diag, resp_one[:, 2], 0.0)
        result.append((corner_a, corner_b, corner_c, corner_d))
    return (result[0], result[1])


def add_corners(total, extra):
    if total is None:
        return extra
    return tuple((first_term + other_term for first_term, other_term in zip(total, extra)))


def scaled_by(corners, factor):
    return tuple((member * factor for member in corners))


def own_nodes(corners):
    corner_a, corner_b, corner_c, corner_d = corners
    return corner_a[:, 1:, 1:] + corner_b[:, :-1, 1:] + corner_c[:, 1:, :-1] + corner_d[:, :-1, :-1]


def exchange(axis, sent_up, sent_down):
    count = lax.axis_size(axis)
    up = [(i, i + 1) for i in range(count - 1)]
    down = [(i + 1, i) for i in range(count - 1)]
    return lax.ppermute(sent_up, axis, up), lax.ppermute(sent_down, axis, down)


def packed_halo(arrays, dims, axis):
    ups, downs, shapes = [], [], []
    for array, dim in zip(arrays, dims):
        length = array.shape[dim]
        last = lax.slice_in_dim(array, length - 1, length, axis=dim)
        first = lax.slice_in_dim(array, 0, 1, axis=dim)
        shapes.append(last.shape)
        ups.append(last.reshape(-1))
        downs.append(first.reshape(-1))
    before, after = exchange(axis, jnp.concatenate(ups), jnp.concatenate(downs))
    widened = []
    offset = 0
    for array, dim, shape in zip(arrays, dims, shapes):
        size = 1
        for extent in shape:
            size *= extent
        head = before[offset:offset + size].reshape(shape)
        tail = after[offset:offset + size].reshape(shape)
        offset += size
        widened.append(jnp.concatenate([head, array, tail], axis=dim))
    return widened


def per_device(
    ssa_velocity,
    shelf_viscosity,
    basal_friction,
    driving_stress,
    stokes_velocity,
    ice_viscosity,
    body_force,
    diagonals,
    element_matrix,
    iface_columns,
    iface_nodes,
):
    row_count = ssa_velocity.shape[1]
    col_count = ssa_velocity.shape[2]
    depth_count = stokes_velocity.shape[1]
    block_x = stokes_velocity.shape[2]
    block_y = stokes_velocity.shape[3]
    stacked = jnp.concatenate([ssa_velocity, shelf_viscosity[None]], 0)
    owner_nodes = iface_nodes[0]
    slot_count = owner_nodes.shape[1]
    node_row, node_col = slot_selectors(owner_nodes.reshape(-1), row_count, col_count)
    outgoing = gather_slots(ssa_velocity, node_row, node_col).reshape(2, 3, 3, slot_count)
    raw_planes = jnp.concatenate(
        [
            stokes_velocity.reshape(3 * depth_count, block_x, block_y),
            ice_viscosity,
            diagonals.astype(jnp.float32)[None],
        ],
        0,
    )
    shelf_x, planes_x, slots_x = packed_halo((stacked, raw_planes, outgoing), (1, 1, 1), "mx")
    padded, widened, extended = packed_halo((shelf_x, planes_x, slots_x), (2, 2, 2), "my")
    shelf_res = shelf_residual(padded, basal_friction, driving_stress)
    returned = extended[:, 0::2, 0::2].reshape(2, 9, slot_count)
    columns = iface_columns[0]
    col_row, col_col = slot_selectors(columns.reshape(-1), block_x, block_y)
    placed = scatter_slots(returned.reshape(2, -1), col_row, col_col)
    marked = jnp.einsum("sr,sc->rc", col_row, col_col)
    ring = jnp.concatenate([jnp.minimum(marked, 1.0)[None], placed], 0)
    field_ext = widened[:-1].reshape(4, depth_count, block_x + 2, block_y + 2)
    below_raw, above_raw = layer_neighbours(field_ext[:, -1], field_ext[:, 0])
    (ring_x,) = packed_halo((ring,), (1,), "mx")
    (ring_ext,) = packed_halo((ring_x,), (2,), "my")
    imposed_at = ring_ext[0] > 0.5
    all_layers = jnp.concatenate([below_raw[:, None], field_ext, above_raw[:, None]], 1)
    uv_ext = jnp.where(imposed_at[None, None], ring_ext[1:3, None], all_layers[:2])
    extended_layers = jnp.concatenate([uv_ext, all_layers[2:]], 0)
    grid = (block_x, block_y, lax.axis_size("mx"), lax.axis_size("my"))
    fld = fem_inputs(extended_layers, widened[-1])
    partial_residual, depth_sum = fem_first(grid, fld, element_matrix, body_force)
    stokes_residual = fem_second(grid, fld, element_matrix, body_force, partial_residual)
    bucket = gather_slots(depth_sum, col_row, col_col).reshape(2, 9, slot_count)
    depth_total = layer_total(bucket)
    depth_total, stokes_residual = lax.optimization_barrier((depth_total, stokes_residual))
    grid_back = depth_total.reshape(2, 3, 3, slot_count)
    (back_x,) = packed_halo((grid_back,), (1,), "mx")
    (extended_back,) = packed_halo((back_x,), (2,), "my")
    at_owner = extended_back[:, 0::2, 0::2].reshape(2, 9, slot_count)
    node_force = scatter_slots(at_owner.reshape(2, -1), node_row, node_col)
    coupled_residual = shelf_res - node_force
    return (coupled_residual, stokes_residual)


def solution(mesh):
    return jax.shard_map(
        per_device,
        mesh=mesh,
        in_specs=(
            P(None, "mx", "my"),
            P("mx", "my"),
            P("mx", "my"),
            P(None, "mx", "my"),
            P(None, "layer", "mx", "my"),
            P("layer", "mx", "my"),
            P(None, "layer", "mx", "my"),
            P("mx", "my"),
            P(),
            P(("mx", "my"), None, None),
            P(("mx", "my"), None, None),
        ),
        out_specs=(P(None, "mx", "my"), P(None, "layer", "mx", "my")),
        check_vma=False,
    )
```

```python
import functools

import jax
import jax.numpy as jnp
from jax import lax
from jax.sharding import PartitionSpec as P
from jax.experimental import pallas as pl
from jax.experimental.pallas import tpu as pltpu

ROWS_PAD, LANES_PAD = 24, 384


def cell_weight(grid):
    block_x, block_y, count_x, count_y = grid
    rows = lax.broadcasted_iota(jnp.int32, (ROWS_PAD, LANES_PAD), 0)
    lanes = lax.broadcasted_iota(jnp.int32, (ROWS_PAD, LANES_PAD), 1)
    global_x = lax.axis_index("mx") * block_x + rows - 1
    global_y = lax.axis_index("my") * block_y + lanes - 1
    valid = (global_x >= 0) & (global_x <= count_x * block_x - 2) & (rows <= block_x)
    valid = valid & (global_y >= 0) & (global_y <= count_y * block_y - 2) & (lanes <= block_y)
    return valid.astype(jnp.float32)


def fem_body(comps, grid, own_ref, below_ref, above_ref, ring_ref, kmat_ref, body_ref, out_ref, vals_ref, vis_ref, resp_ref):
    own_layers = (own_ref.shape[0] - 1) // 4
    layers = own_layers + 2
    main = own_ref[4 * own_layers] == 0.0
    imposed = ring_ref[0] > 0.5

    def plane_of(comp, layer):
        if layer == 0:
            plane = below_ref[comp]
        elif layer == layers - 1:
            plane = above_ref[comp]
        else:
            plane = own_ref[comp * own_layers + layer - 1]
        if comp < 2:
            plane = jnp.where(imposed, ring_ref[1 + comp], plane)
        return plane

    weight = cell_weight(grid)
    layer_index = lax.axis_index("layer")
    below_live = (layer_index > 0).astype(jnp.float32)
    above_live = (layer_index < lax.axis_size("layer") - 1).astype(jnp.float32)
    zero = jnp.zeros((ROWS_PAD, LANES_PAD), jnp.float32)
    for comp in comps:
        out_ref[comp] = -body_ref[comp]
    rows_out = [height * 9 + comp * 3 + vertex for height in range(2) for comp in comps for vertex in range(3)]
    pairs = layers - 1

    def layer_views(layer):
        slot = layer % 2
        for comp in range(4):
            plane = plane_of(comp, layer)
            below = pltpu.roll(plane, ROWS_PAD - 1, 0)
            right = pltpu.roll(plane, LANES_PAD - 1, 1)
            diag = pltpu.roll(below, LANES_PAD - 1, 1)
            far = jnp.where(main, diag, right)
            near = jnp.where(main, plane, below)
            for tri, views in enumerate(((plane, below, far), (near, diag, right))):
                for vertex in range(3):
                    vals_ref[slot, tri, comp * 3 + vertex] = views[vertex]

    layer_views(0)
    for pair in range(pairs):
        layer_views(pair + 1)
        slots = (pair % 2, (pair + 1) % 2)
        for tri in range(2):
            total = None
            for height in range(2):
                for vertex in range(3):
                    term = vals_ref[slots[height], tri, 9 + vertex]
                    total = term if total is None else total + term
            vis_ref[tri] = total / 6.0 * weight

        def tile_body(block, carry):
            row = pl.multiple_of(block * 8, 8)
            for tri in range(2):
                vis = vis_ref[tri, pl.ds(row, 8), :]
                values = [vals_ref[slots[beta // 9], tri, beta % 9, pl.ds(row, 8), :] for beta in range(18)]
                for alpha in rows_out:
                    acc = kmat_ref[alpha, 0] * values[0]
                    for beta in range(1, 18):
                        acc = acc + kmat_ref[alpha, beta] * values[beta]
                    resp_ref[tri, alpha, pl.ds(row, 8), :] = acc * vis
            return carry

        lax.fori_loop(0, ROWS_PAD // 8, tile_body, 0)
        for height in range(2):
            own_layer = pair + height - 1
            if own_layer < 0 or own_layer > pairs - 2:
                continue
            scale = None
            if pair == 0 and height == 1:
                scale = below_live
            if pair == pairs - 1 and height == 0:
                scale = above_live
            for comp in comps:
                base = height * 9 + comp * 3
                one = [resp_ref[0, base + v] for v in range(3)]
                two = [resp_ref[1, base + v] for v in range(3)]
                corner_a = one[0] + jnp.where(main, two[0], zero)
                corner_b = one[1] + jnp.where(main, zero, two[0])
                corner_c = two[2] + jnp.where(main, zero, one[2])
                corner_d = two[1] + jnp.where(main, one[2], zero)
                node = (pltpu.roll(pltpu.roll(corner_a, ROWS_PAD - 1, 0), LANES_PAD - 1, 1)
                        + pltpu.roll(corner_b, LANES_PAD - 1, 1)
                        + pltpu.roll(corner_c, ROWS_PAD - 1, 0) + corner_d)
                part = node[0:16, 0:256]
                if scale is not None:
                    part = part * scale
                out_ref[comp, own_layer] = out_ref[comp, own_layer] + part


def fem_horizontal(grid, own_ref, below_ref, above_ref, ring_ref, kmat_ref, body_ref, out_ref, depth_ref, vals_ref, vis_ref, resp_ref):
    fem_body((0, 1), grid, own_ref, below_ref, above_ref, ring_ref, kmat_ref, body_ref, out_ref, vals_ref, vis_ref, resp_ref)
    for comp in range(2):
        total = out_ref[comp, 0]
        for layer in range(1, out_ref.shape[1]):
            total = total + out_ref[comp, layer]
        depth_ref[comp] = total


def fem_vertical(grid, own_ref, below_ref, above_ref, ring_ref, kmat_ref, body_ref, prev_ref, out_ref, vals_ref, vis_ref, resp_ref):
    out_ref[0:2] = prev_ref[0:2]
    fem_body((2,), grid, own_ref, below_ref, above_ref, ring_ref, kmat_ref, body_ref, out_ref, vals_ref, vis_ref, resp_ref)


def padded_planes(planes):
    rows, lanes = planes.shape[-2:]
    return jnp.pad(planes, ((0, 0), (0, ROWS_PAD - rows), (0, LANES_PAD - lanes)))


def fem_scratch():
    return [
        pltpu.VMEM((2, 2, 12, ROWS_PAD, LANES_PAD), jnp.float32),
        pltpu.VMEM((2, ROWS_PAD, LANES_PAD), jnp.float32),
        pltpu.VMEM((2, 18, ROWS_PAD, LANES_PAD), jnp.float32),
    ]


def fem_first(grid, fields, element_matrix, body_force):
    vmem = pl.BlockSpec(memory_space=pltpu.VMEM)
    smem = pl.BlockSpec(memory_space=pltpu.SMEM)
    depth_shape = (2,) + body_force.shape[2:]
    return pl.pallas_call(
        functools.partial(fem_horizontal, grid),
        out_shape=(
            jax.ShapeDtypeStruct(body_force.shape, jnp.float32),
            jax.ShapeDtypeStruct(depth_shape, jnp.float32),
        ),
        in_specs=[vmem] * 4 + [smem, vmem],
        out_specs=(vmem, vmem),
        scratch_shapes=fem_scratch(),
    )(*fields, element_matrix, body_force)


def fem_second(grid, fields, element_matrix, body_force, previous):
    vmem = pl.BlockSpec(memory_space=pltpu.VMEM)
    smem = pl.BlockSpec(memory_space=pltpu.SMEM)
    return pl.pallas_call(
        functools.partial(fem_vertical, grid),
        out_shape=jax.ShapeDtypeStruct(body_force.shape, jnp.float32),
        in_specs=[vmem] * 4 + [smem, vmem, vmem],
        out_specs=vmem,
        scratch_shapes=fem_scratch(),
    )(*fields, element_matrix, body_force, previous)


HIGH = lax.Precision.HIGHEST


def slot_selectors(index, rows, cols):
    live = index >= 0
    row_of = jnp.where(live, index // cols, -1)
    col_of = jnp.where(live, index % cols, -1)
    pick_row = (row_of[:, None] == jnp.arange(rows, dtype=jnp.int32)[None]).astype(jnp.float32)
    pick_col = (col_of[:, None] == jnp.arange(cols, dtype=jnp.int32)[None]).astype(jnp.float32)
    return pick_row, pick_col


def gather_slots(field, pick_row, pick_col):
    cols_taken = jnp.einsum("krc,sc->krs", field, pick_col, precision=HIGH)
    return jnp.sum(jnp.where(pick_row.T[None] > 0.5, cols_taken, 0.0), axis=1)


def scatter_slots(values, pick_row, pick_col):
    weighted = pick_row[None] * values[:, :, None]
    return jnp.einsum("ksr,sc->krc", weighted, pick_col, precision=HIGH)


def layer_total(part):
    count = lax.axis_size("layer")
    copies = jnp.broadcast_to(part[None], (count,) + part.shape)
    gathered = lax.all_to_all(copies, "layer", 0, 0, tiled=True)
    total = gathered[0]
    for source in range(1, count):
        total = total + gathered[source]
    return total


def layer_neighbours(top, bottom):
    count = lax.axis_size("layer")
    place = lax.axis_index("layer")
    chunks = []
    for target in range(count):
        chunk = jnp.where(target == place + 1, top, jnp.where(target == place - 1, bottom, 0.0))
        chunks.append(chunk[None])
    received = lax.all_to_all(jnp.concatenate(chunks, 0), "layer", 0, 0, tiled=True)
    below = jnp.zeros_like(top)
    above = jnp.zeros_like(top)
    for source in range(count):
        below = jnp.where(source == place - 1, received[source], below)
        above = jnp.where(source == place + 1, received[source], above)
    return below, above


def cell_dx(plane):
    return 0.5 * (plane[1:, :-1] + plane[1:, 1:] - (plane[:-1, :-1] + plane[:-1, 1:]))


def cell_dy(plane):
    return 0.5 * (plane[:-1, 1:] + plane[1:, 1:] - (plane[:-1, :-1] + plane[1:, :-1]))


def shelf_residual(padded, friction, driving):
    u_field = padded[0]
    v_field = padded[1]
    h_field = padded[2]
    du_dx = cell_dx(u_field)
    du_dy = cell_dy(u_field)
    dv_dx = cell_dx(v_field)
    dv_dy = cell_dy(v_field)
    h_cell = 0.25 * (h_field[1:, :-1] + h_field[1:, 1:] + h_field[:-1, :-1] + h_field[:-1, 1:])
    tau_xx = h_cell * (4.0 * du_dx + 2.0 * dv_dy)
    tau_yy = h_cell * (4.0 * dv_dy + 2.0 * du_dx)
    tau_xy = h_cell * (du_dy + dv_dx)
    res_x = cell_dx(tau_xx) + cell_dy(tau_xy) - friction * u_field[1:-1, 1:-1] - driving[0]
    res_y = cell_dy(tau_yy) + cell_dx(tau_xy) - friction * v_field[1:-1, 1:-1] - driving[1]
    return jnp.stack([res_x, res_y])


def triangle(stiffness, lows, ups, weight):
    values = jnp.stack(
        [plane[comp] for group in (lows, ups) for comp in range(3) for plane in group]
    )
    viscous = (
        (lows[0][3] + lows[1][3] + lows[2][3] + ups[0][3] + ups[1][3] + ups[2][3]) / 6.0 * weight
    )
    response = (
        jnp.einsum("ab,bxy->axy", stiffness, values, precision=lax.Precision.HIGHEST) * viscous
    )
    return response.reshape((2, 3, 3) + response.shape[1:])


def cell_terms(lower, upper, flag_cells, stiffness, weight):
    low_a, low_b, low_c, low_d = (
        lower[:, :-1, :-1],
        lower[:, 1:, :-1],
        lower[:, :-1, 1:],
        lower[:, 1:, 1:],
    )
    up_a, up_b, up_c, up_d = (
        upper[:, :-1, :-1],
        upper[:, 1:, :-1],
        upper[:, :-1, 1:],
        upper[:, 1:, 1:],
    )
    main_diag = (flag_cells == 0)[None]
    low_far = jnp.where(main_diag, low_d, low_c)
    up_far = jnp.where(main_diag, up_d, up_c)
    low_near = jnp.where(main_diag, low_a, low_b)
    up_near = jnp.where(main_diag, up_a, up_b)
    tri_one = triangle(stiffness, (low_a, low_b, low_far), (up_a, up_b, up_far), weight)
    tri_two = triangle(stiffness, (low_near, low_d, low_c), (up_near, up_d, up_c), weight)
    result = []
    for height in range(2):
        resp_one = tri_one[height]
        resp_two = tri_two[height]
        corner_a = resp_one[:, 0] + jnp.where(main_diag, resp_two[:, 0], 0.0)
        corner_b = resp_one[:, 1] + jnp.where(main_diag, 0.0, resp_two[:, 0])
        corner_c = resp_two[:, 2] + jnp.where(main_diag, 0.0, resp_one[:, 2])
        corner_d = resp_two[:, 1] + jnp.where(main_diag, resp_one[:, 2], 0.0)
        result.append((corner_a, corner_b, corner_c, corner_d))
    return (result[0], result[1])


def add_corners(total, extra):
    if total is None:
        return extra
    return tuple((first_term + other_term for first_term, other_term in zip(total, extra)))


def scaled_by(corners, factor):
    return tuple((member * factor for member in corners))


def own_nodes(corners):
    corner_a, corner_b, corner_c, corner_d = corners
    return corner_a[:, 1:, 1:] + corner_b[:, :-1, 1:] + corner_c[:, 1:, :-1] + corner_d[:, :-1, :-1]


def exchange(axis, sent_up, sent_down):
    count = lax.axis_size(axis)
    up = [(i, i + 1) for i in range(count - 1)]
    down = [(i + 1, i) for i in range(count - 1)]
    return lax.ppermute(sent_up, axis, up), lax.ppermute(sent_down, axis, down)


def packed_halo(arrays, dims, axis):
    ups, downs, shapes = [], [], []
    for array, dim in zip(arrays, dims):
        length = array.shape[dim]
        last = lax.slice_in_dim(array, length - 1, length, axis=dim)
        first = lax.slice_in_dim(array, 0, 1, axis=dim)
        shapes.append(last.shape)
        ups.append(last.reshape(-1))
        downs.append(first.reshape(-1))
    before, after = exchange(axis, jnp.concatenate(ups), jnp.concatenate(downs))
    widened = []
    offset = 0
    for array, dim, shape in zip(arrays, dims, shapes):
        size = 1
        for extent in shape:
            size *= extent
        head = before[offset:offset + size].reshape(shape)
        tail = after[offset:offset + size].reshape(shape)
        offset += size
        widened.append(jnp.concatenate([head, array, tail], axis=dim))
    return widened


def per_device(
    ssa_velocity,
    shelf_viscosity,
    basal_friction,
    driving_stress,
    stokes_velocity,
    ice_viscosity,
    body_force,
    diagonals,
    element_matrix,
    iface_columns,
    iface_nodes,
):
    row_count = ssa_velocity.shape[1]
    col_count = ssa_velocity.shape[2]
    depth_count = stokes_velocity.shape[1]
    block_x = stokes_velocity.shape[2]
    block_y = stokes_velocity.shape[3]
    stacked = jnp.concatenate([ssa_velocity, shelf_viscosity[None]], 0)
    owner_nodes = iface_nodes[0]
    slot_count = owner_nodes.shape[1]
    node_row, node_col = slot_selectors(owner_nodes.reshape(-1), row_count, col_count)
    outgoing = gather_slots(ssa_velocity, node_row, node_col).reshape(2, 3, 3, slot_count)
    raw_planes = jnp.concatenate(
        [
            stokes_velocity.reshape(3 * depth_count, block_x, block_y),
            ice_viscosity,
            diagonals.astype(jnp.float32)[None],
        ],
        0,
    )
    shelf_x, planes_x, slots_x = packed_halo((stacked, raw_planes, outgoing), (1, 1, 1), "mx")
    padded, widened, extended = packed_halo((shelf_x, planes_x, slots_x), (2, 2, 2), "my")
    shelf_res = shelf_residual(padded, basal_friction, driving_stress)
    returned = extended[:, 0::2, 0::2].reshape(2, 9, slot_count)
    columns = iface_columns[0]
    col_row, col_col = slot_selectors(columns.reshape(-1), block_x, block_y)
    placed = scatter_slots(returned.reshape(2, -1), col_row, col_col)
    marked = jnp.einsum("sr,sc->rc", col_row, col_col)
    ring = jnp.concatenate([jnp.minimum(marked, 1.0)[None], placed], 0)
    field_ext = widened[:-1].reshape(4, depth_count, block_x + 2, block_y + 2)
    below_raw, above_raw = layer_neighbours(field_ext[:, -1], field_ext[:, 0])
    (ring_x,) = packed_halo((ring,), (1,), "mx")
    (ring_ext,) = packed_halo((ring_x,), (2,), "my")
    fields = (padded_planes(widened), padded_planes(below_raw), padded_planes(above_raw), padded_planes(ring_ext))
    grid = (block_x, block_y, lax.axis_size("mx"), lax.axis_size("my"))
    partial_residual, depth_sum = fem_first(grid, fields, element_matrix, body_force)
    stokes_residual = fem_second(grid, fields, element_matrix, body_force, partial_residual)
    bucket = gather_slots(depth_sum, col_row, col_col).reshape(2, 9, slot_count)
    depth_total = layer_total(bucket)
    depth_total, stokes_residual = lax.optimization_barrier((depth_total, stokes_residual))
    grid_back = depth_total.reshape(2, 3, 3, slot_count)
    (back_x,) = packed_halo((grid_back,), (1,), "mx")
    (extended_back,) = packed_halo((back_x,), (2,), "my")
    at_owner = extended_back[:, 0::2, 0::2].reshape(2, 9, slot_count)
    node_force = scatter_slots(at_owner.reshape(2, -1), node_row, node_col)
    coupled_residual = shelf_res - node_force
    return (coupled_residual, stokes_residual)


def solution(mesh):
    return jax.shard_map(
        per_device,
        mesh=mesh,
        in_specs=(
            P(None, "mx", "my"),
            P("mx", "my"),
            P("mx", "my"),
            P(None, "mx", "my"),
            P(None, "layer", "mx", "my"),
            P("layer", "mx", "my"),
            P(None, "layer", "mx", "my"),
            P("mx", "my"),
            P(),
            P(("mx", "my"), None, None),
            P(("mx", "my"), None, None),
        ),
        out_specs=(P(None, "mx", "my"), P(None, "layer", "mx", "my")),
        check_vma=False,
    )
```

```python
import functools

import jax
import jax.numpy as jnp
from jax import lax
from jax.sharding import PartitionSpec as P
from jax.experimental import pallas as pl
from jax.experimental.pallas import tpu as pltpu

ROWS_PAD, LANES_PAD = 24, 384


def cell_weight(grid):
    block_x, block_y, count_x, count_y = grid
    rows = lax.broadcasted_iota(jnp.int32, (ROWS_PAD, LANES_PAD), 0)
    lanes = lax.broadcasted_iota(jnp.int32, (ROWS_PAD, LANES_PAD), 1)
    global_x = lax.axis_index("mx") * block_x + rows - 1
    global_y = lax.axis_index("my") * block_y + lanes - 1
    valid = (global_x >= 0) & (global_x <= count_x * block_x - 2) & (rows <= block_x)
    valid = valid & (global_y >= 0) & (global_y <= count_y * block_y - 2) & (lanes <= block_y)
    return valid.astype(jnp.float32)


def fem_body(comps, grid, fld_ref, kmat_ref, body_ref, out_ref, vals_ref, vis_ref, resp_ref):
    layers = (fld_ref.shape[0] - 1) // 4
    main = fld_ref[4 * layers] == 0.0
    weight = cell_weight(grid)
    layer_index = lax.axis_index("layer")
    below_live = (layer_index > 0).astype(jnp.float32)
    above_live = (layer_index < lax.axis_size("layer") - 1).astype(jnp.float32)
    zero = jnp.zeros((ROWS_PAD, LANES_PAD), jnp.float32)
    for comp in comps:
        out_ref[comp] = -body_ref[comp]
    rows_out = [height * 9 + comp * 3 + vertex for height in range(2) for comp in comps for vertex in range(3)]
    pairs = layers - 1

    def layer_views(layer):
        slot = layer % 2
        for comp in range(4):
            plane = fld_ref[comp * layers + layer]
            below = pltpu.roll(plane, ROWS_PAD - 1, 0)
            right = pltpu.roll(plane, LANES_PAD - 1, 1)
            diag = pltpu.roll(below, LANES_PAD - 1, 1)
            far = jnp.where(main, diag, right)
            near = jnp.where(main, plane, below)
            for tri, views in enumerate(((plane, below, far), (near, diag, right))):
                for vertex in range(3):
                    vals_ref[slot, tri, comp * 3 + vertex] = views[vertex]

    layer_views(0)
    for pair in range(pairs):
        layer_views(pair + 1)
        slots = (pair % 2, (pair + 1) % 2)
        for tri in range(2):
            total = None
            for height in range(2):
                for vertex in range(3):
                    term = vals_ref[slots[height], tri, 9 + vertex]
                    total = term if total is None else total + term
            vis_ref[tri] = total / 6.0 * weight

        def tile_body(block, carry):
            row = pl.multiple_of(block * 8, 8)
            for tri in range(2):
                vis = vis_ref[tri, pl.ds(row, 8), :]
                values = [vals_ref[slots[beta // 9], tri, beta % 9, pl.ds(row, 8), :] for beta in range(18)]
                for alpha in rows_out:
                    acc = kmat_ref[alpha, 0] * values[0]
                    for beta in range(1, 18):
                        acc = acc + kmat_ref[alpha, beta] * values[beta]
                    resp_ref[tri, alpha, pl.ds(row, 8), :] = acc * vis
            return carry

        lax.fori_loop(0, ROWS_PAD // 8, tile_body, 0)
        for height in range(2):
            own_layer = pair + height - 1
            if own_layer < 0 or own_layer > pairs - 2:
                continue
            scale = None
            if pair == 0 and height == 1:
                scale = below_live
            if pair == pairs - 1 and height == 0:
                scale = above_live
            for comp in comps:
                base = height * 9 + comp * 3
                one = [resp_ref[0, base + v] for v in range(3)]
                two = [resp_ref[1, base + v] for v in range(3)]
                corner_a = one[0] + jnp.where(main, two[0], zero)
                corner_b = one[1] + jnp.where(main, zero, two[0])
                corner_c = two[2] + jnp.where(main, zero, one[2])
                corner_d = two[1] + jnp.where(main, one[2], zero)
                node = (pltpu.roll(pltpu.roll(corner_a, ROWS_PAD - 1, 0), LANES_PAD - 1, 1)
                        + pltpu.roll(corner_b, LANES_PAD - 1, 1)
                        + pltpu.roll(corner_c, ROWS_PAD - 1, 0) + corner_d)
                part = node[0:16, 0:256]
                if scale is not None:
                    part = part * scale
                out_ref[comp, own_layer] = out_ref[comp, own_layer] + part


def fem_horizontal(grid, fld_ref, kmat_ref, body_ref, out_ref, depth_ref, vals_ref, vis_ref, resp_ref):
    fem_body((0, 1), grid, fld_ref, kmat_ref, body_ref, out_ref, vals_ref, vis_ref, resp_ref)
    for comp in range(2):
        total = out_ref[comp, 0]
        for layer in range(1, out_ref.shape[1]):
            total = total + out_ref[comp, layer]
        depth_ref[comp] = total


def fem_vertical(grid, fld_ref, kmat_ref, body_ref, prev_ref, out_ref, vals_ref, vis_ref, resp_ref):
    out_ref[0:2] = prev_ref[0:2]
    fem_body((2,), grid, fld_ref, kmat_ref, body_ref, out_ref, vals_ref, vis_ref, resp_ref)


def fem_inputs(extended_layers, diag_ext):
    comps, layers, rows, lanes = extended_layers.shape
    planes = jnp.concatenate([extended_layers.reshape(comps * layers, rows, lanes), diag_ext[None]], 0)
    return jnp.pad(planes, ((0, 0), (0, ROWS_PAD - rows), (0, LANES_PAD - lanes)))


def fem_scratch():
    return [
        pltpu.VMEM((2, 2, 12, ROWS_PAD, LANES_PAD), jnp.float32),
        pltpu.VMEM((2, ROWS_PAD, LANES_PAD), jnp.float32),
        pltpu.VMEM((2, 18, ROWS_PAD, LANES_PAD), jnp.float32),
    ]


def fem_first(grid, fld, element_matrix, body_force):
    vmem = pl.BlockSpec(memory_space=pltpu.VMEM)
    smem = pl.BlockSpec(memory_space=pltpu.SMEM)
    depth_shape = (2,) + body_force.shape[2:]
    return pl.pallas_call(
        functools.partial(fem_horizontal, grid),
        out_shape=(
            jax.ShapeDtypeStruct(body_force.shape, jnp.float32),
            jax.ShapeDtypeStruct(depth_shape, jnp.float32),
        ),
        in_specs=[vmem, smem, vmem],
        out_specs=(vmem, vmem),
        scratch_shapes=fem_scratch(),
    )(fld, element_matrix, body_force)


def fem_second(grid, fld, element_matrix, body_force, previous):
    vmem = pl.BlockSpec(memory_space=pltpu.VMEM)
    smem = pl.BlockSpec(memory_space=pltpu.SMEM)
    return pl.pallas_call(
        functools.partial(fem_vertical, grid),
        out_shape=jax.ShapeDtypeStruct(body_force.shape, jnp.float32),
        in_specs=[vmem, smem, vmem, vmem],
        out_specs=vmem,
        scratch_shapes=fem_scratch(),
    )(fld, element_matrix, body_force, previous)


HIGH = lax.Precision.HIGHEST


def slot_selectors(index, rows, cols):
    live = index >= 0
    row_of = jnp.where(live, index // cols, -1)
    col_of = jnp.where(live, index % cols, -1)
    pick_row = (row_of[:, None] == jnp.arange(rows, dtype=jnp.int32)[None]).astype(jnp.float32)
    pick_col = (col_of[:, None] == jnp.arange(cols, dtype=jnp.int32)[None]).astype(jnp.float32)
    return pick_row, pick_col


def gather_slots(field, pick_row, pick_col):
    cols_taken = jnp.einsum("krc,sc->krs", field, pick_col, precision=HIGH)
    return jnp.sum(jnp.where(pick_row.T[None] > 0.5, cols_taken, 0.0), axis=1)


def scatter_slots(values, pick_row, pick_col):
    weighted = pick_row[None] * values[:, :, None]
    return jnp.einsum("ksr,sc->krc", weighted, pick_col, precision=HIGH)


def layer_total(copies):
    gathered = lax.all_to_all(copies, "layer", 0, 0, tiled=True)
    total = gathered[0]
    for source in range(1, copies.shape[0]):
        total = total + gathered[source]
    return total


def layer_neighbours(top, bottom):
    count = lax.axis_size("layer")
    place = lax.axis_index("layer")
    chunks = []
    for target in range(count):
        chunk = jnp.where(target == place + 1, top, jnp.where(target == place - 1, bottom, 0.0))
        chunks.append(chunk[None])
    received = lax.all_to_all(jnp.concatenate(chunks, 0), "layer", 0, 0, tiled=True)
    below = jnp.zeros_like(top)
    above = jnp.zeros_like(top)
    for source in range(count):
        below = jnp.where(source == place - 1, received[source], below)
        above = jnp.where(source == place + 1, received[source], above)
    return below, above


def cell_dx(plane):
    return 0.5 * (plane[1:, :-1] + plane[1:, 1:] - (plane[:-1, :-1] + plane[:-1, 1:]))


def cell_dy(plane):
    return 0.5 * (plane[:-1, 1:] + plane[1:, 1:] - (plane[:-1, :-1] + plane[1:, :-1]))


def shelf_residual(padded, friction, driving):
    u_field = padded[0]
    v_field = padded[1]
    h_field = padded[2]
    du_dx = cell_dx(u_field)
    du_dy = cell_dy(u_field)
    dv_dx = cell_dx(v_field)
    dv_dy = cell_dy(v_field)
    h_cell = 0.25 * (h_field[1:, :-1] + h_field[1:, 1:] + h_field[:-1, :-1] + h_field[:-1, 1:])
    tau_xx = h_cell * (4.0 * du_dx + 2.0 * dv_dy)
    tau_yy = h_cell * (4.0 * dv_dy + 2.0 * du_dx)
    tau_xy = h_cell * (du_dy + dv_dx)
    res_x = cell_dx(tau_xx) + cell_dy(tau_xy) - friction * u_field[1:-1, 1:-1] - driving[0]
    res_y = cell_dy(tau_yy) + cell_dx(tau_xy) - friction * v_field[1:-1, 1:-1] - driving[1]
    return jnp.stack([res_x, res_y])


def triangle(stiffness, lows, ups, weight):
    values = jnp.stack(
        [plane[comp] for group in (lows, ups) for comp in range(3) for plane in group]
    )
    viscous = (
        (lows[0][3] + lows[1][3] + lows[2][3] + ups[0][3] + ups[1][3] + ups[2][3]) / 6.0 * weight
    )
    response = (
        jnp.einsum("ab,bxy->axy", stiffness, values, precision=lax.Precision.HIGHEST) * viscous
    )
    return response.reshape((2, 3, 3) + response.shape[1:])


def cell_terms(lower, upper, flag_cells, stiffness, weight):
    low_a, low_b, low_c, low_d = (
        lower[:, :-1, :-1],
        lower[:, 1:, :-1],
        lower[:, :-1, 1:],
        lower[:, 1:, 1:],
    )
    up_a, up_b, up_c, up_d = (
        upper[:, :-1, :-1],
        upper[:, 1:, :-1],
        upper[:, :-1, 1:],
        upper[:, 1:, 1:],
    )
    main_diag = (flag_cells == 0)[None]
    low_far = jnp.where(main_diag, low_d, low_c)
    up_far = jnp.where(main_diag, up_d, up_c)
    low_near = jnp.where(main_diag, low_a, low_b)
    up_near = jnp.where(main_diag, up_a, up_b)
    tri_one = triangle(stiffness, (low_a, low_b, low_far), (up_a, up_b, up_far), weight)
    tri_two = triangle(stiffness, (low_near, low_d, low_c), (up_near, up_d, up_c), weight)
    result = []
    for height in range(2):
        resp_one = tri_one[height]
        resp_two = tri_two[height]
        corner_a = resp_one[:, 0] + jnp.where(main_diag, resp_two[:, 0], 0.0)
        corner_b = resp_one[:, 1] + jnp.where(main_diag, 0.0, resp_two[:, 0])
        corner_c = resp_two[:, 2] + jnp.where(main_diag, 0.0, resp_one[:, 2])
        corner_d = resp_two[:, 1] + jnp.where(main_diag, resp_one[:, 2], 0.0)
        result.append((corner_a, corner_b, corner_c, corner_d))
    return (result[0], result[1])


def add_corners(total, extra):
    if total is None:
        return extra
    return tuple((first_term + other_term for first_term, other_term in zip(total, extra)))


def scaled_by(corners, factor):
    return tuple((member * factor for member in corners))


def own_nodes(corners):
    corner_a, corner_b, corner_c, corner_d = corners
    return corner_a[:, 1:, 1:] + corner_b[:, :-1, 1:] + corner_c[:, 1:, :-1] + corner_d[:, :-1, :-1]


def exchange(axis, sent_up, sent_down):
    count = lax.axis_size(axis)
    up = [(i, i + 1) for i in range(count - 1)]
    down = [(i + 1, i) for i in range(count - 1)]
    return lax.ppermute(sent_up, axis, up), lax.ppermute(sent_down, axis, down)


def packed_halo(arrays, dims, axis):
    ups, downs, shapes = [], [], []
    for array, dim in zip(arrays, dims):
        length = array.shape[dim]
        last = lax.slice_in_dim(array, length - 1, length, axis=dim)
        first = lax.slice_in_dim(array, 0, 1, axis=dim)
        shapes.append(last.shape)
        ups.append(last.reshape(-1))
        downs.append(first.reshape(-1))
    before, after = exchange(axis, jnp.concatenate(ups), jnp.concatenate(downs))
    widened = []
    offset = 0
    for array, dim, shape in zip(arrays, dims, shapes):
        size = 1
        for extent in shape:
            size *= extent
        head = before[offset:offset + size].reshape(shape)
        tail = after[offset:offset + size].reshape(shape)
        offset += size
        widened.append(jnp.concatenate([head, array, tail], axis=dim))
    return widened


def per_device(
    ssa_velocity,
    shelf_viscosity,
    basal_friction,
    driving_stress,
    stokes_velocity,
    ice_viscosity,
    body_force,
    diagonals,
    element_matrix,
    iface_columns,
    iface_nodes,
):
    row_count = ssa_velocity.shape[1]
    col_count = ssa_velocity.shape[2]
    depth_count = stokes_velocity.shape[1]
    block_x = stokes_velocity.shape[2]
    block_y = stokes_velocity.shape[3]
    stacked = jnp.concatenate([ssa_velocity, shelf_viscosity[None]], 0)
    owner_nodes = iface_nodes[0]
    slot_count = owner_nodes.shape[1]
    node_row, node_col = slot_selectors(owner_nodes.reshape(-1), row_count, col_count)
    outgoing = gather_slots(ssa_velocity, node_row, node_col).reshape(2, 3, 3, slot_count)
    raw_planes = jnp.concatenate(
        [
            stokes_velocity.reshape(3 * depth_count, block_x, block_y),
            ice_viscosity,
            diagonals.astype(jnp.float32)[None],
        ],
        0,
    )
    shelf_x, planes_x, slots_x = packed_halo((stacked, raw_planes, outgoing), (1, 1, 1), "mx")
    padded, widened, extended = packed_halo((shelf_x, planes_x, slots_x), (2, 2, 2), "my")
    shelf_res = shelf_residual(padded, basal_friction, driving_stress)
    returned = extended[:, 0::2, 0::2].reshape(2, 9, slot_count)
    columns = iface_columns[0]
    col_row, col_col = slot_selectors(columns.reshape(-1), block_x, block_y)
    placed = scatter_slots(returned.reshape(2, -1), col_row, col_col)
    marked = jnp.einsum("sr,sc->rc", col_row, col_col)
    ring = jnp.concatenate([jnp.minimum(marked, 1.0)[None], placed], 0)
    field_ext = widened[:-1].reshape(4, depth_count, block_x + 2, block_y + 2)
    below_raw, above_raw = layer_neighbours(field_ext[:, -1], field_ext[:, 0])
    (ring_x,) = packed_halo((ring,), (1,), "mx")
    (ring_ext,) = packed_halo((ring_x,), (2,), "my")
    imposed_at = ring_ext[0] > 0.5
    all_layers = jnp.concatenate([below_raw[:, None], field_ext, above_raw[:, None]], 1)
    uv_ext = jnp.where(imposed_at[None, None], ring_ext[1:3, None], all_layers[:2])
    extended_layers = jnp.concatenate([uv_ext, all_layers[2:]], 0)
    grid = (block_x, block_y, lax.axis_size("mx"), lax.axis_size("my"))
    fld = fem_inputs(extended_layers, widened[-1])
    partial_residual, depth_sum = fem_first(grid, fld, element_matrix, body_force)
    stokes_residual = fem_second(grid, fld, element_matrix, body_force, partial_residual)
    count = lax.axis_size("layer")
    cols_taken = jnp.einsum("krc,sc->krs", depth_sum, col_col, precision=HIGH)
    spread = jnp.broadcast_to(cols_taken[None], (count,) + cols_taken.shape)
    copies = jnp.sum(jnp.where(col_row.T[None, None] > 0.5, spread, 0.0), axis=2)
    depth_total = layer_total(copies.reshape(count, 2, 9, slot_count))
    depth_total, stokes_residual = lax.optimization_barrier((depth_total, stokes_residual))
    grid_back = depth_total.reshape(2, 3, 3, slot_count)
    (back_x,) = packed_halo((grid_back,), (1,), "mx")
    (extended_back,) = packed_halo((back_x,), (2,), "my")
    at_owner = extended_back[:, 0::2, 0::2].reshape(2, 9, slot_count)
    node_force = scatter_slots(at_owner.reshape(2, -1), node_row, node_col)
    coupled_residual = shelf_res - node_force
    return (coupled_residual, stokes_residual)


def solution(mesh):
    return jax.shard_map(
        per_device,
        mesh=mesh,
        in_specs=(
            P(None, "mx", "my"),
            P("mx", "my"),
            P("mx", "my"),
            P(None, "mx", "my"),
            P(None, "layer", "mx", "my"),
            P("layer", "mx", "my"),
            P(None, "layer", "mx", "my"),
            P("mx", "my"),
            P(),
            P(("mx", "my"), None, None),
            P(("mx", "my"), None, None),
        ),
        out_specs=(P(None, "mx", "my"), P(None, "layer", "mx", "my")),
        check_vma=False,
    )
```

```python
import functools

import jax
import jax.numpy as jnp
from jax import lax
from jax.sharding import PartitionSpec as P
from jax.experimental import pallas as pl
from jax.experimental.pallas import tpu as pltpu

ROWS_PAD, LANES_PAD = 24, 384


def cell_weight(grid):
    block_x, block_y, count_x, count_y = grid
    rows = lax.broadcasted_iota(jnp.int32, (ROWS_PAD, LANES_PAD), 0)
    lanes = lax.broadcasted_iota(jnp.int32, (ROWS_PAD, LANES_PAD), 1)
    global_x = lax.axis_index("mx") * block_x + rows - 1
    global_y = lax.axis_index("my") * block_y + lanes - 1
    valid = (global_x >= 0) & (global_x <= count_x * block_x - 2) & (rows <= block_x)
    valid = valid & (global_y >= 0) & (global_y <= count_y * block_y - 2) & (lanes <= block_y)
    return valid.astype(jnp.float32)


def fem_body(comps, grid, fld_ref, kmat_ref, body_ref, out_ref, vals_ref, vis_ref, resp_ref):
    layers = (fld_ref.shape[0] - 1) // 4
    main = fld_ref[4 * layers] == 0.0
    weight = cell_weight(grid)
    layer_index = lax.axis_index("layer")
    below_live = (layer_index > 0).astype(jnp.float32)
    above_live = (layer_index < lax.axis_size("layer") - 1).astype(jnp.float32)
    zero = jnp.zeros((ROWS_PAD, LANES_PAD), jnp.float32)
    for comp in comps:
        out_ref[comp] = -body_ref[comp]
    rows_out = [height * 9 + comp * 3 + vertex for height in range(2) for comp in comps for vertex in range(3)]
    pairs = layers - 1

    def layer_views(layer):
        slot = layer % 2
        for comp in range(4):
            plane = fld_ref[comp * layers + layer]
            below = pltpu.roll(plane, ROWS_PAD - 1, 0)
            right = pltpu.roll(plane, LANES_PAD - 1, 1)
            diag = pltpu.roll(below, LANES_PAD - 1, 1)
            far = jnp.where(main, diag, right)
            near = jnp.where(main, plane, below)
            for tri, views in enumerate(((plane, below, far), (near, diag, right))):
                for vertex in range(3):
                    vals_ref[slot, tri, comp * 3 + vertex] = views[vertex]

    layer_views(0)
    for pair in range(pairs):
        layer_views(pair + 1)
        slots = (pair % 2, (pair + 1) % 2)
        for tri in range(2):
            total = None
            for height in range(2):
                for vertex in range(3):
                    term = vals_ref[slots[height], tri, 9 + vertex]
                    total = term if total is None else total + term
            vis_ref[tri] = total / 6.0 * weight

        def tile_body(block, carry):
            row = pl.multiple_of(block * 8, 8)
            for tri in range(2):
                vis = vis_ref[tri, pl.ds(row, 8), :]
                values = [vals_ref[slots[beta // 9], tri, beta % 9, pl.ds(row, 8), :] for beta in range(18)]
                for alpha in rows_out:
                    acc = kmat_ref[alpha, 0] * values[0]
                    for beta in range(1, 18):
                        acc = acc + kmat_ref[alpha, beta] * values[beta]
                    resp_ref[tri, alpha, pl.ds(row, 8), :] = acc * vis
            return carry

        lax.fori_loop(0, ROWS_PAD // 8, tile_body, 0)
        for height in range(2):
            own_layer = pair + height - 1
            if own_layer < 0 or own_layer > pairs - 2:
                continue
            scale = None
            if pair == 0 and height == 1:
                scale = below_live
            if pair == pairs - 1 and height == 0:
                scale = above_live
            for comp in comps:
                base = height * 9 + comp * 3
                one = [resp_ref[0, base + v] for v in range(3)]
                two = [resp_ref[1, base + v] for v in range(3)]
                corner_a = one[0] + jnp.where(main, two[0], zero)
                corner_b = one[1] + jnp.where(main, zero, two[0])
                corner_c = two[2] + jnp.where(main, zero, one[2])
                corner_d = two[1] + jnp.where(main, one[2], zero)
                node = (pltpu.roll(pltpu.roll(corner_a, ROWS_PAD - 1, 0), LANES_PAD - 1, 1)
                        + pltpu.roll(corner_b, LANES_PAD - 1, 1)
                        + pltpu.roll(corner_c, ROWS_PAD - 1, 0) + corner_d)
                part = node[0:16, 0:256]
                if scale is not None:
                    part = part * scale
                out_ref[comp, own_layer] = out_ref[comp, own_layer] + part


def fem_horizontal(grid, fld_ref, kmat_ref, body_ref, out_ref, depth_ref, vals_ref, vis_ref, resp_ref):
    fem_body((0, 1), grid, fld_ref, kmat_ref, body_ref, out_ref, vals_ref, vis_ref, resp_ref)
    for comp in range(2):
        total = out_ref[comp, 0]
        for layer in range(1, out_ref.shape[1]):
            total = total + out_ref[comp, layer]
        depth_ref[comp] = total


def fem_vertical(grid, fld_ref, kmat_ref, body_ref, prev_ref, out_ref, vals_ref, vis_ref, resp_ref):
    out_ref[0:2] = prev_ref[0:2]
    fem_body((2,), grid, fld_ref, kmat_ref, body_ref, out_ref, vals_ref, vis_ref, resp_ref)


def fem_inputs(extended_layers, diag_ext):
    comps, layers, rows, lanes = extended_layers.shape
    planes = jnp.concatenate([extended_layers.reshape(comps * layers, rows, lanes), diag_ext[None]], 0)
    return jnp.pad(planes, ((0, 0), (0, ROWS_PAD - rows), (0, LANES_PAD - lanes)))


def fem_scratch():
    return [
        pltpu.VMEM((2, 2, 12, ROWS_PAD, LANES_PAD), jnp.float32),
        pltpu.VMEM((2, ROWS_PAD, LANES_PAD), jnp.float32),
        pltpu.VMEM((2, 18, ROWS_PAD, LANES_PAD), jnp.float32),
    ]


def fem_first(grid, fld, element_matrix, body_force):
    vmem = pl.BlockSpec(memory_space=pltpu.VMEM)
    smem = pl.BlockSpec(memory_space=pltpu.SMEM)
    depth_shape = (2,) + body_force.shape[2:]
    return pl.pallas_call(
        functools.partial(fem_horizontal, grid),
        out_shape=(
            jax.ShapeDtypeStruct(body_force.shape, jnp.float32),
            jax.ShapeDtypeStruct(depth_shape, jnp.float32),
        ),
        in_specs=[vmem, smem, vmem],
        out_specs=(vmem, vmem),
        scratch_shapes=fem_scratch(),
    )(fld, element_matrix, body_force)


def fem_second(grid, fld, element_matrix, body_force, previous):
    vmem = pl.BlockSpec(memory_space=pltpu.VMEM)
    smem = pl.BlockSpec(memory_space=pltpu.SMEM)
    return pl.pallas_call(
        functools.partial(fem_vertical, grid),
        out_shape=jax.ShapeDtypeStruct(body_force.shape, jnp.float32),
        in_specs=[vmem, smem, vmem, vmem],
        out_specs=vmem,
        scratch_shapes=fem_scratch(),
    )(fld, element_matrix, body_force, previous)


HIGH = lax.Precision.HIGHEST


def slot_selectors(index, rows, cols):
    live = index >= 0
    row_of = jnp.where(live, index // cols, -1)
    col_of = jnp.where(live, index % cols, -1)
    pick_row = (row_of[:, None] == jnp.arange(rows, dtype=jnp.int32)[None]).astype(jnp.float32)
    pick_col = (col_of[:, None] == jnp.arange(cols, dtype=jnp.int32)[None]).astype(jnp.float32)
    return pick_row, pick_col


def gather_slots(field, pick_row, pick_col):
    cols_taken = jnp.einsum("krc,sc->krs", field, pick_col, precision=lax.Precision.HIGH)
    return jnp.sum(jnp.where(pick_row.T[None] > 0.5, cols_taken, 0.0), axis=1)


def scatter_slots(values, pick_row, pick_col):
    weighted = pick_row[None] * values[:, :, None]
    return jnp.einsum("ksr,sc->krc", weighted, pick_col, precision=lax.Precision.HIGH)


def layer_total(part):
    count = lax.axis_size("layer")
    copies = jnp.broadcast_to(part[None], (count,) + part.shape)
    gathered = lax.all_to_all(copies, "layer", 0, 0, tiled=True)
    total = gathered[0]
    for source in range(1, count):
        total = total + gathered[source]
    return total


def layer_neighbours(top, bottom):
    count = lax.axis_size("layer")
    place = lax.axis_index("layer")
    chunks = []
    for target in range(count):
        chunk = jnp.where(target == place + 1, top, jnp.where(target == place - 1, bottom, 0.0))
        chunks.append(chunk[None])
    received = lax.all_to_all(jnp.concatenate(chunks, 0), "layer", 0, 0, tiled=True)
    below = jnp.zeros_like(top)
    above = jnp.zeros_like(top)
    for source in range(count):
        below = jnp.where(source == place - 1, received[source], below)
        above = jnp.where(source == place + 1, received[source], above)
    return below, above


def cell_dx(plane):
    return 0.5 * (plane[1:, :-1] + plane[1:, 1:] - (plane[:-1, :-1] + plane[:-1, 1:]))


def cell_dy(plane):
    return 0.5 * (plane[:-1, 1:] + plane[1:, 1:] - (plane[:-1, :-1] + plane[1:, :-1]))


def shelf_residual(padded, friction, driving):
    u_field = padded[0]
    v_field = padded[1]
    h_field = padded[2]
    du_dx = cell_dx(u_field)
    du_dy = cell_dy(u_field)
    dv_dx = cell_dx(v_field)
    dv_dy = cell_dy(v_field)
    h_cell = 0.25 * (h_field[1:, :-1] + h_field[1:, 1:] + h_field[:-1, :-1] + h_field[:-1, 1:])
    tau_xx = h_cell * (4.0 * du_dx + 2.0 * dv_dy)
    tau_yy = h_cell * (4.0 * dv_dy + 2.0 * du_dx)
    tau_xy = h_cell * (du_dy + dv_dx)
    res_x = cell_dx(tau_xx) + cell_dy(tau_xy) - friction * u_field[1:-1, 1:-1] - driving[0]
    res_y = cell_dy(tau_yy) + cell_dx(tau_xy) - friction * v_field[1:-1, 1:-1] - driving[1]
    return jnp.stack([res_x, res_y])


def triangle(stiffness, lows, ups, weight):
    values = jnp.stack(
        [plane[comp] for group in (lows, ups) for comp in range(3) for plane in group]
    )
    viscous = (
        (lows[0][3] + lows[1][3] + lows[2][3] + ups[0][3] + ups[1][3] + ups[2][3]) / 6.0 * weight
    )
    response = (
        jnp.einsum("ab,bxy->axy", stiffness, values, precision=lax.Precision.HIGHEST) * viscous
    )
    return response.reshape((2, 3, 3) + response.shape[1:])


def cell_terms(lower, upper, flag_cells, stiffness, weight):
    low_a, low_b, low_c, low_d = (
        lower[:, :-1, :-1],
        lower[:, 1:, :-1],
        lower[:, :-1, 1:],
        lower[:, 1:, 1:],
    )
    up_a, up_b, up_c, up_d = (
        upper[:, :-1, :-1],
        upper[:, 1:, :-1],
        upper[:, :-1, 1:],
        upper[:, 1:, 1:],
    )
    main_diag = (flag_cells == 0)[None]
    low_far = jnp.where(main_diag, low_d, low_c)
    up_far = jnp.where(main_diag, up_d, up_c)
    low_near = jnp.where(main_diag, low_a, low_b)
    up_near = jnp.where(main_diag, up_a, up_b)
    tri_one = triangle(stiffness, (low_a, low_b, low_far), (up_a, up_b, up_far), weight)
    tri_two = triangle(stiffness, (low_near, low_d, low_c), (up_near, up_d, up_c), weight)
    result = []
    for height in range(2):
        resp_one = tri_one[height]
        resp_two = tri_two[height]
        corner_a = resp_one[:, 0] + jnp.where(main_diag, resp_two[:, 0], 0.0)
        corner_b = resp_one[:, 1] + jnp.where(main_diag, 0.0, resp_two[:, 0])
        corner_c = resp_two[:, 2] + jnp.where(main_diag, 0.0, resp_one[:, 2])
        corner_d = resp_two[:, 1] + jnp.where(main_diag, resp_one[:, 2], 0.0)
        result.append((corner_a, corner_b, corner_c, corner_d))
    return (result[0], result[1])


def add_corners(total, extra):
    if total is None:
        return extra
    return tuple((first_term + other_term for first_term, other_term in zip(total, extra)))


def scaled_by(corners, factor):
    return tuple((member * factor for member in corners))


def own_nodes(corners):
    corner_a, corner_b, corner_c, corner_d = corners
    return corner_a[:, 1:, 1:] + corner_b[:, :-1, 1:] + corner_c[:, 1:, :-1] + corner_d[:, :-1, :-1]


def exchange(axis, sent_up, sent_down):
    count = lax.axis_size(axis)
    up = [(i, i + 1) for i in range(count - 1)]
    down = [(i + 1, i) for i in range(count - 1)]
    return lax.ppermute(sent_up, axis, up), lax.ppermute(sent_down, axis, down)


def packed_halo(arrays, dims, axis):
    ups, downs, shapes = [], [], []
    for array, dim in zip(arrays, dims):
        length = array.shape[dim]
        last = lax.slice_in_dim(array, length - 1, length, axis=dim)
        first = lax.slice_in_dim(array, 0, 1, axis=dim)
        shapes.append(last.shape)
        ups.append(last.reshape(-1))
        downs.append(first.reshape(-1))
    before, after = exchange(axis, jnp.concatenate(ups), jnp.concatenate(downs))
    widened = []
    offset = 0
    for array, dim, shape in zip(arrays, dims, shapes):
        size = 1
        for extent in shape:
            size *= extent
        head = before[offset:offset + size].reshape(shape)
        tail = after[offset:offset + size].reshape(shape)
        offset += size
        widened.append(jnp.concatenate([head, array, tail], axis=dim))
    return widened


def per_device(
    ssa_velocity,
    shelf_viscosity,
    basal_friction,
    driving_stress,
    stokes_velocity,
    ice_viscosity,
    body_force,
    diagonals,
    element_matrix,
    iface_columns,
    iface_nodes,
):
    row_count = ssa_velocity.shape[1]
    col_count = ssa_velocity.shape[2]
    depth_count = stokes_velocity.shape[1]
    block_x = stokes_velocity.shape[2]
    block_y = stokes_velocity.shape[3]
    stacked = jnp.concatenate([ssa_velocity, shelf_viscosity[None]], 0)
    owner_nodes = iface_nodes[0]
    slot_count = owner_nodes.shape[1]
    node_row, node_col = slot_selectors(owner_nodes.reshape(-1), row_count, col_count)
    outgoing = gather_slots(ssa_velocity, node_row, node_col).reshape(2, 3, 3, slot_count)
    raw_planes = jnp.concatenate(
        [
            stokes_velocity.reshape(3 * depth_count, block_x, block_y),
            ice_viscosity,
            diagonals.astype(jnp.float32)[None],
        ],
        0,
    )
    shelf_x, planes_x, slots_x = packed_halo((stacked, raw_planes, outgoing), (1, 1, 1), "mx")
    padded, widened, extended = packed_halo((shelf_x, planes_x, slots_x), (2, 2, 2), "my")
    shelf_res = shelf_residual(padded, basal_friction, driving_stress)
    returned = extended[:, 0::2, 0::2].reshape(2, 9, slot_count)
    columns = iface_columns[0]
    col_row, col_col = slot_selectors(columns.reshape(-1), block_x, block_y)
    placed = scatter_slots(returned.reshape(2, -1), col_row, col_col)
    marked = jnp.einsum("sr,sc->rc", col_row, col_col)
    ring = jnp.concatenate([jnp.minimum(marked, 1.0)[None], placed], 0)
    field_ext = widened[:-1].reshape(4, depth_count, block_x + 2, block_y + 2)
    below_raw, above_raw = layer_neighbours(field_ext[:, -1], field_ext[:, 0])
    (ring_x,) = packed_halo((ring,), (1,), "mx")
    (ring_ext,) = packed_halo((ring_x,), (2,), "my")
    imposed_at = ring_ext[0] > 0.5
    all_layers = jnp.concatenate([below_raw[:, None], field_ext, above_raw[:, None]], 1)
    uv_ext = jnp.where(imposed_at[None, None], ring_ext[1:3, None], all_layers[:2])
    extended_layers = jnp.concatenate([uv_ext, all_layers[2:]], 0)
    grid = (block_x, block_y, lax.axis_size("mx"), lax.axis_size("my"))
    fld = fem_inputs(extended_layers, widened[-1])
    partial_residual, depth_sum = fem_first(grid, fld, element_matrix, body_force)
    stokes_residual = fem_second(grid, fld, element_matrix, body_force, partial_residual)
    bucket = gather_slots(depth_sum, col_row, col_col).reshape(2, 9, slot_count)
    depth_total = layer_total(bucket)
    depth_total, stokes_residual = lax.optimization_barrier((depth_total, stokes_residual))
    grid_back = depth_total.reshape(2, 3, 3, slot_count)
    (back_x,) = packed_halo((grid_back,), (1,), "mx")
    (extended_back,) = packed_halo((back_x,), (2,), "my")
    at_owner = extended_back[:, 0::2, 0::2].reshape(2, 9, slot_count)
    node_force = scatter_slots(at_owner.reshape(2, -1), node_row, node_col)
    coupled_residual = shelf_res - node_force
    return (coupled_residual, stokes_residual)


def solution(mesh):
    return jax.shard_map(
        per_device,
        mesh=mesh,
        in_specs=(
            P(None, "mx", "my"),
            P("mx", "my"),
            P("mx", "my"),
            P(None, "mx", "my"),
            P(None, "layer", "mx", "my"),
            P("layer", "mx", "my"),
            P(None, "layer", "mx", "my"),
            P("mx", "my"),
            P(),
            P(("mx", "my"), None, None),
            P(("mx", "my"), None, None),
        ),
        out_specs=(P(None, "mx", "my"), P(None, "layer", "mx", "my")),
        check_vma=False,
    )
```
